32 devices in a mesh: dp: 8 (over z, y), tensor: 4 (over x, core).
Axes of the slice: x: 2, y: 2, z: 4, core: 2. Of those that a mesh axis runs over, the one named last changes fastest.
Arguments:
- tokens_in: bfloat16 [4096, 8192], P('dp', 'tensor'), may hold values from -6 to 6
- grad_out: bfloat16 [4096, 2, 1024], P('dp', None, 'tensor'), may hold values from -6 to 6
- base_weight: bfloat16 [2, 8192, 1024], P(None, None, 'tensor'), may hold values from -0.1875 to 0.1875
- a_master: float32 [65536, 128], P(('tensor', 'dp')), may hold values from -0.0625 to 0.0625
- b_master: float32 [4096, 256], P(('tensor', 'dp')), may hold values from -0.1875 to 0.1875
- a_first: float32 [65536, 128], P(('tensor', 'dp')), may hold values from -120 to 120
- a_second: float32 [65536, 128], P(('tensor', 'dp')), may hold values from 20 to 5000
- b_first: float32 [4096, 256], P(('tensor', 'dp')), may hold values from -120 to 120
- b_second: float32 [4096, 256], P(('tensor', 'dp')), may hold values from 20 to 5000
- block_tenant: int32 [32], P('dp'), may hold values from 0 to 7
- tenant_rank: int32 [8], replicated, may hold values from 16 to 64, as said below
- tenant_slot: int32 [8], replicated, may hold values from 0 to 7, each once
Outputs:
- input_gradient_layer: float32 [4096, 8192], P('dp', 'tensor')
- a_grad: float32 [65536, 128], P(('tensor', 'dp'))
- b_grad: float32 [4096, 256], P(('tensor', 'dp'))
- a_step: float32 [65536, 128], P(('tensor', 'dp'))
- b_step: float32 [4096, 256], P(('tensor', 'dp'))
The draws below stay inside these ranges and needn't reach their ends.
Inputs may be any that keep to these rules, and one draw needn't show every extreme that they name: `tenant_rank`: a whole multiple of 16; some tenant has rank 64 and some has 16. `tenant_slot`: each slot is taken by exactly one tenant.
All inputs are finite; a program needn't handle non-finite values.
Results may differ from the reference program's by a relative error of at most 0.0041.
Values may be sent and summed in bfloat16 or wider, within the bound.
No kernel may reach another device: no remote copies, remote signals or barrier semaphores. Data moves between devices by JAX's collectives and lax.ppermute only.
A program may use at most 128 MiB of HBM per device.

```python
import math
import jax
import jax.numpy as jnp
import numpy as np
from jax import lax

D = 8192
KV = 1024
PADDED_RANK = 64
TENANTS = 8
TENANT_BLOCK = 128
TOKENS = 4096
BLOCKS = 32
N_TENSOR = 4


def draw_tenant_rank(key, part):
    rank_step = PADDED_RANK // 4
    values = rank_step * jax.random.randint(key, (TENANTS,), 1, 5)
    order = jax.random.permutation(jax.random.fold_in(key, 7), TENANTS)
    values = values.at[order[0]].set(PADDED_RANK)
    values = values.at[order[1]].set(rank_step)
    return values.astype(jnp.int32)


def set_ends(values, key, smallest, largest):
    shape = values.shape
    place = [jax.random.randint(jax.random.fold_in(key, axis), (), 0, shape[axis]) for axis in range(len(shape))]
    values = values.at[tuple(place)].set(smallest)
    longest = shape.index(max(shape))
    place[longest] = (place[longest] + 1) % shape[longest]
    return values.at[tuple(place)].set(largest)


def block_scale(key, dims, cuts, smallest, high):
    level = 1.0
    for axis_at, shards_of in cuts:
        draws = jax.random.uniform(jax.random.fold_in(jax.random.fold_in(key, 6), axis_at), (shards_of,), jnp.float32, smallest / len(cuts), high / len(cuts))
        level = level * jnp.repeat(jnp.exp(draws), dims[axis_at] // shards_of).reshape((-1,) + (1,) * (len(dims) - 1 - axis_at))
    return level


def cumulative_ranks(amount, slope):
    weights = [(1 << 20) // math.isqrt(rank ** slope) + 1 for rank in range(1, amount + 1)]
    scale = 1 + sum(weights) // (1 << 30)
    return np.cumsum(np.array([max(1, weight // scale) for weight in weights]))


def ranked(stream_key, dims, amount, lean):
    listing = cumulative_ranks(amount, lean)
    ticket = jax.random.randint(jax.random.fold_in(stream_key, 1), dims, 0, int(listing[amount - 1]))
    rank = jnp.searchsorted(jnp.asarray(listing, jnp.int32), ticket, side="right")
    return jax.random.permutation(jax.random.fold_in(stream_key, 2), amount)[rank].astype(jnp.int32)


def scatter_about(own_key, dims, spread, reach, split=(), held_as=jnp.bfloat16):
    values = jax.random.normal(own_key, dims, jnp.float32) * spread
    if len(split) > 0:
        values = block_scale(own_key, dims, split, -0.22, 0.18) * values
    return jnp.clip(values, min=-reach, max=reach).astype(held_as)


def setup_inputs(seed: int = 0) -> dict:
    streams_of = jax.random.split(jax.random.key(seed), 13)
    tokens_in = scatter_about(streams_of[0], (TOKENS, D), 1.0, 6.0, ((0, 8), (1, 4)))
    grad_out = scatter_about(streams_of[1], (TOKENS, 2, KV), 1.0, 6.0, ((0, 8), (2, 4)))
    base_weight = scatter_about(streams_of[2], (2, D, KV), KV ** -0.5, 0.1875, ((2, 4),))
    a_master = scatter_about(streams_of[3], (TENANTS * D, 2 * PADDED_RANK), D ** -0.5, 0.0625, ((0, 32),), jnp.float32)
    b_master = scatter_about(streams_of[4], (N_TENSOR * TENANTS * 2 * PADDED_RANK, KV // N_TENSOR), KV ** -0.5, 0.1875, ((0, 32),), jnp.float32)
    a_first = scatter_about(streams_of[5], (TENANTS * D, 2 * PADDED_RANK), 20.0, 120.0, ((0, 32),), jnp.float32)
    a_second = jnp.clip(jnp.exp(math.log(5000.0) - 5.521461 * jax.random.uniform(streams_of[6], (TENANTS * D, 2 * PADDED_RANK), jnp.float32) ** block_scale(streams_of[6], (TENANTS * D, 2 * PADDED_RANK), ((0, 32),), -0.2, 0.2)), 20.0, 5000.0)
    b_first = scatter_about(streams_of[7], (N_TENSOR * TENANTS * 2 * PADDED_RANK, KV // N_TENSOR), 20.0, 120.0, ((0, 32),), jnp.float32)
    b_second = jnp.clip(jnp.exp(math.log(5000.0) - 5.521461 * jax.random.uniform(streams_of[8], (N_TENSOR * TENANTS * 2 * PADDED_RANK, KV // N_TENSOR), jnp.float32) ** block_scale(streams_of[8], (N_TENSOR * TENANTS * 2 * PADDED_RANK, KV // N_TENSOR), ((0, 32),), -0.2, 0.2)), 20.0, 5000.0)
    block_tenant = set_ends(ranked(streams_of[9], (BLOCKS,), TENANTS, 2), jax.random.fold_in(streams_of[9], 3), 0, TENANTS - 1).astype(jnp.int32)
    tenant_rank = draw_tenant_rank(jax.random.fold_in(streams_of[12], 71), 0)
    tenant_slot = jax.random.permutation(streams_of[11], TENANTS).astype(jnp.int32)
    return dict(tokens_in=tokens_in, grad_out=grad_out, base_weight=base_weight, a_master=a_master, b_master=b_master, a_first=a_first, a_second=a_second, b_first=b_first, b_second=b_second, block_tenant=block_tenant, tenant_rank=tenant_rank, tenant_slot=tenant_slot)


adapter_alpha_factor = 32.0
beta_one = 0.9
beta_two = 0.999
adam_eps = 1e-08
corr_one = 1.0 - 0.9 ** 3
corr_two = 1.0 - 0.999 ** 3

def adam_step(grad_value, first_moment, second_moment):
    new_first = beta_one * first_moment + (1.0 - beta_one) * grad_value
    new_second = beta_two * second_moment + (1.0 - beta_two) * grad_value * grad_value
    return new_first / corr_one / (jnp.sqrt(new_second / corr_two) + adam_eps)

def reference(tokens_in, grad_out, base_weight, a_master, b_master, a_first, a_second, b_first, b_second, block_tenant, tenant_rank, tenant_slot):
    feat_shard = D // N_TENSOR
    kv_shard = KV // N_TENSOR
    rank_width = 2 * PADDED_RANK
    a_slots = jnp.transpose(a_master.astype(jnp.bfloat16).reshape(N_TENSOR, TENANTS, feat_shard, rank_width), (1, 0, 2, 3)).reshape(TENANTS, D, rank_width)
    b_slots = jnp.transpose(b_master.astype(jnp.bfloat16).reshape(N_TENSOR, TENANTS, rank_width, kv_shard), (1, 2, 0, 3)).reshape(TENANTS, rank_width, KV)
    weight_wide = base_weight.astype(jnp.float32)
    block_slot = tenant_slot[block_tenant].astype(jnp.int32)
    rank_of_block = tenant_rank[block_tenant].astype(jnp.float32)
    column_rank = (jnp.arange(rank_width) % PADDED_RANK).astype(jnp.float32)
    tokens_blocks = tokens_in.reshape(BLOCKS, TENANT_BLOCK, D)
    grads_blocks = grad_out.reshape(BLOCKS, TENANT_BLOCK, 2, KV)

    def per_block(totals, inputs):
        grad_a, grad_b = totals
        x_rows, dy_rows, slot_now, current_adapter_rank = inputs
        local_down_weight = a_slots[slot_now]
        b_here = b_slots[slot_now]
        column_rank_mask = (column_rank < current_adapter_rank).astype(jnp.float32)
        adapter_scale_factor = adapter_alpha_factor / current_adapter_rank
        middle_rank_rows = (jnp.dot(x_rows, local_down_weight, preferred_element_type=jnp.float32) * column_rank_mask).astype(jnp.bfloat16)
        output_gradient_wide = dy_rows.astype(jnp.float32)
        unscaled_back_gradient = jnp.einsum('npk,prk->npr', output_gradient_wide, b_here.reshape(2, PADDED_RANK, KV).astype(jnp.float32)).reshape(TENANT_BLOCK, rank_width)
        backward_token_rows = (unscaled_back_gradient * (column_rank_mask * adapter_scale_factor)).astype(jnp.bfloat16)
        frozen_gradient_total = jnp.einsum('npk,pdk->nd', output_gradient_wide, weight_wide)
        adapter_gradient_term = jnp.dot(backward_token_rows, local_down_weight.T, preferred_element_type=jnp.float32)
        layer_input_rows = frozen_gradient_total + adapter_gradient_term
        grad_a = grad_a.at[slot_now].add(jnp.dot(x_rows.T, backward_token_rows, preferred_element_type=jnp.float32))
        up_weight_term = jnp.einsum('qbx,qbi->bxi', middle_rank_rows.reshape(TENANT_BLOCK, 2, PADDED_RANK).astype(jnp.float32), output_gradient_wide) * adapter_scale_factor
        grad_b = grad_b.at[slot_now].add(up_weight_term.reshape(rank_width, KV))
        return ((grad_a, grad_b), layer_input_rows)
    start_totals = (jnp.zeros((TENANTS, D, rank_width), jnp.float32), jnp.zeros((TENANTS, rank_width, KV), jnp.float32))
    (grad_a, grad_b), input_blocks = lax.scan(per_block, start_totals, (tokens_blocks, grads_blocks, block_slot, rank_of_block))
    input_gradient_layer = input_blocks.reshape(TOKENS, D)
    a_grad = jnp.transpose(grad_a.reshape(TENANTS, N_TENSOR, feat_shard, rank_width), (1, 0, 2, 3)).reshape(TENANTS * D, rank_width)
    b_grad = jnp.transpose(grad_b.reshape(TENANTS, rank_width, N_TENSOR, kv_shard), (2, 0, 1, 3)).reshape(N_TENSOR * TENANTS * rank_width, kv_shard)
    return (input_gradient_layer, a_grad, b_grad, adam_step(a_grad, a_first, a_second), adam_step(b_grad, b_first, b_second))
```

```python
import jax
import jax.numpy as jnp
from jax import lax
from jax.sharding import PartitionSpec as P

PADDED_RANK = 64
TENANTS = 8
TENANT_BLOCK = 128


adapter_alpha_factor = 32.0
beta_one = 0.9
beta_two = 0.999
adam_eps = 1e-08
corr_one = 1.0 - 0.9**3
corr_two = 1.0 - 0.999**3


def adam_step(grad_value, first_moment, second_moment):
    new_first = beta_one * first_moment + (1.0 - beta_one) * grad_value
    new_second = beta_two * second_moment + (1.0 - beta_two) * grad_value * grad_value
    return new_first / corr_one / (jnp.sqrt(new_second / corr_two) + adam_eps)


def local(
    tokens_in,
    grad_out,
    base_weight,
    a_master,
    b_master,
    a_first,
    a_second,
    b_first,
    b_second,
    block_tenant,
    tenant_rank,
    tenant_slot,
):
    tok_rows, feat_shard = tokens_in.shape
    kv_shard = grad_out.shape[2]
    rank_width = a_master.shape[1]
    block_count = tok_rows // TENANT_BLOCK
    dp_size = lax.axis_size("dp")
    a_rows_own = a_master.shape[0]
    b_rows_own = b_master.shape[0]
    b_as_a = b_master.astype(jnp.bfloat16).reshape(b_rows_own * kv_shard // rank_width, rank_width)
    packed = jnp.concatenate([a_master.astype(jnp.bfloat16), b_as_a], axis=0)
    packed_all = lax.all_gather(packed, "dp", axis=0, tiled=False)
    a_all = packed_all[:, :a_rows_own].reshape(TENANTS, feat_shard, rank_width)
    b_all = packed_all[:, a_rows_own:].reshape(dp_size, b_rows_own, kv_shard).reshape(
        TENANTS, rank_width, kv_shard
    )
    block_slot = tenant_slot[block_tenant]
    rank_of_block = tenant_rank[block_tenant].astype(jnp.float32)
    column_rank = (jnp.arange(rank_width) % PADDED_RANK).astype(jnp.float32)
    column_rank_mask = (column_rank[None, :] < rank_of_block[:, None]).astype(jnp.float32)
    adapter_scale_factor = adapter_alpha_factor / rank_of_block
    a_blocks = a_all[block_slot]
    b_blocks = b_all[block_slot].reshape(block_count, 2, PADDED_RANK, kv_shard)
    x_blocks = tokens_in.reshape(block_count, TENANT_BLOCK, feat_shard)
    dy_blocks = grad_out.reshape(block_count, TENANT_BLOCK, 2, kv_shard)
    mid_part = jnp.einsum("bnd,bdc->bnc", x_blocks, a_blocks, preferred_element_type=jnp.float32)
    back_part = jnp.einsum(
        "bnpk,bprk->bnpr", dy_blocks, b_blocks, preferred_element_type=jnp.float32
    ).reshape(block_count, TENANT_BLOCK, rank_width)
    mid_sum, backward_gradient_sum = lax.psum((mid_part, back_part), "tensor")
    middle_rank_rows = (mid_sum * column_rank_mask[:, None, :]).astype(jnp.bfloat16)
    backward_token_rows = (
        backward_gradient_sum * (column_rank_mask * adapter_scale_factor[:, None])[:, None, :]
    ).astype(jnp.bfloat16)
    t_size = lax.axis_size("tensor")
    dy_full = lax.all_gather(grad_out, "tensor", axis=2, tiled=False)
    weight_split = base_weight.reshape(2, t_size, feat_shard, kv_shard)
    weight_rows = lax.all_to_all(weight_split, "tensor", split_axis=1, concat_axis=1, tiled=True)
    frozen_gradient_share = jnp.einsum(
        "tpjk,pjdk->td", dy_full, weight_rows, preferred_element_type=jnp.float32
    )
    adapter_gradient_term = jnp.einsum(
        "bnc,bdc->bnd", backward_token_rows, a_blocks, preferred_element_type=jnp.float32
    ).reshape(tok_rows, feat_shard)
    input_gradient_layer = frozen_gradient_share + adapter_gradient_term
    a_terms = jnp.einsum(
        "bnd,bnc->bdc", x_blocks, backward_token_rows, preferred_element_type=jnp.float32
    )
    b_terms = (
        jnp.einsum(
            "bnpr,bnpk->bprk",
            middle_rank_rows.reshape(block_count, TENANT_BLOCK, 2, PADDED_RANK),
            dy_blocks,
            preferred_element_type=jnp.float32,
        )
        * adapter_scale_factor[:, None, None, None]
    )
    one_hot = (block_slot[None, :] == jnp.arange(TENANTS)[:, None]).astype(jnp.float32)
    a_flat = jnp.einsum("sb,bdc->sdc", one_hot, a_terms, precision=lax.Precision.HIGHEST).reshape(
        TENANTS * feat_shard, rank_width
    )
    b_flat = jnp.einsum("sb,bprk->sprk", one_hot, b_terms, precision=lax.Precision.HIGHEST).reshape(
        TENANTS * rank_width, kv_shard
    )
    a_grad, b_grad = lax.psum_scatter((a_flat, b_flat), "dp", scatter_dimension=0, tiled=True)
    return (
        input_gradient_layer,
        a_grad,
        b_grad,
        adam_step(a_grad, a_first, a_second),
        adam_step(b_grad, b_first, b_second),
    )


def solution(mesh):
    in_specs = (
        P("dp", "tensor"),
        P("dp", None, "tensor"),
        P(None, None, "tensor"),
        P(("tensor", "dp"), None),
        P(("tensor", "dp"), None),
        P(("tensor", "dp"), None),
        P(("tensor", "dp"), None),
        P(("tensor", "dp"), None),
        P(("tensor", "dp"), None),
        P("dp"),
        P(),
        P(),
    )
    out_specs = (
        P("dp", "tensor"),
        P(("tensor", "dp"), None),
        P(("tensor", "dp"), None),
        P(("tensor", "dp"), None),
        P(("tensor", "dp"), None),
    )
    return jax.shard_map(local, mesh=mesh, in_specs=in_specs, out_specs=out_specs, check_vma=False)
```

```python
import jax
import jax.numpy as jnp
from jax import lax
from jax.sharding import PartitionSpec as P

PADDED_RANK = 64
TENANTS = 8
TENANT_BLOCK = 128


adapter_alpha_factor = 32.0
beta_one = 0.9
beta_two = 0.999
adam_eps = 1e-08
corr_one = 1.0 - 0.9**3
corr_two = 1.0 - 0.999**3


def adam_step(grad_value, first_moment, second_moment):
    new_first = beta_one * first_moment + (1.0 - beta_one) * grad_value
    new_second = beta_two * second_moment + (1.0 - beta_two) * grad_value * grad_value
    return new_first / corr_one / (jnp.sqrt(new_second / corr_two) + adam_eps)


def tensor_sum(parts):
    size = lax.axis_size("tensor")
    step = 1
    while step < size:
        pairs = [(i, i ^ step) for i in range(size)]
        parts = tuple(p + lax.ppermute(p, "tensor", pairs) for p in parts)
        step *= 2
    return parts


def local(
    tokens_in,
    grad_out,
    base_weight,
    a_master,
    b_master,
    a_first,
    a_second,
    b_first,
    b_second,
    block_tenant,
    tenant_rank,
    tenant_slot,
):
    tok_rows, feat_shard = tokens_in.shape
    kv_shard = grad_out.shape[2]
    rank_width = a_master.shape[1]
    block_count = tok_rows // TENANT_BLOCK
    dp_size = lax.axis_size("dp")
    a_rows_own = a_master.shape[0]
    b_rows_own = b_master.shape[0]
    b_as_a = b_master.astype(jnp.bfloat16).reshape(b_rows_own * kv_shard // rank_width, rank_width)
    packed = jnp.concatenate([a_master.astype(jnp.bfloat16), b_as_a], axis=0)
    packed_all = lax.all_gather(packed, "dp", axis=0, tiled=False)
    a_all = packed_all[:, :a_rows_own].reshape(TENANTS, feat_shard, rank_width)
    b_all = packed_all[:, a_rows_own:].reshape(dp_size, b_rows_own, kv_shard).reshape(
        TENANTS, rank_width, kv_shard
    )
    block_slot = tenant_slot[block_tenant]
    rank_of_block = tenant_rank[block_tenant].astype(jnp.float32)
    column_rank = (jnp.arange(rank_width) % PADDED_RANK).astype(jnp.float32)
    column_rank_mask = (column_rank[None, :] < rank_of_block[:, None]).astype(jnp.float32)
    adapter_scale_factor = adapter_alpha_factor / rank_of_block
    a_blocks = a_all[block_slot]
    b_blocks = b_all[block_slot].reshape(block_count, 2, PADDED_RANK, kv_shard)
    x_blocks = tokens_in.reshape(block_count, TENANT_BLOCK, feat_shard)
    dy_blocks = grad_out.reshape(block_count, TENANT_BLOCK, 2, kv_shard)
    mid_part = jnp.einsum("bnd,bdc->bnc", x_blocks, a_blocks, preferred_element_type=jnp.float32)
    back_part = jnp.einsum(
        "bnpk,bprk->bnpr", dy_blocks, b_blocks, preferred_element_type=jnp.float32
    ).reshape(block_count, TENANT_BLOCK, rank_width)
    mid_sum, backward_gradient_sum = tensor_sum((mid_part, back_part))
    middle_rank_rows = (mid_sum * column_rank_mask[:, None, :]).astype(jnp.bfloat16)
    backward_token_rows = (
        backward_gradient_sum * (column_rank_mask * adapter_scale_factor[:, None])[:, None, :]
    ).astype(jnp.bfloat16)
    t_size = lax.axis_size("tensor")
    weight_split = jnp.transpose(base_weight.reshape(2, t_size, feat_shard, kv_shard), (1, 0, 2, 3))
    dy_copies = jnp.broadcast_to(
        jnp.transpose(grad_out, (1, 0, 2))[None], (t_size, 2, tok_rows, kv_shard)
    )
    send = jnp.concatenate([weight_split, dy_copies], axis=2)
    received = lax.all_to_all(send, "tensor", split_axis=0, concat_axis=0, tiled=True)
    weight_rows = received[:, :, :feat_shard]
    dy_full = received[:, :, feat_shard:]
    frozen_gradient_share = jnp.einsum(
        "jptk,jpdk->td", dy_full, weight_rows, preferred_element_type=jnp.float32
    )
    adapter_gradient_term = jnp.einsum(
        "bnc,bdc->bnd", backward_token_rows, a_blocks, preferred_element_type=jnp.float32
    ).reshape(tok_rows, feat_shard)
    input_gradient_layer = frozen_gradient_share + adapter_gradient_term
    a_terms = jnp.einsum(
        "bnd,bnc->bdc", x_blocks, backward_token_rows, preferred_element_type=jnp.float32
    )
    b_terms = (
        jnp.einsum(
            "bnpr,bnpk->bprk",
            middle_rank_rows.reshape(block_count, TENANT_BLOCK, 2, PADDED_RANK),
            dy_blocks,
            preferred_element_type=jnp.float32,
        )
        * adapter_scale_factor[:, None, None, None]
    )
    one_hot = (block_slot[None, :] == jnp.arange(TENANTS)[:, None]).astype(jnp.float32)
    a_flat = jnp.einsum("sb,bdc->sdc", one_hot, a_terms, precision=lax.Precision.HIGHEST).reshape(
        TENANTS * feat_shard, rank_width
    )
    b_flat = jnp.einsum("sb,bprk->sprk", one_hot, b_terms, precision=lax.Precision.HIGHEST).reshape(
        TENANTS * rank_width, kv_shard
    )
    a_per = a_flat.shape[0] // dp_size
    b_per = b_flat.shape[0] // dp_size
    b_wide = b_per * kv_shard // rank_width
    grad_pack = jnp.concatenate(
        [
            a_flat.reshape(dp_size, a_per, rank_width),
            b_flat.reshape(dp_size, b_wide, rank_width),
        ],
        axis=1,
    ).reshape(dp_size * (a_per + b_wide), rank_width)
    grad_own = lax.psum_scatter(grad_pack, "dp", scatter_dimension=0, tiled=True)
    a_grad = grad_own[:a_per]
    b_grad = grad_own[a_per:].reshape(b_per, kv_shard)
    return (
        input_gradient_layer,
        a_grad,
        b_grad,
        adam_step(a_grad, a_first, a_second),
        adam_step(b_grad, b_first, b_second),
    )


def solution(mesh):
    in_specs = (
        P("dp", "tensor"),
        P("dp", None, "tensor"),
        P(None, None, "tensor"),
        P(("tensor", "dp"), None),
        P(("tensor", "dp"), None),
        P(("tensor", "dp"), None),
        P(("tensor", "dp"), None),
        P(("tensor", "dp"), None),
        P(("tensor", "dp"), None),
        P("dp"),
        P(),
        P(),
    )
    out_specs = (
        P("dp", "tensor"),
        P(("tensor", "dp"), None),
        P(("tensor", "dp"), None),
        P(("tensor", "dp"), None),
        P(("tensor", "dp"), None),
    )
    return jax.shard_map(local, mesh=mesh, in_specs=in_specs, out_specs=out_specs, check_vma=False)
```

```python
import jax
import jax.numpy as jnp
from jax import lax
from jax.sharding import PartitionSpec as P

PADDED_RANK = 64
TENANTS = 8
TENANT_BLOCK = 128


adapter_alpha_factor = 32.0
beta_one = 0.9
beta_two = 0.999
adam_eps = 1e-08
corr_one = 1.0 - 0.9**3
corr_two = 1.0 - 0.999**3


def adam_step(grad_value, first_moment, second_moment):
    new_first = beta_one * first_moment + (1.0 - beta_one) * grad_value
    new_second = beta_two * second_moment + (1.0 - beta_two) * grad_value * grad_value
    return new_first / corr_one / (jnp.sqrt(new_second / corr_two) + adam_eps)


def tensor_sum(parts):
    size = lax.axis_size("tensor")
    step = 1
    while step < size:
        pairs = [(i, i ^ step) for i in range(size)]
        parts = tuple(p + lax.ppermute(p, "tensor", pairs) for p in parts)
        step *= 2
    return parts


def frozen_gradient(grad_out, base_weight, feat_shard):
    tok_rows, _, kv_shard = grad_out.shape
    t_size = lax.axis_size("tensor")
    if t_size != 4:
        weight_split = jnp.transpose(
            base_weight.reshape(2, t_size, feat_shard, kv_shard), (1, 0, 2, 3)
        )
        weight_rows = lax.all_to_all(weight_split, "tensor", split_axis=0, concat_axis=0, tiled=True)
        dy_full = lax.all_gather(grad_out, "tensor", axis=0, tiled=False)
        return jnp.einsum("jtpk,jpdk->td", dy_full, weight_rows, preferred_element_type=jnp.float32)
    me = lax.axis_index("tensor")
    core_bit = me % 2
    row_bit = me // 2
    by_bits = base_weight.reshape(2, 2, 2, feat_shard, kv_shard)
    to_partner = lax.dynamic_index_in_dim(by_bits, 1 - core_bit, axis=2, keepdims=False)
    own_w = lax.dynamic_index_in_dim(by_bits, core_bit, axis=2, keepdims=False)
    core_pairs = [(i, i ^ 1) for i in range(t_size)]
    row_pairs = [(i, i ^ 2) for i in range(t_size)]
    partner_w = lax.ppermute(to_partner, "tensor", core_pairs)
    partner_dy = lax.ppermute(grad_out, "tensor", core_pairs)

    def chip_partial(bit):
        own = lax.dynamic_index_in_dim(own_w, bit, axis=1, keepdims=False)
        other = lax.dynamic_index_in_dim(partner_w, bit, axis=1, keepdims=False)
        first = jnp.einsum("tpk,pdk->td", grad_out, own, preferred_element_type=jnp.float32)
        second = jnp.einsum("tpk,pdk->td", partner_dy, other, preferred_element_type=jnp.float32)
        return first + second

    far_part = chip_partial(1 - row_bit).astype(jnp.bfloat16)
    far_in = lax.ppermute(far_part, "tensor", row_pairs)
    return chip_partial(row_bit) + far_in.astype(jnp.float32)


def local(
    tokens_in,
    grad_out,
    base_weight,
    a_master,
    b_master,
    a_first,
    a_second,
    b_first,
    b_second,
    block_tenant,
    tenant_rank,
    tenant_slot,
):
    tok_rows, feat_shard = tokens_in.shape
    kv_shard = grad_out.shape[2]
    rank_width = a_master.shape[1]
    block_count = tok_rows // TENANT_BLOCK
    dp_size = lax.axis_size("dp")
    a_rows_own = a_master.shape[0]
    b_rows_own = b_master.shape[0]
    b_as_a = b_master.astype(jnp.bfloat16).reshape(b_rows_own * kv_shard // rank_width, rank_width)
    packed = jnp.concatenate([a_master.astype(jnp.bfloat16), b_as_a], axis=0)
    packed_all = lax.all_gather(packed, "dp", axis=0, tiled=False)
    a_all = packed_all[:, :a_rows_own].reshape(TENANTS, feat_shard, rank_width)
    b_all = packed_all[:, a_rows_own:].reshape(dp_size, b_rows_own, kv_shard).reshape(
        TENANTS, rank_width, kv_shard
    )
    block_slot = tenant_slot[block_tenant]
    rank_of_block = tenant_rank[block_tenant].astype(jnp.float32)
    column_rank = (jnp.arange(rank_width) % PADDED_RANK).astype(jnp.float32)
    column_rank_mask = (column_rank[None, :] < rank_of_block[:, None]).astype(jnp.float32)
    adapter_scale_factor = adapter_alpha_factor / rank_of_block
    a_blocks = a_all[block_slot]
    b_blocks = b_all[block_slot].reshape(block_count, 2, PADDED_RANK, kv_shard)
    x_blocks = tokens_in.reshape(block_count, TENANT_BLOCK, feat_shard)
    dy_blocks = grad_out.reshape(block_count, TENANT_BLOCK, 2, kv_shard)
    mid_part = jnp.einsum("bnd,bdc->bnc", x_blocks, a_blocks, preferred_element_type=jnp.float32)
    back_part = jnp.einsum(
        "bnpk,bprk->bnpr", dy_blocks, b_blocks, preferred_element_type=jnp.float32
    ).reshape(block_count, TENANT_BLOCK, rank_width)
    mid_sum, backward_gradient_sum = tensor_sum((mid_part, back_part))
    middle_rank_rows = (mid_sum * column_rank_mask[:, None, :]).astype(jnp.bfloat16)
    backward_token_rows = (
        backward_gradient_sum * (column_rank_mask * adapter_scale_factor[:, None])[:, None, :]
    ).astype(jnp.bfloat16)
    frozen_gradient_share = frozen_gradient(grad_out, base_weight, feat_shard)
    adapter_gradient_term = jnp.einsum(
        "bnc,bdc->bnd", backward_token_rows, a_blocks, preferred_element_type=jnp.float32
    ).reshape(tok_rows, feat_shard)
    input_gradient_layer = frozen_gradient_share + adapter_gradient_term
    a_terms = jnp.einsum(
        "bnd,bnc->bdc", x_blocks, backward_token_rows, preferred_element_type=jnp.float32
    )
    b_terms = (
        jnp.einsum(
            "bnpr,bnpk->bprk",
            middle_rank_rows.reshape(block_count, TENANT_BLOCK, 2, PADDED_RANK),
            dy_blocks,
            preferred_element_type=jnp.float32,
        )
        * adapter_scale_factor[:, None, None, None]
    )
    one_hot = (block_slot[None, :] == jnp.arange(TENANTS)[:, None]).astype(jnp.float32)
    a_flat = jnp.einsum("sb,bdc->sdc", one_hot, a_terms, precision=lax.Precision.HIGHEST).reshape(
        TENANTS * feat_shard, rank_width
    )
    b_flat = jnp.einsum("sb,bprk->sprk", one_hot, b_terms, precision=lax.Precision.HIGHEST).reshape(
        TENANTS * rank_width, kv_shard
    )
    a_per = a_flat.shape[0] // dp_size
    b_per = b_flat.shape[0] // dp_size
    b_wide = b_per * kv_shard // rank_width
    grad_pack = jnp.concatenate(
        [
            a_flat.reshape(dp_size, a_per, rank_width),
            b_flat.reshape(dp_size, b_wide, rank_width),
        ],
        axis=1,
    ).reshape(dp_size * (a_per + b_wide), rank_width)
    grad_parts = lax.all_to_all(
        grad_pack.astype(jnp.bfloat16).reshape(dp_size, a_per + b_wide, rank_width),
        "dp",
        split_axis=0,
        concat_axis=0,
        tiled=True,
    )
    grad_own = jnp.sum(grad_parts.astype(jnp.float32), axis=0)
    a_grad = grad_own[:a_per]
    b_grad = grad_own[a_per:].reshape(b_per, kv_shard)
    return (
        input_gradient_layer,
        a_grad,
        b_grad,
        adam_step(a_grad, a_first, a_second),
        adam_step(b_grad, b_first, b_second),
    )


def solution(mesh):
    in_specs = (
        P("dp", "tensor"),
        P("dp", None, "tensor"),
        P(None, None, "tensor"),
        P(("tensor", "dp"), None),
        P(("tensor", "dp"), None),
        P(("tensor", "dp"), None),
        P(("tensor", "dp"), None),
        P(("tensor", "dp"), None),
        P(("tensor", "dp"), None),
        P("dp"),
        P(),
        P(),
    )
    out_specs = (
        P("dp", "tensor"),
        P(("tensor", "dp"), None),
        P(("tensor", "dp"), None),
        P(("tensor", "dp"), None),
        P(("tensor", "dp"), None),
    )
    return jax.shard_map(local, mesh=mesh, in_specs=in_specs, out_specs=out_specs, check_vma=False)
```

```python
import jax
import jax.numpy as jnp
from jax import lax
from jax.sharding import PartitionSpec as P

PADDED_RANK = 64
TENANTS = 8
TENANT_BLOCK = 128


adapter_alpha_factor = 32.0
beta_one = 0.9
beta_two = 0.999
adam_eps = 1e-08
corr_one = 1.0 - 0.9**3
corr_two = 1.0 - 0.999**3


def adam_step(grad_value, first_moment, second_moment):
    new_first = beta_one * first_moment + (1.0 - beta_one) * grad_value
    new_second = beta_two * second_moment + (1.0 - beta_two) * grad_value * grad_value
    return new_first / corr_one / (jnp.sqrt(new_second / corr_two) + adam_eps)


def tensor_sum(parts):
    size = lax.axis_size("tensor")
    step = 1
    while step < size:
        pairs = [(i, i ^ step) for i in range(size)]
        parts = tuple(p + lax.ppermute(p, "tensor", pairs) for p in parts)
        step *= 2
    return parts


def frozen_gradient(grad_out, base_weight, feat_shard):
    tok_rows, _, kv_shard = grad_out.shape
    t_size = lax.axis_size("tensor")
    if t_size != 4:
        weight_split = jnp.transpose(
            base_weight.reshape(2, t_size, feat_shard, kv_shard), (1, 0, 2, 3)
        )
        weight_rows = lax.all_to_all(weight_split, "tensor", split_axis=0, concat_axis=0, tiled=True)
        dy_full = lax.all_gather(grad_out, "tensor", axis=0, tiled=False)
        return jnp.einsum("jtpk,jpdk->td", dy_full, weight_rows, preferred_element_type=jnp.float32)
    me = lax.axis_index("tensor")
    core_bit = me % 2
    row_bit = me // 2
    by_bits = base_weight.reshape(2, 2, 2, feat_shard, kv_shard)
    to_partner = lax.dynamic_index_in_dim(by_bits, 1 - core_bit, axis=2, keepdims=False)
    own_w = lax.dynamic_index_in_dim(by_bits, core_bit, axis=2, keepdims=False)
    core_pairs = [(i, i ^ 1) for i in range(t_size)]
    row_pairs = [(i, i ^ 2) for i in range(t_size)]
    partner_w = lax.ppermute(to_partner, "tensor", core_pairs)
    partner_dy = lax.ppermute(grad_out, "tensor", core_pairs)

    def chip_partial(bit):
        own = lax.dynamic_index_in_dim(own_w, bit, axis=1, keepdims=False)
        other = lax.dynamic_index_in_dim(partner_w, bit, axis=1, keepdims=False)
        first = jnp.einsum("tpk,pdk->td", grad_out, own, preferred_element_type=jnp.float32)
        second = jnp.einsum("tpk,pdk->td", partner_dy, other, preferred_element_type=jnp.float32)
        return first + second

    far_part = chip_partial(1 - row_bit).astype(jnp.bfloat16)
    far_in = lax.ppermute(far_part, "tensor", row_pairs)
    return chip_partial(row_bit) + far_in.astype(jnp.float32)


def local(
    tokens_in,
    grad_out,
    base_weight,
    a_master,
    b_master,
    a_first,
    a_second,
    b_first,
    b_second,
    block_tenant,
    tenant_rank,
    tenant_slot,
):
    tok_rows, feat_shard = tokens_in.shape
    kv_shard = grad_out.shape[2]
    rank_width = a_master.shape[1]
    block_count = tok_rows // TENANT_BLOCK
    dp_size = lax.axis_size("dp")
    a_rows_own = a_master.shape[0]
    b_rows_own = b_master.shape[0]
    b_as_a = b_master.astype(jnp.bfloat16).reshape(b_rows_own * kv_shard // rank_width, rank_width)
    packed = jnp.concatenate([a_master.astype(jnp.bfloat16), b_as_a], axis=0)
    packed_all = lax.all_gather(packed, "dp", axis=0, tiled=False)
    frozen_gradient_share = frozen_gradient(grad_out, base_weight, feat_shard)
    frozen_gradient_share, packed_all = lax.optimization_barrier((frozen_gradient_share, packed_all))
    a_all = packed_all[:, :a_rows_own].reshape(TENANTS, feat_shard, rank_width)
    b_all = packed_all[:, a_rows_own:].reshape(dp_size, b_rows_own, kv_shard).reshape(
        TENANTS, rank_width, kv_shard
    )
    block_slot = tenant_slot[block_tenant]
    rank_of_block = tenant_rank[block_tenant].astype(jnp.float32)
    column_rank = (jnp.arange(rank_width) % PADDED_RANK).astype(jnp.float32)
    column_rank_mask = (column_rank[None, :] < rank_of_block[:, None]).astype(jnp.float32)
    adapter_scale_factor = adapter_alpha_factor / rank_of_block
    a_blocks = a_all[block_slot]
    b_blocks = b_all[block_slot].reshape(block_count, 2, PADDED_RANK, kv_shard)
    x_blocks = tokens_in.reshape(block_count, TENANT_BLOCK, feat_shard)
    dy_blocks = grad_out.reshape(block_count, TENANT_BLOCK, 2, kv_shard)
    mid_part = jnp.einsum("bnd,bdc->bnc", x_blocks, a_blocks, preferred_element_type=jnp.float32)
    back_part = jnp.einsum(
        "bnpk,bprk->bnpr", dy_blocks, b_blocks, preferred_element_type=jnp.float32
    ).reshape(block_count, TENANT_BLOCK, rank_width)
    both_sum = tensor_sum((jnp.concatenate([mid_part, back_part], axis=2),))[0]
    mid_sum = both_sum[:, :, :rank_width]
    backward_gradient_sum = both_sum[:, :, rank_width:]
    middle_rank_rows = (mid_sum * column_rank_mask[:, None, :]).astype(jnp.bfloat16)
    backward_token_rows = (
        backward_gradient_sum * (column_rank_mask * adapter_scale_factor[:, None])[:, None, :]
    ).astype(jnp.bfloat16)
    adapter_gradient_term = jnp.einsum(
        "bnc,bdc->bnd", backward_token_rows, a_blocks, preferred_element_type=jnp.float32
    ).reshape(tok_rows, feat_shard)
    input_gradient_layer = frozen_gradient_share + adapter_gradient_term
    a_terms = jnp.einsum(
        "bnd,bnc->bdc", x_blocks, backward_token_rows, preferred_element_type=jnp.float32
    )
    b_terms = (
        jnp.einsum(
            "bnpr,bnpk->bprk",
            middle_rank_rows.reshape(block_count, TENANT_BLOCK, 2, PADDED_RANK),
            dy_blocks,
            preferred_element_type=jnp.float32,
        )
        * adapter_scale_factor[:, None, None, None]
    )
    one_hot = (block_slot[None, :] == jnp.arange(TENANTS)[:, None]).astype(jnp.float32)
    a_flat = jnp.einsum("sb,bdc->sdc", one_hot, a_terms, precision=lax.Precision.HIGHEST).reshape(
        TENANTS * feat_shard, rank_width
    )
    b_flat = jnp.einsum("sb,bprk->sprk", one_hot, b_terms, precision=lax.Precision.HIGHEST).reshape(
        TENANTS * rank_width, kv_shard
    )
    a_per = a_flat.shape[0] // dp_size
    b_per = b_flat.shape[0] // dp_size
    b_wide = b_per * kv_shard // rank_width
    grad_pack = jnp.concatenate(
        [
            a_flat.reshape(dp_size, a_per, rank_width),
            b_flat.reshape(dp_size, b_wide, rank_width),
        ],
        axis=1,
    ).reshape(dp_size * (a_per + b_wide), rank_width)
    grad_parts = lax.all_to_all(
        grad_pack.astype(jnp.bfloat16).reshape(dp_size, a_per + b_wide, rank_width),
        "dp",
        split_axis=0,
        concat_axis=0,
        tiled=True,
    )
    grad_own = jnp.sum(grad_parts.astype(jnp.float32), axis=0)
    a_grad = grad_own[:a_per]
    b_grad = grad_own[a_per:].reshape(b_per, kv_shard)
    return (
        input_gradient_layer,
        a_grad,
        b_grad,
        adam_step(a_grad, a_first, a_second),
        adam_step(b_grad, b_first, b_second),
    )


def solution(mesh):
    in_specs = (
        P("dp", "tensor"),
        P("dp", None, "tensor"),
        P(None, None, "tensor"),
        P(("tensor", "dp"), None),
        P(("tensor", "dp"), None),
        P(("tensor", "dp"), None),
        P(("tensor", "dp"), None),
        P(("tensor", "dp"), None),
        P(("tensor", "dp"), None),
        P("dp"),
        P(),
        P(),
    )
    out_specs = (
        P("dp", "tensor"),
        P(("tensor", "dp"), None),
        P(("tensor", "dp"), None),
        P(("tensor", "dp"), None),
        P(("tensor", "dp"), None),
    )
    return jax.shard_map(local, mesh=mesh, in_specs=in_specs, out_specs=out_specs, check_vma=False)
```

```python
import jax
import jax.numpy as jnp
from jax import lax
from jax.sharding import PartitionSpec as P

PADDED_RANK = 64
TENANTS = 8
TENANT_BLOCK = 128


adapter_alpha_factor = 32.0
beta_one = 0.9
beta_two = 0.999
adam_eps = 1e-08
corr_one = 1.0 - 0.9**3
corr_two = 1.0 - 0.999**3


def adam_step(grad_value, first_moment, second_moment):
    new_first = beta_one * first_moment + (1.0 - beta_one) * grad_value
    new_second = beta_two * second_moment + (1.0 - beta_two) * grad_value * grad_value
    return new_first / corr_one / (jnp.sqrt(new_second / corr_two) + adam_eps)


def tensor_sum(parts):
    size = lax.axis_size("tensor")
    step = 1
    while step < size:
        pairs = [(i, i ^ step) for i in range(size)]
        parts = tuple(p + lax.ppermute(p, "tensor", pairs) for p in parts)
        step *= 2
    return parts


def frozen_gradient(grad_out, base_weight, feat_shard):
    tok_rows, _, kv_shard = grad_out.shape
    t_size = lax.axis_size("tensor")
    if t_size != 4:
        weight_split = jnp.transpose(
            base_weight.reshape(2, t_size, feat_shard, kv_shard), (1, 0, 2, 3)
        )
        weight_rows = lax.all_to_all(weight_split, "tensor", split_axis=0, concat_axis=0, tiled=True)
        dy_full = lax.all_gather(grad_out, "tensor", axis=0, tiled=False)
        return jnp.einsum("jtpk,jpdk->td", dy_full, weight_rows, preferred_element_type=jnp.float32)
    me = lax.axis_index("tensor")
    core_bit = me % 2
    row_bit = me // 2
    by_bits = base_weight.reshape(2, 2, 2, feat_shard, kv_shard)
    to_partner = lax.dynamic_index_in_dim(by_bits, 1 - core_bit, axis=2, keepdims=False)
    own_w = lax.dynamic_index_in_dim(by_bits, core_bit, axis=2, keepdims=False)
    core_pairs = [(i, i ^ 1) for i in range(t_size)]
    row_pairs = [(i, i ^ 2) for i in range(t_size)]
    partner_w = lax.ppermute(to_partner, "tensor", core_pairs)
    partner_dy = lax.ppermute(grad_out, "tensor", core_pairs)

    def chip_partial(bit):
        own = lax.dynamic_index_in_dim(own_w, bit, axis=1, keepdims=False)
        other = lax.dynamic_index_in_dim(partner_w, bit, axis=1, keepdims=False)
        first = jnp.einsum("tpk,pdk->td", grad_out, own, preferred_element_type=jnp.float32)
        second = jnp.einsum("tpk,pdk->td", partner_dy, other, preferred_element_type=jnp.float32)
        return first + second

    far_part = chip_partial(1 - row_bit).astype(jnp.bfloat16)
    far_in = lax.ppermute(far_part, "tensor", row_pairs)
    return chip_partial(row_bit) + far_in.astype(jnp.float32)


def local(
    tokens_in,
    grad_out,
    base_weight,
    a_master,
    b_master,
    a_first,
    a_second,
    b_first,
    b_second,
    block_tenant,
    tenant_rank,
    tenant_slot,
):
    tok_rows, feat_shard = tokens_in.shape
    kv_shard = grad_out.shape[2]
    rank_width = a_master.shape[1]
    block_count = tok_rows // TENANT_BLOCK
    dp_size = lax.axis_size("dp")
    a_rows_own = a_master.shape[0]
    b_rows_own = b_master.shape[0]
    b_as_a = b_master.astype(jnp.bfloat16).reshape(b_rows_own * kv_shard // rank_width, rank_width)
    packed = jnp.concatenate([a_master.astype(jnp.bfloat16), b_as_a], axis=0)
    packed_all = lax.all_gather(packed, "dp", axis=0, tiled=False)
    frozen_gradient_share = frozen_gradient(grad_out, base_weight, feat_shard)
    frozen_gradient_share, packed_all = lax.optimization_barrier((frozen_gradient_share, packed_all))
    a_all = packed_all[:, :a_rows_own].reshape(TENANTS, feat_shard, rank_width)
    b_all = packed_all[:, a_rows_own:].reshape(dp_size, b_rows_own, kv_shard).reshape(
        TENANTS, rank_width, kv_shard
    )
    block_slot = tenant_slot[block_tenant]
    rank_of_block = tenant_rank[block_tenant].astype(jnp.float32)
    column_rank = (jnp.arange(rank_width) % PADDED_RANK).astype(jnp.float32)
    column_rank_mask = (column_rank[None, :] < rank_of_block[:, None]).astype(jnp.float32)
    adapter_scale_factor = adapter_alpha_factor / rank_of_block
    a_blocks = a_all[block_slot]
    b_blocks = b_all[block_slot].reshape(block_count, 2, PADDED_RANK, kv_shard)
    x_blocks = tokens_in.reshape(block_count, TENANT_BLOCK, feat_shard)
    dy_blocks = grad_out.reshape(block_count, TENANT_BLOCK, 2, kv_shard)
    mid_part = jnp.einsum("bnd,bdc->bnc", x_blocks, a_blocks, preferred_element_type=jnp.float32)
    back_part = jnp.einsum(
        "bnpk,bprk->bnpr", dy_blocks, b_blocks, preferred_element_type=jnp.float32
    ).reshape(block_count, TENANT_BLOCK, rank_width)
    both_sum = tensor_sum((jnp.concatenate([mid_part, back_part], axis=2),))[0]
    mid_sum = both_sum[:, :, :rank_width]
    backward_gradient_sum = both_sum[:, :, rank_width:]
    middle_rank_rows = (mid_sum * column_rank_mask[:, None, :]).astype(jnp.bfloat16)
    backward_token_rows = (
        backward_gradient_sum * (column_rank_mask * adapter_scale_factor[:, None])[:, None, :]
    ).astype(jnp.bfloat16)
    adapter_gradient_term = jnp.einsum(
        "bnc,bdc->bnd", backward_token_rows, a_blocks, preferred_element_type=jnp.float32
    ).reshape(tok_rows, feat_shard)
    input_gradient_layer = frozen_gradient_share + adapter_gradient_term
    a_terms = jnp.einsum(
        "bnd,bnc->bdc", x_blocks, backward_token_rows, preferred_element_type=jnp.float32
    )
    b_terms = (
        jnp.einsum(
            "bnpr,bnpk->bprk",
            middle_rank_rows.reshape(block_count, TENANT_BLOCK, 2, PADDED_RANK),
            dy_blocks,
            preferred_element_type=jnp.float32,
        )
        * adapter_scale_factor[:, None, None, None]
    )
    one_hot = (block_slot[None, :] == jnp.arange(TENANTS)[:, None]).astype(jnp.float32)
    a_flat = jnp.einsum("sb,bdc->sdc", one_hot, a_terms, precision=lax.Precision.HIGHEST).reshape(
        TENANTS * feat_shard, rank_width
    )
    b_flat = jnp.einsum("sb,bprk->sprk", one_hot, b_terms, precision=lax.Precision.HIGHEST).reshape(
        TENANTS * rank_width, kv_shard
    )
    a_per = a_flat.shape[0] // dp_size
    b_per = b_flat.shape[0] // dp_size
    b_wide = b_per * kv_shard // rank_width
    rows = a_per + b_wide
    grad_pack = jnp.concatenate(
        [
            a_flat.reshape(dp_size, a_per, rank_width),
            b_flat.reshape(dp_size, b_wide, rank_width),
        ],
        axis=1,
    )
    sc_rows = (rows * 2 // 5) // 8 * 8
    sc_own = lax.psum_scatter(
        grad_pack[:, :sc_rows].reshape(dp_size * sc_rows, rank_width),
        "dp",
        scatter_dimension=0,
        tiled=True,
    )
    tc_parts = lax.all_to_all(
        grad_pack[:, sc_rows:].astype(jnp.bfloat16),
        "dp",
        split_axis=0,
        concat_axis=0,
        tiled=True,
    )
    grad_own = jnp.concatenate([sc_own, jnp.sum(tc_parts.astype(jnp.float32), axis=0)], axis=0)
    a_grad = grad_own[:a_per]
    b_grad = grad_own[a_per:].reshape(b_per, kv_shard)
    return (
        input_gradient_layer,
        a_grad,
        b_grad,
        adam_step(a_grad, a_first, a_second),
        adam_step(b_grad, b_first, b_second),
    )


def solution(mesh):
    in_specs = (
        P("dp", "tensor"),
        P("dp", None, "tensor"),
        P(None, None, "tensor"),
        P(("tensor", "dp"), None),
        P(("tensor", "dp"), None),
        P(("tensor", "dp"), None),
        P(("tensor", "dp"), None),
        P(("tensor", "dp"), None),
        P(("tensor", "dp"), None),
        P("dp"),
        P(),
        P(),
    )
    out_specs = (
        P("dp", "tensor"),
        P(("tensor", "dp"), None),
        P(("tensor", "dp"), None),
        P(("tensor", "dp"), None),
        P(("tensor", "dp"), None),
    )
    return jax.shard_map(local, mesh=mesh, in_specs=in_specs, out_specs=out_specs, check_vma=False)
```

```python
import jax
import jax.numpy as jnp
from jax import lax
from jax.sharding import PartitionSpec as P

PADDED_RANK = 64
TENANTS = 8
TENANT_BLOCK = 128


adapter_alpha_factor = 32.0
beta_one = 0.9
beta_two = 0.999
adam_eps = 1e-08
corr_one = 1.0 - 0.9**3
corr_two = 1.0 - 0.999**3


def adam_step(grad_value, first_moment, second_moment):
    new_first = beta_one * first_moment + (1.0 - beta_one) * grad_value
    new_second = beta_two * second_moment + (1.0 - beta_two) * grad_value * grad_value
    return new_first / corr_one / (jnp.sqrt(new_second / corr_two) + adam_eps)


def ring_order(n):
    if n % 2:
        return list(range(n))
    return list(range(0, n, 2)) + list(range(n - 1, 0, -2))


def ring_all_gather(x):
    n = lax.axis_size("dp")
    order = ring_order(n)
    pos_of = [0] * n
    for p, d in enumerate(order):
        pos_of[d] = p
    fwd = [(order[p], order[(p + 1) % n]) for p in range(n)]
    bwd = [(order[p], order[(p - 1) % n]) for p in range(n)]
    half = x.shape[0] // 2
    cw, ccw = x[:half], x[half:]
    cw_steps, ccw_steps = [cw], [ccw]
    for _ in range(n - 1):
        cw = lax.ppermute(cw, "dp", fwd)
        ccw = lax.ppermute(ccw, "dp", bwd)
        cw_steps.append(cw)
        ccw_steps.append(ccw)
    ring_pos = jnp.asarray(pos_of, jnp.int32)
    pos = ring_pos[lax.axis_index("dp")]
    cw_all = jnp.take(jnp.stack(cw_steps), (pos - ring_pos) % n, axis=0)
    ccw_all = jnp.take(jnp.stack(ccw_steps), (ring_pos - pos) % n, axis=0)
    return jnp.concatenate([cw_all, ccw_all], axis=1)


def tensor_sum(parts):
    size = lax.axis_size("tensor")
    step = 1
    while step < size:
        pairs = [(i, i ^ step) for i in range(size)]
        parts = tuple(p + lax.ppermute(p, "tensor", pairs) for p in parts)
        step *= 2
    return parts


def frozen_gradient(grad_out, base_weight, feat_shard):
    tok_rows, _, kv_shard = grad_out.shape
    t_size = lax.axis_size("tensor")
    if t_size != 4:
        weight_split = jnp.transpose(
            base_weight.reshape(2, t_size, feat_shard, kv_shard), (1, 0, 2, 3)
        )
        weight_rows = lax.all_to_all(weight_split, "tensor", split_axis=0, concat_axis=0, tiled=True)
        dy_full = lax.all_gather(grad_out, "tensor", axis=0, tiled=False)
        return jnp.einsum("jtpk,jpdk->td", dy_full, weight_rows, preferred_element_type=jnp.float32)
    me = lax.axis_index("tensor")
    core_bit = me % 2
    row_bit = me // 2
    by_bits = base_weight.reshape(2, 2, 2, feat_shard, kv_shard)
    to_partner = lax.dynamic_index_in_dim(by_bits, 1 - core_bit, axis=2, keepdims=False)
    own_w = lax.dynamic_index_in_dim(by_bits, core_bit, axis=2, keepdims=False)
    core_pairs = [(i, i ^ 1) for i in range(t_size)]
    row_pairs = [(i, i ^ 2) for i in range(t_size)]
    partner_w = lax.ppermute(to_partner, "tensor", core_pairs)
    partner_dy = lax.ppermute(grad_out, "tensor", core_pairs)

    def chip_partial(bit):
        own = lax.dynamic_index_in_dim(own_w, bit, axis=1, keepdims=False)
        other = lax.dynamic_index_in_dim(partner_w, bit, axis=1, keepdims=False)
        first = jnp.einsum("tpk,pdk->td", grad_out, own, preferred_element_type=jnp.float32)
        second = jnp.einsum("tpk,pdk->td", partner_dy, other, preferred_element_type=jnp.float32)
        return first + second

    far_part = chip_partial(1 - row_bit).astype(jnp.bfloat16)
    far_in = lax.ppermute(far_part, "tensor", row_pairs)
    return chip_partial(row_bit) + far_in.astype(jnp.float32)


def local(
    tokens_in,
    grad_out,
    base_weight,
    a_master,
    b_master,
    a_first,
    a_second,
    b_first,
    b_second,
    block_tenant,
    tenant_rank,
    tenant_slot,
):
    tok_rows, feat_shard = tokens_in.shape
    kv_shard = grad_out.shape[2]
    rank_width = a_master.shape[1]
    block_count = tok_rows // TENANT_BLOCK
    dp_size = lax.axis_size("dp")
    a_rows_own = a_master.shape[0]
    b_rows_own = b_master.shape[0]
    b_as_a = b_master.astype(jnp.bfloat16).reshape(b_rows_own * kv_shard // rank_width, rank_width)
    packed = jnp.concatenate([a_master.astype(jnp.bfloat16), b_as_a], axis=0)
    packed_all = ring_all_gather(packed)
    frozen_gradient_share = frozen_gradient(grad_out, base_weight, feat_shard)
    frozen_gradient_share, packed_all = lax.optimization_barrier((frozen_gradient_share, packed_all))
    a_all = packed_all[:, :a_rows_own].reshape(TENANTS, feat_shard, rank_width)
    b_all = packed_all[:, a_rows_own:].reshape(dp_size, b_rows_own, kv_shard).reshape(
        TENANTS, rank_width, kv_shard
    )
    block_slot = tenant_slot[block_tenant]
    rank_of_block = tenant_rank[block_tenant].astype(jnp.float32)
    column_rank = (jnp.arange(rank_width) % PADDED_RANK).astype(jnp.float32)
    column_rank_mask = (column_rank[None, :] < rank_of_block[:, None]).astype(jnp.float32)
    adapter_scale_factor = adapter_alpha_factor / rank_of_block
    a_blocks = a_all[block_slot]
    b_blocks = b_all[block_slot].reshape(block_count, 2, PADDED_RANK, kv_shard)
    x_blocks = tokens_in.reshape(block_count, TENANT_BLOCK, feat_shard)
    dy_blocks = grad_out.reshape(block_count, TENANT_BLOCK, 2, kv_shard)
    mid_part = jnp.einsum("bnd,bdc->bnc", x_blocks, a_blocks, preferred_element_type=jnp.float32)
    back_part = jnp.einsum(
        "bnpk,bprk->bnpr", dy_blocks, b_blocks, preferred_element_type=jnp.float32
    ).reshape(block_count, TENANT_BLOCK, rank_width)
    both_sum = tensor_sum((jnp.concatenate([mid_part, back_part], axis=2),))[0]
    mid_sum = both_sum[:, :, :rank_width]
    backward_gradient_sum = both_sum[:, :, rank_width:]
    middle_rank_rows = (mid_sum * column_rank_mask[:, None, :]).astype(jnp.bfloat16)
    backward_token_rows = (
        backward_gradient_sum * (column_rank_mask * adapter_scale_factor[:, None])[:, None, :]
    ).astype(jnp.bfloat16)
    adapter_gradient_term = jnp.einsum(
        "bnc,bdc->bnd", backward_token_rows, a_blocks, preferred_element_type=jnp.float32
    ).reshape(tok_rows, feat_shard)
    input_gradient_layer = frozen_gradient_share + adapter_gradient_term
    a_terms = jnp.einsum(
        "bnd,bnc->bdc", x_blocks, backward_token_rows, preferred_element_type=jnp.float32
    )
    b_terms = (
        jnp.einsum(
            "bnpr,bnpk->bprk",
            middle_rank_rows.reshape(block_count, TENANT_BLOCK, 2, PADDED_RANK),
            dy_blocks,
            preferred_element_type=jnp.float32,
        )
        * adapter_scale_factor[:, None, None, None]
    )
    one_hot = (block_slot[None, :] == jnp.arange(TENANTS)[:, None]).astype(jnp.float32)
    a_flat = jnp.einsum("sb,bdc->sdc", one_hot, a_terms, precision=lax.Precision.HIGHEST).reshape(
        TENANTS * feat_shard, rank_width
    )
    b_flat = jnp.einsum("sb,bprk->sprk", one_hot, b_terms, precision=lax.Precision.HIGHEST).reshape(
        TENANTS * rank_width, kv_shard
    )
    a_per = a_flat.shape[0] // dp_size
    b_per = b_flat.shape[0] // dp_size
    b_wide = b_per * kv_shard // rank_width
    grad_pack = jnp.concatenate(
        [
            a_flat.reshape(dp_size, a_per, rank_width),
            b_flat.reshape(dp_size, b_wide, rank_width),
        ],
        axis=1,
    ).reshape(dp_size * (a_per + b_wide), rank_width)
    grad_parts = lax.all_to_all(
        grad_pack.astype(jnp.bfloat16).reshape(dp_size, a_per + b_wide, rank_width),
        "dp",
        split_axis=0,
        concat_axis=0,
        tiled=True,
    )
    grad_own = jnp.sum(grad_parts.astype(jnp.float32), axis=0)
    a_grad = grad_own[:a_per]
    b_grad = grad_own[a_per:].reshape(b_per, kv_shard)
    return (
        input_gradient_layer,
        a_grad,
        b_grad,
        adam_step(a_grad, a_first, a_second),
        adam_step(b_grad, b_first, b_second),
    )


def solution(mesh):
    in_specs = (
        P("dp", "tensor"),
        P("dp", None, "tensor"),
        P(None, None, "tensor"),
        P(("tensor", "dp"), None),
        P(("tensor", "dp"), None),
        P(("tensor", "dp"), None),
        P(("tensor", "dp"), None),
        P(("tensor", "dp"), None),
        P(("tensor", "dp"), None),
        P("dp"),
        P(),
        P(),
    )
    out_specs = (
        P("dp", "tensor"),
        P(("tensor", "dp"), None),
        P(("tensor", "dp"), None),
        P(("tensor", "dp"), None),
        P(("tensor", "dp"), None),
    )
    return jax.shard_map(local, mesh=mesh, in_specs=in_specs, out_specs=out_specs, check_vma=False)
```

```python
import jax
import jax.numpy as jnp
from jax import lax
from jax.sharding import PartitionSpec as P

PADDED_RANK = 64
TENANTS = 8
TENANT_BLOCK = 128


adapter_alpha_factor = 32.0
beta_one = 0.9
beta_two = 0.999
adam_eps = 1e-08
corr_one = 1.0 - 0.9**3
corr_two = 1.0 - 0.999**3


def adam_step(grad_value, first_moment, second_moment):
    new_first = beta_one * first_moment + (1.0 - beta_one) * grad_value
    new_second = beta_two * second_moment + (1.0 - beta_two) * grad_value * grad_value
    return new_first / corr_one / (jnp.sqrt(new_second / corr_two) + adam_eps)


def tensor_sum_pair(first, second):
    size = lax.axis_size("tensor")
    width = first.shape[-1]
    both = jnp.concatenate([first, second], axis=-1)
    both = both + lax.ppermute(both, "tensor", [(i, i ^ 1) for i in range(size)])
    first, second = both[..., :width], both[..., width:]
    step = 2
    while step < size:
        pairs = [(i, i ^ step) for i in range(size)]
        first = first + lax.ppermute(first, "tensor", pairs)
        second = second + lax.ppermute(second, "tensor", pairs)
        step *= 2
    return first, second


def tensor_sum(parts):
    size = lax.axis_size("tensor")
    step = 1
    while step < size:
        pairs = [(i, i ^ step) for i in range(size)]
        parts = tuple(p + lax.ppermute(p, "tensor", pairs) for p in parts)
        step *= 2
    return parts


def frozen_gradient(grad_out, base_weight, feat_shard):
    tok_rows, _, kv_shard = grad_out.shape
    t_size = lax.axis_size("tensor")
    if t_size != 4:
        weight_split = jnp.transpose(
            base_weight.reshape(2, t_size, feat_shard, kv_shard), (1, 0, 2, 3)
        )
        weight_rows = lax.all_to_all(weight_split, "tensor", split_axis=0, concat_axis=0, tiled=True)
        dy_full = lax.all_gather(grad_out, "tensor", axis=0, tiled=False)
        return jnp.einsum("jtpk,jpdk->td", dy_full, weight_rows, preferred_element_type=jnp.float32)
    me = lax.axis_index("tensor")
    core_bit = me % 2
    row_bit = me // 2
    by_bits = base_weight.reshape(2, 2, 2, feat_shard, kv_shard)
    to_partner = lax.dynamic_index_in_dim(by_bits, 1 - core_bit, axis=2, keepdims=False)
    own_w = lax.dynamic_index_in_dim(by_bits, core_bit, axis=2, keepdims=False)
    core_pairs = [(i, i ^ 1) for i in range(t_size)]
    row_pairs = [(i, i ^ 2) for i in range(t_size)]
    partner_w = lax.ppermute(to_partner, "tensor", core_pairs)
    partner_dy = lax.ppermute(grad_out, "tensor", core_pairs)

    def chip_partial(bit):
        own = lax.dynamic_index_in_dim(own_w, bit, axis=1, keepdims=False)
        other = lax.dynamic_index_in_dim(partner_w, bit, axis=1, keepdims=False)
        first = jnp.einsum("tpk,pdk->td", grad_out, own, preferred_element_type=jnp.float32)
        second = jnp.einsum("tpk,pdk->td", partner_dy, other, preferred_element_type=jnp.float32)
        return first + second

    far_part = chip_partial(1 - row_bit).astype(jnp.bfloat16)
    half = tok_rows // 2
    far_in = jnp.concatenate(
        [
            lax.ppermute(far_part[:half], "tensor", row_pairs),
            lax.ppermute(far_part[half:], "tensor", row_pairs),
        ],
        axis=0,
    )
    return chip_partial(row_bit) + far_in.astype(jnp.float32)


def slot_major_grads(
    tokens_in, grad_out, middle_rank_rows, backward_token_rows, block_slot, tenant_rank, tenant_slot
):
    tok_rows, feat_shard = tokens_in.shape
    kv_shard = grad_out.shape[2]
    rank_width = backward_token_rows.shape[-1]
    token_slot = jnp.repeat(block_slot, TENANT_BLOCK)
    slot_hot = token_slot[:, None] == jnp.arange(TENANTS)[None, :]
    back_rows = backward_token_rows.reshape(tok_rows, rank_width)
    back_sel = jnp.where(slot_hot[:, :, None], back_rows[:, None, :], jnp.zeros((), back_rows.dtype))
    a_sc = jnp.einsum("nsc,nd->scd", back_sel, tokens_in, preferred_element_type=jnp.float32)
    mid_rows = middle_rank_rows.reshape(tok_rows, 2, PADDED_RANK)
    mid_sel = jnp.where(
        slot_hot[:, :, None, None], mid_rows[:, None, :, :], jnp.zeros((), mid_rows.dtype)
    )
    b_sc = jnp.einsum("nspr,npk->sprk", mid_sel, grad_out, preferred_element_type=jnp.float32)
    slot_tenant = jnp.argsort(tenant_slot)
    slot_scale = adapter_alpha_factor / tenant_rank[slot_tenant].astype(jnp.float32)
    b_sc = b_sc * slot_scale[:, None, None, None]
    send = jnp.concatenate(
        [
            a_sc.astype(jnp.bfloat16),
            b_sc.reshape(TENANTS, rank_width, kv_shard).astype(jnp.bfloat16),
        ],
        axis=2,
    )
    recv = lax.all_to_all(send, "dp", split_axis=0, concat_axis=0, tiled=True)
    own = jnp.sum(recv.astype(jnp.float32), axis=0)
    return own[:, :feat_shard].T, own[:, feat_shard:]


def local(
    tokens_in,
    grad_out,
    base_weight,
    a_master,
    b_master,
    a_first,
    a_second,
    b_first,
    b_second,
    block_tenant,
    tenant_rank,
    tenant_slot,
):
    tok_rows, feat_shard = tokens_in.shape
    kv_shard = grad_out.shape[2]
    rank_width = a_master.shape[1]
    block_count = tok_rows // TENANT_BLOCK
    dp_size = lax.axis_size("dp")
    a_rows_own = a_master.shape[0]
    b_rows_own = b_master.shape[0]
    b_as_a = b_master.astype(jnp.bfloat16).reshape(b_rows_own * kv_shard // rank_width, rank_width)
    packed = jnp.concatenate([a_master.astype(jnp.bfloat16), b_as_a], axis=0)
    packed_all = lax.all_gather(packed, "dp", axis=0, tiled=False)
    block_slot = tenant_slot[block_tenant]
    slot_major = dp_size == TENANTS
    if slot_major:
        picked = jnp.take(packed_all, block_slot, axis=0)
        a_blocks = picked[:, :a_rows_own]
        b_blocks = picked[:, a_rows_own:].reshape(block_count, 2, PADDED_RANK, kv_shard)
    else:
        a_all = packed_all[:, :a_rows_own].reshape(TENANTS, feat_shard, rank_width)
        b_all = packed_all[:, a_rows_own:].reshape(dp_size, b_rows_own, kv_shard).reshape(
            TENANTS, rank_width, kv_shard
        )
        a_blocks = a_all[block_slot]
        b_blocks = b_all[block_slot].reshape(block_count, 2, PADDED_RANK, kv_shard)
    rank_of_block = tenant_rank[block_tenant].astype(jnp.float32)
    column_rank = (jnp.arange(rank_width) % PADDED_RANK).astype(jnp.float32)
    column_rank_mask = (column_rank[None, :] < rank_of_block[:, None]).astype(jnp.float32)
    adapter_scale_factor = adapter_alpha_factor / rank_of_block
    x_blocks = tokens_in.reshape(block_count, TENANT_BLOCK, feat_shard)
    dy_blocks = grad_out.reshape(block_count, TENANT_BLOCK, 2, kv_shard)
    mid_part = jnp.einsum("bnd,bdc->bnc", x_blocks, a_blocks, preferred_element_type=jnp.float32)
    back_part = jnp.einsum(
        "bnpk,bprk->bnpr", dy_blocks, b_blocks, preferred_element_type=jnp.float32
    ).reshape(block_count, TENANT_BLOCK, rank_width)
    mid_sum, backward_gradient_sum = tensor_sum_pair(mid_part, back_part)
    middle_rank_rows = (mid_sum * column_rank_mask[:, None, :]).astype(jnp.bfloat16)
    backward_token_rows = (
        backward_gradient_sum * (column_rank_mask * adapter_scale_factor[:, None])[:, None, :]
    ).astype(jnp.bfloat16)
    frozen_gradient_share = frozen_gradient(grad_out, base_weight, feat_shard)
    adapter_gradient_term = jnp.einsum(
        "bnc,bdc->bnd", backward_token_rows, a_blocks, preferred_element_type=jnp.float32
    ).reshape(tok_rows, feat_shard)
    input_gradient_layer = frozen_gradient_share + adapter_gradient_term
    if slot_major:
        a_grad, b_grad = slot_major_grads(
            tokens_in, grad_out, middle_rank_rows, backward_token_rows, block_slot,
            tenant_rank, tenant_slot,
        )
    else:
        a_terms = jnp.einsum(
            "bnd,bnc->bdc", x_blocks, backward_token_rows, preferred_element_type=jnp.float32
        )
        b_terms = (
            jnp.einsum(
                "bnpr,bnpk->bprk",
                middle_rank_rows.reshape(block_count, TENANT_BLOCK, 2, PADDED_RANK),
                dy_blocks,
                preferred_element_type=jnp.float32,
            )
            * adapter_scale_factor[:, None, None, None]
        )
        one_hot = (block_slot[None, :] == jnp.arange(TENANTS)[:, None]).astype(jnp.float32)
        a_flat = jnp.einsum("sb,bdc->sdc", one_hot, a_terms, precision=lax.Precision.HIGHEST).reshape(
            TENANTS * feat_shard, rank_width
        )
        b_flat = jnp.einsum("sb,bprk->sprk", one_hot, b_terms, precision=lax.Precision.HIGHEST).reshape(
            TENANTS * rank_width, kv_shard
        )
        a_per = a_flat.shape[0] // dp_size
        b_per = b_flat.shape[0] // dp_size
        b_wide = b_per * kv_shard // rank_width
        grad_pack = jnp.concatenate(
            [
                a_flat.reshape(dp_size, a_per, rank_width),
                b_flat.reshape(dp_size, b_wide, rank_width),
            ],
            axis=1,
        ).reshape(dp_size * (a_per + b_wide), rank_width)
        grad_parts = lax.all_to_all(
            grad_pack.astype(jnp.bfloat16).reshape(dp_size, a_per + b_wide, rank_width),
            "dp",
            split_axis=0,
            concat_axis=0,
            tiled=True,
        )
        grad_own = jnp.sum(grad_parts.astype(jnp.float32), axis=0)
        a_grad = grad_own[:a_per]
        b_grad = grad_own[a_per:].reshape(b_per, kv_shard)
    return (
        input_gradient_layer,
        a_grad,
        b_grad,
        adam_step(a_grad, a_first, a_second),
        adam_step(b_grad, b_first, b_second),
    )


def solution(mesh):
    in_specs = (
        P("dp", "tensor"),
        P("dp", None, "tensor"),
        P(None, None, "tensor"),
        P(("tensor", "dp"), None),
        P(("tensor", "dp"), None),
        P(("tensor", "dp"), None),
        P(("tensor", "dp"), None),
        P(("tensor", "dp"), None),
        P(("tensor", "dp"), None),
        P("dp"),
        P(),
        P(),
    )
    out_specs = (
        P("dp", "tensor"),
        P(("tensor", "dp"), None),
        P(("tensor", "dp"), None),
        P(("tensor", "dp"), None),
        P(("tensor", "dp"), None),
    )
    return jax.shard_map(local, mesh=mesh, in_specs=in_specs, out_specs=out_specs, check_vma=False)
```

```python
import jax
import jax.numpy as jnp
from jax import lax
from jax.sharding import PartitionSpec as P

PADDED_RANK = 64
TENANTS = 8
TENANT_BLOCK = 128


adapter_alpha_factor = 32.0
beta_one = 0.9
beta_two = 0.999
adam_eps = 1e-08
corr_one = 1.0 - 0.9**3
corr_two = 1.0 - 0.999**3


def adam_step(grad_value, first_moment, second_moment):
    new_first = beta_one * first_moment + (1.0 - beta_one) * grad_value
    new_second = beta_two * second_moment + (1.0 - beta_two) * grad_value * grad_value
    return new_first / corr_one / (jnp.sqrt(new_second / corr_two) + adam_eps)


def tensor_sum_pair(first, second):
    size = lax.axis_size("tensor")
    width = first.shape[-1]
    both = jnp.concatenate([first, second], axis=-1)
    both = both + lax.ppermute(both, "tensor", [(i, i ^ 1) for i in range(size)])
    first, second = both[..., :width], both[..., width:]
    step = 2
    while step < size:
        pairs = [(i, i ^ step) for i in range(size)]
        first = first + lax.ppermute(first, "tensor", pairs)
        second = second + lax.ppermute(second, "tensor", pairs)
        step *= 2
    return first, second


def tensor_sum(parts):
    size = lax.axis_size("tensor")
    step = 1
    while step < size:
        pairs = [(i, i ^ step) for i in range(size)]
        parts = tuple(p + lax.ppermute(p, "tensor", pairs) for p in parts)
        step *= 2
    return parts


def frozen_gradient(grad_out, base_weight, feat_shard):
    tok_rows, _, kv_shard = grad_out.shape
    t_size = lax.axis_size("tensor")
    if t_size != 4:
        weight_split = jnp.transpose(
            base_weight.reshape(2, t_size, feat_shard, kv_shard), (1, 0, 2, 3)
        )
        weight_rows = lax.all_to_all(weight_split, "tensor", split_axis=0, concat_axis=0, tiled=True)
        dy_full = lax.all_gather(grad_out, "tensor", axis=0, tiled=False)
        return jnp.einsum("jtpk,jpdk->td", dy_full, weight_rows, preferred_element_type=jnp.float32)
    me = lax.axis_index("tensor")
    core_bit = me % 2
    row_bit = me // 2
    by_bits = base_weight.reshape(2, 2, 2, feat_shard, kv_shard)
    to_partner = lax.dynamic_index_in_dim(by_bits, 1 - core_bit, axis=2, keepdims=False)
    own_w = lax.dynamic_index_in_dim(by_bits, core_bit, axis=2, keepdims=False)
    core_pairs = [(i, i ^ 1) for i in range(t_size)]
    row_pairs = [(i, i ^ 2) for i in range(t_size)]
    partner_w = lax.ppermute(to_partner, "tensor", core_pairs)
    partner_dy = lax.ppermute(grad_out, "tensor", core_pairs)

    def chip_partial(bit):
        own = lax.dynamic_index_in_dim(own_w, bit, axis=1, keepdims=False)
        other = lax.dynamic_index_in_dim(partner_w, bit, axis=1, keepdims=False)
        first = jnp.einsum("tpk,pdk->td", grad_out, own, preferred_element_type=jnp.float32)
        second = jnp.einsum("tpk,pdk->td", partner_dy, other, preferred_element_type=jnp.float32)
        return first + second

    far_part = chip_partial(1 - row_bit).astype(jnp.bfloat16)
    half = tok_rows // 2
    far_in = jnp.concatenate(
        [
            lax.ppermute(far_part[:half], "tensor", row_pairs),
            lax.ppermute(far_part[half:], "tensor", row_pairs),
        ],
        axis=0,
    )
    return chip_partial(row_bit) + far_in.astype(jnp.float32)


def slot_major_grads(
    tokens_in, grad_out, middle_rank_rows, backward_token_rows, block_slot, tenant_rank, tenant_slot
):
    tok_rows, feat_shard = tokens_in.shape
    kv_shard = grad_out.shape[2]
    rank_width = backward_token_rows.shape[-1]
    token_slot = jnp.repeat(block_slot, TENANT_BLOCK)
    slot_hot = token_slot[:, None] == jnp.arange(TENANTS)[None, :]
    back_rows = backward_token_rows.reshape(tok_rows, rank_width)
    back_sel = jnp.where(slot_hot[:, :, None], back_rows[:, None, :], jnp.zeros((), back_rows.dtype))
    a_sc = jnp.einsum("nsc,nd->scd", back_sel, tokens_in, preferred_element_type=jnp.float32)
    mid_rows = middle_rank_rows.reshape(tok_rows, 2, PADDED_RANK)
    mid_sel = jnp.where(
        slot_hot[:, :, None, None], mid_rows[:, None, :, :], jnp.zeros((), mid_rows.dtype)
    )
    b_sc = jnp.einsum("nspr,npk->sprk", mid_sel, grad_out, preferred_element_type=jnp.float32)
    slot_tenant = jnp.argsort(tenant_slot)
    slot_scale = adapter_alpha_factor / tenant_rank[slot_tenant].astype(jnp.float32)
    b_sc = b_sc * slot_scale[:, None, None, None]
    full = jnp.concatenate([a_sc, b_sc.reshape(TENANTS, rank_width, kv_shard)], axis=2)
    own = grouped_exchange(full)
    return own[:, :feat_shard].T, own[:, feat_shard:]


def grouped_exchange(full):
    n = full.shape[0]
    if n % 4:
        recv = lax.all_to_all(full.astype(jnp.bfloat16), "dp", split_axis=0, concat_axis=0, tiled=True)
        return jnp.sum(recv.astype(jnp.float32), axis=0)
    groups = n // 4
    me = lax.axis_index("dp")
    member = me % 4
    group = me // 4
    by_member = full.reshape(groups, 4, *full.shape[1:])
    acc = lax.dynamic_index_in_dim(by_member, member, axis=1, keepdims=False)
    for m in (1, 2, 3):
        pairs = [(i, (i // 4) * 4 + ((i % 4) ^ m)) for i in range(n)]
        part = lax.dynamic_index_in_dim(by_member, member ^ m, axis=1, keepdims=False)
        acc = acc + lax.ppermute(part.astype(jnp.bfloat16), "dp", pairs).astype(jnp.float32)
    total = lax.dynamic_index_in_dim(acc, group, axis=0, keepdims=False)
    for m in range(1, groups):
        pairs = [(i, ((i // 4 + m) % groups) * 4 + i % 4) for i in range(n)]
        part = lax.dynamic_index_in_dim(acc, (group + m) % groups, axis=0, keepdims=False)
        total = total + lax.ppermute(part.astype(jnp.bfloat16), "dp", pairs).astype(jnp.float32)
    return total


def local(
    tokens_in,
    grad_out,
    base_weight,
    a_master,
    b_master,
    a_first,
    a_second,
    b_first,
    b_second,
    block_tenant,
    tenant_rank,
    tenant_slot,
):
    tok_rows, feat_shard = tokens_in.shape
    kv_shard = grad_out.shape[2]
    rank_width = a_master.shape[1]
    block_count = tok_rows // TENANT_BLOCK
    dp_size = lax.axis_size("dp")
    a_rows_own = a_master.shape[0]
    b_rows_own = b_master.shape[0]
    b_as_a = b_master.astype(jnp.bfloat16).reshape(b_rows_own * kv_shard // rank_width, rank_width)
    packed = jnp.concatenate([a_master.astype(jnp.bfloat16), b_as_a], axis=0)
    packed_all = lax.all_gather(packed, "dp", axis=0, tiled=False)
    block_slot = tenant_slot[block_tenant]
    slot_major = dp_size == TENANTS
    if slot_major:
        picked = jnp.take(packed_all, block_slot, axis=0)
        a_blocks = picked[:, :a_rows_own]
        b_blocks = picked[:, a_rows_own:].reshape(block_count, 2, PADDED_RANK, kv_shard)
    else:
        a_all = packed_all[:, :a_rows_own].reshape(TENANTS, feat_shard, rank_width)
        b_all = packed_all[:, a_rows_own:].reshape(dp_size, b_rows_own, kv_shard).reshape(
            TENANTS, rank_width, kv_shard
        )
        a_blocks = a_all[block_slot]
        b_blocks = b_all[block_slot].reshape(block_count, 2, PADDED_RANK, kv_shard)
    rank_of_block = tenant_rank[block_tenant].astype(jnp.float32)
    column_rank = (jnp.arange(rank_width) % PADDED_RANK).astype(jnp.float32)
    column_rank_mask = (column_rank[None, :] < rank_of_block[:, None]).astype(jnp.float32)
    adapter_scale_factor = adapter_alpha_factor / rank_of_block
    x_blocks = tokens_in.reshape(block_count, TENANT_BLOCK, feat_shard)
    dy_blocks = grad_out.reshape(block_count, TENANT_BLOCK, 2, kv_shard)
    mid_part = jnp.einsum("bnd,bdc->bnc", x_blocks, a_blocks, preferred_element_type=jnp.float32)
    back_part = jnp.einsum(
        "bnpk,bprk->bnpr", dy_blocks, b_blocks, preferred_element_type=jnp.float32
    ).reshape(block_count, TENANT_BLOCK, rank_width)
    mid_sum, backward_gradient_sum = tensor_sum_pair(mid_part, back_part)
    middle_rank_rows = (mid_sum * column_rank_mask[:, None, :]).astype(jnp.bfloat16)
    backward_token_rows = (
        backward_gradient_sum * (column_rank_mask * adapter_scale_factor[:, None])[:, None, :]
    ).astype(jnp.bfloat16)
    frozen_gradient_share = frozen_gradient(grad_out, base_weight, feat_shard)
    adapter_gradient_term = jnp.einsum(
        "bnc,bdc->bnd", backward_token_rows, a_blocks, preferred_element_type=jnp.float32
    ).reshape(tok_rows, feat_shard)
    input_gradient_layer = frozen_gradient_share + adapter_gradient_term
    if slot_major:
        a_grad, b_grad = slot_major_grads(
            tokens_in, grad_out, middle_rank_rows, backward_token_rows, block_slot,
            tenant_rank, tenant_slot,
        )
    else:
        a_terms = jnp.einsum(
            "bnd,bnc->bdc", x_blocks, backward_token_rows, preferred_element_type=jnp.float32
        )
        b_terms = (
            jnp.einsum(
                "bnpr,bnpk->bprk",
                middle_rank_rows.reshape(block_count, TENANT_BLOCK, 2, PADDED_RANK),
                dy_blocks,
                preferred_element_type=jnp.float32,
            )
            * adapter_scale_factor[:, None, None, None]
        )
        one_hot = (block_slot[None, :] == jnp.arange(TENANTS)[:, None]).astype(jnp.float32)
        a_flat = jnp.einsum("sb,bdc->sdc", one_hot, a_terms, precision=lax.Precision.HIGHEST).reshape(
            TENANTS * feat_shard, rank_width
        )
        b_flat = jnp.einsum("sb,bprk->sprk", one_hot, b_terms, precision=lax.Precision.HIGHEST).reshape(
            TENANTS * rank_width, kv_shard
        )
        a_per = a_flat.shape[0] // dp_size
        b_per = b_flat.shape[0] // dp_size
        b_wide = b_per * kv_shard // rank_width
        grad_pack = jnp.concatenate(
            [
                a_flat.reshape(dp_size, a_per, rank_width),
                b_flat.reshape(dp_size, b_wide, rank_width),
            ],
            axis=1,
        ).reshape(dp_size * (a_per + b_wide), rank_width)
        grad_parts = lax.all_to_all(
            grad_pack.astype(jnp.bfloat16).reshape(dp_size, a_per + b_wide, rank_width),
            "dp",
            split_axis=0,
            concat_axis=0,
            tiled=True,
        )
        grad_own = jnp.sum(grad_parts.astype(jnp.float32), axis=0)
        a_grad = grad_own[:a_per]
        b_grad = grad_own[a_per:].reshape(b_per, kv_shard)
    return (
        input_gradient_layer,
        a_grad,
        b_grad,
        adam_step(a_grad, a_first, a_second),
        adam_step(b_grad, b_first, b_second),
    )


def solution(mesh):
    in_specs = (
        P("dp", "tensor"),
        P("dp", None, "tensor"),
        P(None, None, "tensor"),
        P(("tensor", "dp"), None),
        P(("tensor", "dp"), None),
        P(("tensor", "dp"), None),
        P(("tensor", "dp"), None),
        P(("tensor", "dp"), None),
        P(("tensor", "dp"), None),
        P("dp"),
        P(),
        P(),
    )
    out_specs = (
        P("dp", "tensor"),
        P(("tensor", "dp"), None),
        P(("tensor", "dp"), None),
        P(("tensor", "dp"), None),
        P(("tensor", "dp"), None),
    )
    return jax.shard_map(local, mesh=mesh, in_specs=in_specs, out_specs=out_specs, check_vma=False)
```

```python
import jax
import jax.numpy as jnp
from jax import lax
from jax.sharding import PartitionSpec as P

PADDED_RANK = 64
TENANTS = 8
TENANT_BLOCK = 128


adapter_alpha_factor = 32.0
beta_one = 0.9
beta_two = 0.999
adam_eps = 1e-08
corr_one = 1.0 - 0.9**3
corr_two = 1.0 - 0.999**3


def adam_step(grad_value, first_moment, second_moment):
    new_first = beta_one * first_moment + (1.0 - beta_one) * grad_value
    new_second = beta_two * second_moment + (1.0 - beta_two) * grad_value * grad_value
    return new_first / corr_one / (jnp.sqrt(new_second / corr_two) + adam_eps)


def tensor_sum_pair(first, second):
    size = lax.axis_size("tensor")
    width = first.shape[-1]
    both = jnp.concatenate([first, second], axis=-1)
    both = both + lax.ppermute(both, "tensor", [(i, i ^ 1) for i in range(size)])
    first, second = both[..., :width], both[..., width:]
    step = 2
    while step < size:
        pairs = [(i, i ^ step) for i in range(size)]
        first = first + lax.ppermute(first, "tensor", pairs)
        second = second + lax.ppermute(second, "tensor", pairs)
        step *= 2
    return first, second


def tensor_sum(parts):
    size = lax.axis_size("tensor")
    step = 1
    while step < size:
        pairs = [(i, i ^ step) for i in range(size)]
        parts = tuple(p + lax.ppermute(p, "tensor", pairs) for p in parts)
        step *= 2
    return parts


def frozen_gradient(grad_out, base_weight, feat_shard):
    tok_rows, _, kv_shard = grad_out.shape
    t_size = lax.axis_size("tensor")
    if t_size != 4:
        weight_split = jnp.transpose(
            base_weight.reshape(2, t_size, feat_shard, kv_shard), (1, 0, 2, 3)
        )
        weight_rows = lax.all_to_all(weight_split, "tensor", split_axis=0, concat_axis=0, tiled=True)
        dy_full = lax.all_gather(grad_out, "tensor", axis=0, tiled=False)
        return jnp.einsum("jtpk,jpdk->td", dy_full, weight_rows, preferred_element_type=jnp.float32)
    me = lax.axis_index("tensor")
    core_bit = me % 2
    row_bit = me // 2
    by_bits = base_weight.reshape(2, 2, 2, feat_shard, kv_shard)
    to_partner = lax.dynamic_index_in_dim(by_bits, 1 - core_bit, axis=2, keepdims=False)
    own_w = lax.dynamic_index_in_dim(by_bits, core_bit, axis=2, keepdims=False)
    core_pairs = [(i, i ^ 1) for i in range(t_size)]
    row_pairs = [(i, i ^ 2) for i in range(t_size)]
    partner_w = lax.ppermute(to_partner, "tensor", core_pairs)
    partner_dy = lax.ppermute(grad_out, "tensor", core_pairs)

    def chip_partial(bit):
        own = lax.dynamic_index_in_dim(own_w, bit, axis=1, keepdims=False)
        other = lax.dynamic_index_in_dim(partner_w, bit, axis=1, keepdims=False)
        first = jnp.einsum("tpk,pdk->td", grad_out, own, preferred_element_type=jnp.float32)
        second = jnp.einsum("tpk,pdk->td", partner_dy, other, preferred_element_type=jnp.float32)
        return first + second

    far_part = chip_partial(1 - row_bit).astype(jnp.bfloat16)
    half = tok_rows // 2
    far_in = jnp.concatenate(
        [
            lax.ppermute(far_part[:half], "tensor", row_pairs),
            lax.ppermute(far_part[half:], "tensor", row_pairs),
        ],
        axis=0,
    )
    return chip_partial(row_bit) + far_in.astype(jnp.float32)


def slot_major_grads(
    tokens_in, grad_out, middle_rank_rows, backward_token_rows, block_slot, tenant_rank, tenant_slot
):
    tok_rows, feat_shard = tokens_in.shape
    kv_shard = grad_out.shape[2]
    rank_width = backward_token_rows.shape[-1]
    token_slot = jnp.repeat(block_slot, TENANT_BLOCK)
    slot_hot = token_slot[:, None] == jnp.arange(TENANTS)[None, :]
    back_rows = backward_token_rows.reshape(tok_rows, rank_width)
    back_sel = jnp.where(slot_hot[:, :, None], back_rows[:, None, :], jnp.zeros((), back_rows.dtype))
    a_sc = jnp.einsum("nsc,nd->scd", back_sel, tokens_in, preferred_element_type=jnp.float32)
    mid_rows = middle_rank_rows.reshape(tok_rows, 2, PADDED_RANK)
    mid_sel = jnp.where(
        slot_hot[:, :, None, None], mid_rows[:, None, :, :], jnp.zeros((), mid_rows.dtype)
    )
    b_sc = jnp.einsum("nspr,npk->sprk", mid_sel, grad_out, preferred_element_type=jnp.float32)
    slot_tenant = jnp.argsort(tenant_slot)
    slot_scale = adapter_alpha_factor / tenant_rank[slot_tenant].astype(jnp.float32)
    b_sc = b_sc * slot_scale[:, None, None, None]
    full = jnp.concatenate([a_sc, b_sc.reshape(TENANTS, rank_width, kv_shard)], axis=2)
    if full.shape[0] % 4:
        own = grouped_exchange(full)
    else:
        split = full.shape[2] // 2
        first = group_stage(full[..., :split])
        later, first = lax.optimization_barrier((full[..., split:], first))
        second = group_stage(later)
        own = jnp.concatenate([cross_stage(first), cross_stage(second)], axis=-1)
    return own[:, :feat_shard].T, own[:, feat_shard:]


def group_stage(full):
    n = full.shape[0]
    member = lax.axis_index("dp") % 4
    by_member = full.reshape(n // 4, 4, *full.shape[1:])
    acc = lax.dynamic_index_in_dim(by_member, member, axis=1, keepdims=False)
    for m in (1, 2, 3):
        pairs = [(i, (i // 4) * 4 + ((i % 4) ^ m)) for i in range(n)]
        part = lax.dynamic_index_in_dim(by_member, member ^ m, axis=1, keepdims=False)
        acc = acc + lax.ppermute(part.astype(jnp.bfloat16), "dp", pairs).astype(jnp.float32)
    return acc


def cross_stage(acc):
    groups = acc.shape[0]
    n = groups * 4
    group = lax.axis_index("dp") // 4
    total = lax.dynamic_index_in_dim(acc, group, axis=0, keepdims=False)
    for m in range(1, groups):
        pairs = [(i, ((i // 4 + m) % groups) * 4 + i % 4) for i in range(n)]
        part = lax.dynamic_index_in_dim(acc, (group + m) % groups, axis=0, keepdims=False)
        total = total + lax.ppermute(part.astype(jnp.bfloat16), "dp", pairs).astype(jnp.float32)
    return total


def grouped_exchange(full):
    n = full.shape[0]
    if n % 4:
        recv = lax.all_to_all(full.astype(jnp.bfloat16), "dp", split_axis=0, concat_axis=0, tiled=True)
        return jnp.sum(recv.astype(jnp.float32), axis=0)
    groups = n // 4
    me = lax.axis_index("dp")
    member = me % 4
    group = me // 4
    by_member = full.reshape(groups, 4, *full.shape[1:])
    acc = lax.dynamic_index_in_dim(by_member, member, axis=1, keepdims=False)
    for m in (1, 2, 3):
        pairs = [(i, (i // 4) * 4 + ((i % 4) ^ m)) for i in range(n)]
        part = lax.dynamic_index_in_dim(by_member, member ^ m, axis=1, keepdims=False)
        acc = acc + lax.ppermute(part.astype(jnp.bfloat16), "dp", pairs).astype(jnp.float32)
    total = lax.dynamic_index_in_dim(acc, group, axis=0, keepdims=False)
    for m in range(1, groups):
        pairs = [(i, ((i // 4 + m) % groups) * 4 + i % 4) for i in range(n)]
        part = lax.dynamic_index_in_dim(acc, (group + m) % groups, axis=0, keepdims=False)
        total = total + lax.ppermute(part.astype(jnp.bfloat16), "dp", pairs).astype(jnp.float32)
    return total


def local(
    tokens_in,
    grad_out,
    base_weight,
    a_master,
    b_master,
    a_first,
    a_second,
    b_first,
    b_second,
    block_tenant,
    tenant_rank,
    tenant_slot,
):
    tok_rows, feat_shard = tokens_in.shape
    kv_shard = grad_out.shape[2]
    rank_width = a_master.shape[1]
    block_count = tok_rows // TENANT_BLOCK
    dp_size = lax.axis_size("dp")
    a_rows_own = a_master.shape[0]
    b_rows_own = b_master.shape[0]
    b_as_a = b_master.astype(jnp.bfloat16).reshape(b_rows_own * kv_shard // rank_width, rank_width)
    packed = jnp.concatenate([a_master.astype(jnp.bfloat16), b_as_a], axis=0)
    packed_all = lax.all_gather(packed, "dp", axis=0, tiled=False)
    block_slot = tenant_slot[block_tenant]
    slot_major = dp_size == TENANTS
    if slot_major:
        picked = jnp.take(packed_all, block_slot, axis=0)
        a_blocks = picked[:, :a_rows_own]
        b_blocks = picked[:, a_rows_own:].reshape(block_count, 2, PADDED_RANK, kv_shard)
    else:
        a_all = packed_all[:, :a_rows_own].reshape(TENANTS, feat_shard, rank_width)
        b_all = packed_all[:, a_rows_own:].reshape(dp_size, b_rows_own, kv_shard).reshape(
            TENANTS, rank_width, kv_shard
        )
        a_blocks = a_all[block_slot]
        b_blocks = b_all[block_slot].reshape(block_count, 2, PADDED_RANK, kv_shard)
    rank_of_block = tenant_rank[block_tenant].astype(jnp.float32)
    column_rank = (jnp.arange(rank_width) % PADDED_RANK).astype(jnp.float32)
    column_rank_mask = (column_rank[None, :] < rank_of_block[:, None]).astype(jnp.float32)
    adapter_scale_factor = adapter_alpha_factor / rank_of_block
    x_blocks = tokens_in.reshape(block_count, TENANT_BLOCK, feat_shard)
    dy_blocks = grad_out.reshape(block_count, TENANT_BLOCK, 2, kv_shard)
    mid_part = jnp.einsum("bnd,bdc->bnc", x_blocks, a_blocks, preferred_element_type=jnp.float32)
    back_part = jnp.einsum(
        "bnpk,bprk->bnpr", dy_blocks, b_blocks, preferred_element_type=jnp.float32
    ).reshape(block_count, TENANT_BLOCK, rank_width)
    mid_sum, backward_gradient_sum = tensor_sum_pair(mid_part, back_part)
    middle_rank_rows = (mid_sum * column_rank_mask[:, None, :]).astype(jnp.bfloat16)
    backward_token_rows = (
        backward_gradient_sum * (column_rank_mask * adapter_scale_factor[:, None])[:, None, :]
    ).astype(jnp.bfloat16)
    frozen_gradient_share = frozen_gradient(grad_out, base_weight, feat_shard)
    adapter_gradient_term = jnp.einsum(
        "bnc,bdc->bnd", backward_token_rows, a_blocks, preferred_element_type=jnp.float32
    ).reshape(tok_rows, feat_shard)
    input_gradient_layer = frozen_gradient_share + adapter_gradient_term
    if slot_major:
        a_grad, b_grad = slot_major_grads(
            tokens_in, grad_out, middle_rank_rows, backward_token_rows, block_slot,
            tenant_rank, tenant_slot,
        )
    else:
        a_terms = jnp.einsum(
            "bnd,bnc->bdc", x_blocks, backward_token_rows, preferred_element_type=jnp.float32
        )
        b_terms = (
            jnp.einsum(
                "bnpr,bnpk->bprk",
                middle_rank_rows.reshape(block_count, TENANT_BLOCK, 2, PADDED_RANK),
                dy_blocks,
                preferred_element_type=jnp.float32,
            )
            * adapter_scale_factor[:, None, None, None]
        )
        one_hot = (block_slot[None, :] == jnp.arange(TENANTS)[:, None]).astype(jnp.float32)
        a_flat = jnp.einsum("sb,bdc->sdc", one_hot, a_terms, precision=lax.Precision.HIGHEST).reshape(
            TENANTS * feat_shard, rank_width
        )
        b_flat = jnp.einsum("sb,bprk->sprk", one_hot, b_terms, precision=lax.Precision.HIGHEST).reshape(
            TENANTS * rank_width, kv_shard
        )
        a_per = a_flat.shape[0] // dp_size
        b_per = b_flat.shape[0] // dp_size
        b_wide = b_per * kv_shard // rank_width
        grad_pack = jnp.concatenate(
            [
                a_flat.reshape(dp_size, a_per, rank_width),
                b_flat.reshape(dp_size, b_wide, rank_width),
            ],
            axis=1,
        ).reshape(dp_size * (a_per + b_wide), rank_width)
        grad_parts = lax.all_to_all(
            grad_pack.astype(jnp.bfloat16).reshape(dp_size, a_per + b_wide, rank_width),
            "dp",
            split_axis=0,
            concat_axis=0,
            tiled=True,
        )
        grad_own = jnp.sum(grad_parts.astype(jnp.float32), axis=0)
        a_grad = grad_own[:a_per]
        b_grad = grad_own[a_per:].reshape(b_per, kv_shard)
    return (
        input_gradient_layer,
        a_grad,
        b_grad,
        adam_step(a_grad, a_first, a_second),
        adam_step(b_grad, b_first, b_second),
    )


def solution(mesh):
    in_specs = (
        P("dp", "tensor"),
        P("dp", None, "tensor"),
        P(None, None, "tensor"),
        P(("tensor", "dp"), None),
        P(("tensor", "dp"), None),
        P(("tensor", "dp"), None),
        P(("tensor", "dp"), None),
        P(("tensor", "dp"), None),
        P(("tensor", "dp"), None),
        P("dp"),
        P(),
        P(),
    )
    out_specs = (
        P("dp", "tensor"),
        P(("tensor", "dp"), None),
        P(("tensor", "dp"), None),
        P(("tensor", "dp"), None),
        P(("tensor", "dp"), None),
    )
    return jax.shard_map(local, mesh=mesh, in_specs=in_specs, out_specs=out_specs, check_vma=False)
```

```python
import jax
import jax.numpy as jnp
from jax import lax
from jax.sharding import PartitionSpec as P

PADDED_RANK = 64
TENANTS = 8
TENANT_BLOCK = 128


adapter_alpha_factor = 32.0
beta_one = 0.9
beta_two = 0.999
adam_eps = 1e-08
corr_one = 1.0 - 0.9**3
corr_two = 1.0 - 0.999**3


def adam_step(grad_value, first_moment, second_moment):
    new_first = beta_one * first_moment + (1.0 - beta_one) * grad_value
    new_second = beta_two * second_moment + (1.0 - beta_two) * grad_value * grad_value
    return new_first / corr_one / (jnp.sqrt(new_second / corr_two) + adam_eps)


def tensor_sum_pair(first, second):
    size = lax.axis_size("tensor")
    width = first.shape[-1]
    both = jnp.concatenate([first, second], axis=-1)
    both = both + lax.ppermute(both, "tensor", [(i, i ^ 1) for i in range(size)])
    first, second = both[..., :width], both[..., width:]
    step = 2
    while step < size:
        pairs = [(i, i ^ step) for i in range(size)]
        first = first + lax.ppermute(first, "tensor", pairs)
        second = second + lax.ppermute(second, "tensor", pairs)
        step *= 2
    return first, second


def tensor_sum(parts):
    size = lax.axis_size("tensor")
    step = 1
    while step < size:
        pairs = [(i, i ^ step) for i in range(size)]
        parts = tuple(p + lax.ppermute(p, "tensor", pairs) for p in parts)
        step *= 2
    return parts


def frozen_gradient(grad_out, base_weight, feat_shard):
    tok_rows, _, kv_shard = grad_out.shape
    t_size = lax.axis_size("tensor")
    if t_size != 4:
        weight_split = jnp.transpose(
            base_weight.reshape(2, t_size, feat_shard, kv_shard), (1, 0, 2, 3)
        )
        weight_rows = lax.all_to_all(weight_split, "tensor", split_axis=0, concat_axis=0, tiled=True)
        dy_full = lax.all_gather(grad_out, "tensor", axis=0, tiled=False)
        return jnp.einsum("jtpk,jpdk->td", dy_full, weight_rows, preferred_element_type=jnp.float32)
    me = lax.axis_index("tensor")
    core_bit = me % 2
    row_bit = me // 2
    by_bits = base_weight.reshape(2, 2, 2, feat_shard, kv_shard)
    to_partner = lax.dynamic_index_in_dim(by_bits, 1 - core_bit, axis=2, keepdims=False)
    own_w = lax.dynamic_index_in_dim(by_bits, core_bit, axis=2, keepdims=False)
    core_pairs = [(i, i ^ 1) for i in range(t_size)]
    row_pairs = [(i, i ^ 2) for i in range(t_size)]
    partner_w = lax.ppermute(to_partner, "tensor", core_pairs)
    partner_dy = lax.ppermute(grad_out, "tensor", core_pairs)

    def chip_partial(bit):
        own = lax.dynamic_index_in_dim(own_w, bit, axis=1, keepdims=False)
        other = lax.dynamic_index_in_dim(partner_w, bit, axis=1, keepdims=False)
        first = jnp.einsum("tpk,pdk->td", grad_out, own, preferred_element_type=jnp.float32)
        second = jnp.einsum("tpk,pdk->td", partner_dy, other, preferred_element_type=jnp.float32)
        return first + second

    far_part = chip_partial(1 - row_bit).astype(jnp.bfloat16)
    half = tok_rows // 2
    far_in = jnp.concatenate(
        [
            lax.ppermute(far_part[:half], "tensor", row_pairs),
            lax.ppermute(far_part[half:], "tensor", row_pairs),
        ],
        axis=0,
    )
    return chip_partial(row_bit) + far_in.astype(jnp.float32)


def slot_major_grads(
    tokens_in, grad_out, middle_rank_rows, backward_token_rows, block_slot, tenant_rank, tenant_slot
):
    tok_rows, feat_shard = tokens_in.shape
    kv_shard = grad_out.shape[2]
    rank_width = backward_token_rows.shape[-1]
    token_slot = jnp.repeat(block_slot, TENANT_BLOCK)
    slot_hot = token_slot[:, None] == jnp.arange(TENANTS)[None, :]
    back_rows = backward_token_rows.reshape(tok_rows, rank_width)
    back_sel = jnp.where(slot_hot[:, :, None], back_rows[:, None, :], jnp.zeros((), back_rows.dtype))
    a_sc = jnp.einsum("nsc,nd->scd", back_sel, tokens_in, preferred_element_type=jnp.float32)
    mid_rows = middle_rank_rows.reshape(tok_rows, 2, PADDED_RANK)
    mid_sel = jnp.where(
        slot_hot[:, :, None, None], mid_rows[:, None, :, :], jnp.zeros((), mid_rows.dtype)
    )
    b_sc = jnp.einsum("nspr,npk->sprk", mid_sel, grad_out, preferred_element_type=jnp.float32)
    slot_tenant = jnp.argsort(tenant_slot)
    slot_scale = adapter_alpha_factor / tenant_rank[slot_tenant].astype(jnp.float32)
    b_sc = b_sc * slot_scale[:, None, None, None]
    full = jnp.concatenate([a_sc, b_sc.reshape(TENANTS, rank_width, kv_shard)], axis=2)
    own = grouped_exchange(full)
    return own[:, :feat_shard].T, own[:, feat_shard:]


def grouped_exchange(full):
    n = full.shape[0]
    if n % 4:
        recv = lax.all_to_all(full.astype(jnp.bfloat16), "dp", split_axis=0, concat_axis=0, tiled=True)
        return jnp.sum(recv.astype(jnp.float32), axis=0)
    groups = n // 4
    me = lax.axis_index("dp")
    member = me % 4
    group = me // 4
    by_member = full.reshape(groups, 4, *full.shape[1:])
    acc = lax.dynamic_index_in_dim(by_member, member, axis=1, keepdims=False)
    for m in (1, 2, 3):
        pairs = [(i, (i // 4) * 4 + ((i % 4) ^ m)) for i in range(n)]
        part = lax.dynamic_index_in_dim(by_member, member ^ m, axis=1, keepdims=False)
        acc = acc + lax.ppermute(part.astype(jnp.bfloat16), "dp", pairs).astype(jnp.float32)
    total = lax.dynamic_index_in_dim(acc, group, axis=0, keepdims=False)
    for m in range(1, groups):
        pairs = [(i, ((i // 4 + m) % groups) * 4 + i % 4) for i in range(n)]
        part = lax.dynamic_index_in_dim(acc, (group + m) % groups, axis=0, keepdims=False)
        total = total + lax.ppermute(part.astype(jnp.bfloat16), "dp", pairs).astype(jnp.float32)
    return total


def split_local(
    tokens_in,
    grad_out,
    base_weight,
    a_master,
    b_master,
    a_first,
    a_second,
    b_first,
    b_second,
    block_tenant,
    tenant_rank,
    tenant_slot,
):
    tok_rows, feat_shard = tokens_in.shape
    kv_shard = grad_out.shape[2]
    rank_width = a_master.shape[1]
    block_count = tok_rows // TENANT_BLOCK
    block_slot = tenant_slot[block_tenant]
    b_all = lax.all_gather(b_master.astype(jnp.bfloat16), "dp", axis=0, tiled=False)
    a_in, b_all = lax.optimization_barrier((a_master.astype(jnp.bfloat16), b_all))
    a_all = lax.all_gather(a_in, "dp", axis=0, tiled=False)
    rank_of_block = tenant_rank[block_tenant].astype(jnp.float32)
    column_rank = (jnp.arange(rank_width) % PADDED_RANK).astype(jnp.float32)
    column_rank_mask = (column_rank[None, :] < rank_of_block[:, None]).astype(jnp.float32)
    adapter_scale_factor = adapter_alpha_factor / rank_of_block
    dy_blocks = grad_out.reshape(block_count, TENANT_BLOCK, 2, kv_shard)
    b_blocks = jnp.take(b_all, block_slot, axis=0).reshape(block_count, 2, PADDED_RANK, kv_shard)
    back_part = jnp.einsum(
        "bnpk,bprk->bnpr", dy_blocks, b_blocks, preferred_element_type=jnp.float32
    ).reshape(block_count, TENANT_BLOCK, rank_width)
    backward_gradient_sum = tensor_sum((back_part,))[0]
    backward_token_rows = (
        backward_gradient_sum * (column_rank_mask * adapter_scale_factor[:, None])[:, None, :]
    ).astype(jnp.bfloat16)
    token_slot = jnp.repeat(block_slot, TENANT_BLOCK)
    slot_hot = token_slot[:, None] == jnp.arange(TENANTS)[None, :]
    back_rows = backward_token_rows.reshape(tok_rows, rank_width)
    back_sel = jnp.where(slot_hot[:, :, None], back_rows[:, None, :], jnp.zeros((), back_rows.dtype))
    a_sc = jnp.einsum("nsc,nd->scd", back_sel, tokens_in, preferred_element_type=jnp.float32)
    a_grad = grouped_exchange(a_sc).T
    a_blocks = jnp.take(a_all, block_slot, axis=0)
    x_blocks = tokens_in.reshape(block_count, TENANT_BLOCK, feat_shard)
    mid_part = jnp.einsum("bnd,bdc->bnc", x_blocks, a_blocks, preferred_element_type=jnp.float32)
    mid_sum = tensor_sum((mid_part,))[0]
    middle_rank_rows = (mid_sum * column_rank_mask[:, None, :]).astype(jnp.bfloat16)
    mid_rows = middle_rank_rows.reshape(tok_rows, 2, PADDED_RANK)
    mid_sel = jnp.where(
        slot_hot[:, :, None, None], mid_rows[:, None, :, :], jnp.zeros((), mid_rows.dtype)
    )
    b_sc = jnp.einsum("nspr,npk->sprk", mid_sel, grad_out, preferred_element_type=jnp.float32)
    slot_tenant = jnp.argsort(tenant_slot)
    slot_scale = adapter_alpha_factor / tenant_rank[slot_tenant].astype(jnp.float32)
    b_sc = b_sc * slot_scale[:, None, None, None]
    b_grad = grouped_exchange(b_sc.reshape(TENANTS, rank_width, kv_shard))
    frozen_gradient_share = frozen_gradient(grad_out, base_weight, feat_shard)
    adapter_gradient_term = jnp.einsum(
        "bnc,bdc->bnd", backward_token_rows, a_blocks, preferred_element_type=jnp.float32
    ).reshape(tok_rows, feat_shard)
    input_gradient_layer = frozen_gradient_share + adapter_gradient_term
    return (
        input_gradient_layer,
        a_grad,
        b_grad,
        adam_step(a_grad, a_first, a_second),
        adam_step(b_grad, b_first, b_second),
    )


def local(
    tokens_in,
    grad_out,
    base_weight,
    a_master,
    b_master,
    a_first,
    a_second,
    b_first,
    b_second,
    block_tenant,
    tenant_rank,
    tenant_slot,
):
    tok_rows, feat_shard = tokens_in.shape
    kv_shard = grad_out.shape[2]
    rank_width = a_master.shape[1]
    block_count = tok_rows // TENANT_BLOCK
    dp_size = lax.axis_size("dp")
    a_rows_own = a_master.shape[0]
    b_rows_own = b_master.shape[0]
    b_as_a = b_master.astype(jnp.bfloat16).reshape(b_rows_own * kv_shard // rank_width, rank_width)
    packed = jnp.concatenate([a_master.astype(jnp.bfloat16), b_as_a], axis=0)
    packed_all = lax.all_gather(packed, "dp", axis=0, tiled=False)
    block_slot = tenant_slot[block_tenant]
    slot_major = dp_size == TENANTS
    if slot_major:
        picked = jnp.take(packed_all, block_slot, axis=0)
        a_blocks = picked[:, :a_rows_own]
        b_blocks = picked[:, a_rows_own:].reshape(block_count, 2, PADDED_RANK, kv_shard)
    else:
        a_all = packed_all[:, :a_rows_own].reshape(TENANTS, feat_shard, rank_width)
        b_all = packed_all[:, a_rows_own:].reshape(dp_size, b_rows_own, kv_shard).reshape(
            TENANTS, rank_width, kv_shard
        )
        a_blocks = a_all[block_slot]
        b_blocks = b_all[block_slot].reshape(block_count, 2, PADDED_RANK, kv_shard)
    rank_of_block = tenant_rank[block_tenant].astype(jnp.float32)
    column_rank = (jnp.arange(rank_width) % PADDED_RANK).astype(jnp.float32)
    column_rank_mask = (column_rank[None, :] < rank_of_block[:, None]).astype(jnp.float32)
    adapter_scale_factor = adapter_alpha_factor / rank_of_block
    x_blocks = tokens_in.reshape(block_count, TENANT_BLOCK, feat_shard)
    dy_blocks = grad_out.reshape(block_count, TENANT_BLOCK, 2, kv_shard)
    mid_part = jnp.einsum("bnd,bdc->bnc", x_blocks, a_blocks, preferred_element_type=jnp.float32)
    back_part = jnp.einsum(
        "bnpk,bprk->bnpr", dy_blocks, b_blocks, preferred_element_type=jnp.float32
    ).reshape(block_count, TENANT_BLOCK, rank_width)
    mid_sum, backward_gradient_sum = tensor_sum_pair(mid_part, back_part)
    middle_rank_rows = (mid_sum * column_rank_mask[:, None, :]).astype(jnp.bfloat16)
    backward_token_rows = (
        backward_gradient_sum * (column_rank_mask * adapter_scale_factor[:, None])[:, None, :]
    ).astype(jnp.bfloat16)
    frozen_gradient_share = frozen_gradient(grad_out, base_weight, feat_shard)
    adapter_gradient_term = jnp.einsum(
        "bnc,bdc->bnd", backward_token_rows, a_blocks, preferred_element_type=jnp.float32
    ).reshape(tok_rows, feat_shard)
    input_gradient_layer = frozen_gradient_share + adapter_gradient_term
    if slot_major:
        a_grad, b_grad = slot_major_grads(
            tokens_in, grad_out, middle_rank_rows, backward_token_rows, block_slot,
            tenant_rank, tenant_slot,
        )
    else:
        a_terms = jnp.einsum(
            "bnd,bnc->bdc", x_blocks, backward_token_rows, preferred_element_type=jnp.float32
        )
        b_terms = (
            jnp.einsum(
                "bnpr,bnpk->bprk",
                middle_rank_rows.reshape(block_count, TENANT_BLOCK, 2, PADDED_RANK),
                dy_blocks,
                preferred_element_type=jnp.float32,
            )
            * adapter_scale_factor[:, None, None, None]
        )
        one_hot = (block_slot[None, :] == jnp.arange(TENANTS)[:, None]).astype(jnp.float32)
        a_flat = jnp.einsum("sb,bdc->sdc", one_hot, a_terms, precision=lax.Precision.HIGHEST).reshape(
            TENANTS * feat_shard, rank_width
        )
        b_flat = jnp.einsum("sb,bprk->sprk", one_hot, b_terms, precision=lax.Precision.HIGHEST).reshape(
            TENANTS * rank_width, kv_shard
        )
        a_per = a_flat.shape[0] // dp_size
        b_per = b_flat.shape[0] // dp_size
        b_wide = b_per * kv_shard // rank_width
        grad_pack = jnp.concatenate(
            [
                a_flat.reshape(dp_size, a_per, rank_width),
                b_flat.reshape(dp_size, b_wide, rank_width),
            ],
            axis=1,
        ).reshape(dp_size * (a_per + b_wide), rank_width)
        grad_parts = lax.all_to_all(
            grad_pack.astype(jnp.bfloat16).reshape(dp_size, a_per + b_wide, rank_width),
            "dp",
            split_axis=0,
            concat_axis=0,
            tiled=True,
        )
        grad_own = jnp.sum(grad_parts.astype(jnp.float32), axis=0)
        a_grad = grad_own[:a_per]
        b_grad = grad_own[a_per:].reshape(b_per, kv_shard)
    return (
        input_gradient_layer,
        a_grad,
        b_grad,
        adam_step(a_grad, a_first, a_second),
        adam_step(b_grad, b_first, b_second),
    )


def solution(mesh):
    in_specs = (
        P("dp", "tensor"),
        P("dp", None, "tensor"),
        P(None, None, "tensor"),
        P(("tensor", "dp"), None),
        P(("tensor", "dp"), None),
        P(("tensor", "dp"), None),
        P(("tensor", "dp"), None),
        P(("tensor", "dp"), None),
        P(("tensor", "dp"), None),
        P("dp"),
        P(),
        P(),
    )
    out_specs = (
        P("dp", "tensor"),
        P(("tensor", "dp"), None),
        P(("tensor", "dp"), None),
        P(("tensor", "dp"), None),
        P(("tensor", "dp"), None),
    )
    body = split_local if mesh.shape["dp"] == TENANTS else local
    return jax.shard_map(body, mesh=mesh, in_specs=in_specs, out_specs=out_specs, check_vma=False)
```

```python
import jax
import jax.numpy as jnp
from jax import lax
from jax.sharding import PartitionSpec as P

PADDED_RANK = 64
TENANTS = 8
TENANT_BLOCK = 128


adapter_alpha_factor = 32.0
beta_one = 0.9
beta_two = 0.999
adam_eps = 1e-08
corr_one = 1.0 - 0.9**3
corr_two = 1.0 - 0.999**3


def adam_step(grad_value, first_moment, second_moment):
    new_first = beta_one * first_moment + (1.0 - beta_one) * grad_value
    new_second = beta_two * second_moment + (1.0 - beta_two) * grad_value * grad_value
    return new_first / corr_one / (jnp.sqrt(new_second / corr_two) + adam_eps)


def tensor_sum_pair(first, second):
    size = lax.axis_size("tensor")
    width = first.shape[-1]
    both = jnp.concatenate([first, second], axis=-1)
    both = both + lax.ppermute(both, "tensor", [(i, i ^ 1) for i in range(size)])
    first, second = both[..., :width], both[..., width:]
    step = 2
    while step < size:
        pairs = [(i, i ^ step) for i in range(size)]
        first = first + lax.ppermute(first, "tensor", pairs)
        second = second + lax.ppermute(second, "tensor", pairs)
        step *= 2
    return first, second


def tensor_sum(parts):
    size = lax.axis_size("tensor")
    step = 1
    while step < size:
        pairs = [(i, i ^ step) for i in range(size)]
        parts = tuple(p + lax.ppermute(p, "tensor", pairs) for p in parts)
        step *= 2
    return parts


def frozen_gradient(grad_out, base_weight, feat_shard):
    tok_rows, _, kv_shard = grad_out.shape
    t_size = lax.axis_size("tensor")
    if t_size != 4:
        weight_split = jnp.transpose(
            base_weight.reshape(2, t_size, feat_shard, kv_shard), (1, 0, 2, 3)
        )
        weight_rows = lax.all_to_all(weight_split, "tensor", split_axis=0, concat_axis=0, tiled=True)
        dy_full = lax.all_gather(grad_out, "tensor", axis=0, tiled=False)
        return jnp.einsum("jtpk,jpdk->td", dy_full, weight_rows, preferred_element_type=jnp.float32)
    me = lax.axis_index("tensor")
    core_bit = me % 2
    row_bit = me // 2
    by_bits = base_weight.reshape(2, 2, 2, feat_shard, kv_shard)
    to_partner = lax.dynamic_index_in_dim(by_bits, 1 - core_bit, axis=2, keepdims=False)
    own_w = lax.dynamic_index_in_dim(by_bits, core_bit, axis=2, keepdims=False)
    core_pairs = [(i, i ^ 1) for i in range(t_size)]
    row_pairs = [(i, i ^ 2) for i in range(t_size)]
    partner_w = lax.ppermute(to_partner, "tensor", core_pairs)
    partner_dy = lax.ppermute(grad_out, "tensor", core_pairs)

    def chip_partial(bit):
        own = lax.dynamic_index_in_dim(own_w, bit, axis=1, keepdims=False)
        other = lax.dynamic_index_in_dim(partner_w, bit, axis=1, keepdims=False)
        first = jnp.einsum("tpk,pdk->td", grad_out, own, preferred_element_type=jnp.float32)
        second = jnp.einsum("tpk,pdk->td", partner_dy, other, preferred_element_type=jnp.float32)
        return first + second

    far_part = chip_partial(1 - row_bit).astype(jnp.bfloat16)
    half = tok_rows // 2
    far_in = jnp.concatenate(
        [
            lax.ppermute(far_part[:half], "tensor", row_pairs),
            lax.ppermute(far_part[half:], "tensor", row_pairs),
        ],
        axis=0,
    )
    return chip_partial(row_bit) + far_in.astype(jnp.float32)


def slot_major_grads(
    tokens_in, grad_out, middle_rank_rows, backward_token_rows, block_slot, tenant_rank, tenant_slot
):
    tok_rows, feat_shard = tokens_in.shape
    kv_shard = grad_out.shape[2]
    rank_width = backward_token_rows.shape[-1]
    token_slot = jnp.repeat(block_slot, TENANT_BLOCK)
    slot_hot = token_slot[:, None] == jnp.arange(TENANTS)[None, :]
    back_rows = backward_token_rows.reshape(tok_rows, rank_width)
    back_sel = jnp.where(slot_hot[:, :, None], back_rows[:, None, :], jnp.zeros((), back_rows.dtype))
    a_sc = jnp.einsum("nsc,nd->scd", back_sel, tokens_in, preferred_element_type=jnp.float32)
    mid_rows = middle_rank_rows.reshape(tok_rows, 2, PADDED_RANK)
    mid_sel = jnp.where(
        slot_hot[:, :, None, None], mid_rows[:, None, :, :], jnp.zeros((), mid_rows.dtype)
    )
    b_sc = jnp.einsum("nspr,npk->sprk", mid_sel, grad_out, preferred_element_type=jnp.float32)
    slot_tenant = jnp.argsort(tenant_slot)
    slot_scale = adapter_alpha_factor / tenant_rank[slot_tenant].astype(jnp.float32)
    b_sc = b_sc * slot_scale[:, None, None, None]
    full = jnp.concatenate([a_sc, b_sc.reshape(TENANTS, rank_width, kv_shard)], axis=2)
    own = grouped_exchange(full)
    return own[:, :feat_shard].T, own[:, feat_shard:]


def grouped_exchange(full):
    n = full.shape[0]
    if n % 4:
        recv = lax.all_to_all(full.astype(jnp.bfloat16), "dp", split_axis=0, concat_axis=0, tiled=True)
        return jnp.sum(recv.astype(jnp.float32), axis=0)
    groups = n // 4
    me = lax.axis_index("dp")
    member = me % 4
    group = me // 4
    by_member = full.reshape(groups, 4, *full.shape[1:])
    acc = lax.dynamic_index_in_dim(by_member, member, axis=1, keepdims=False)
    for m in (1, 2, 3):
        pairs = [(i, (i // 4) * 4 + ((i % 4) ^ m)) for i in range(n)]
        part = lax.dynamic_index_in_dim(by_member, member ^ m, axis=1, keepdims=False)
        acc = acc + lax.ppermute(part.astype(jnp.bfloat16), "dp", pairs).astype(jnp.float32)
    total = lax.dynamic_index_in_dim(acc, group, axis=0, keepdims=False)
    for m in range(1, groups):
        pairs = [(i, ((i // 4 + m) % groups) * 4 + i % 4) for i in range(n)]
        part = lax.dynamic_index_in_dim(acc, (group + m) % groups, axis=0, keepdims=False)
        total = total + lax.ppermute(part.astype(jnp.bfloat16), "dp", pairs).astype(jnp.float32)
    return total


def local(
    tokens_in,
    grad_out,
    base_weight,
    a_master,
    b_master,
    a_first,
    a_second,
    b_first,
    b_second,
    block_tenant,
    tenant_rank,
    tenant_slot,
):
    tok_rows, feat_shard = tokens_in.shape
    kv_shard = grad_out.shape[2]
    rank_width = a_master.shape[1]
    block_count = tok_rows // TENANT_BLOCK
    dp_size = lax.axis_size("dp")
    a_rows_own = a_master.shape[0]
    b_rows_own = b_master.shape[0]
    b_as_a = b_master.astype(jnp.bfloat16).reshape(b_rows_own * kv_shard // rank_width, rank_width)
    packed = jnp.concatenate([a_master.astype(jnp.bfloat16), b_as_a], axis=0)
    packed_all = lax.all_gather(packed, "dp", axis=0, tiled=False)
    frozen_gradient_share = frozen_gradient(grad_out, base_weight, feat_shard)
    frozen_gradient_share, packed_all = lax.optimization_barrier((frozen_gradient_share, packed_all))
    block_slot = tenant_slot[block_tenant]
    slot_major = dp_size == TENANTS
    if slot_major:
        picked = jnp.take(packed_all, block_slot, axis=0, mode="clip")
        a_blocks = picked[:, :a_rows_own]
        b_blocks = picked[:, a_rows_own:].reshape(block_count, 2, PADDED_RANK, kv_shard)
    else:
        a_all = packed_all[:, :a_rows_own].reshape(TENANTS, feat_shard, rank_width)
        b_all = packed_all[:, a_rows_own:].reshape(dp_size, b_rows_own, kv_shard).reshape(
            TENANTS, rank_width, kv_shard
        )
        a_blocks = a_all[block_slot]
        b_blocks = b_all[block_slot].reshape(block_count, 2, PADDED_RANK, kv_shard)
    rank_of_block = tenant_rank[block_tenant].astype(jnp.float32)
    column_rank = (jnp.arange(rank_width) % PADDED_RANK).astype(jnp.float32)
    column_rank_mask = (column_rank[None, :] < rank_of_block[:, None]).astype(jnp.float32)
    adapter_scale_factor = adapter_alpha_factor / rank_of_block
    x_blocks = tokens_in.reshape(block_count, TENANT_BLOCK, feat_shard)
    dy_blocks = grad_out.reshape(block_count, TENANT_BLOCK, 2, kv_shard)
    mid_part = jnp.einsum("bnd,bdc->bnc", x_blocks, a_blocks, preferred_element_type=jnp.float32)
    back_part = jnp.einsum(
        "bnpk,bprk->bnpr", dy_blocks, b_blocks, preferred_element_type=jnp.float32
    ).reshape(block_count, TENANT_BLOCK, rank_width)
    mid_sum, backward_gradient_sum = tensor_sum_pair(mid_part, back_part)
    middle_rank_rows = (mid_sum * column_rank_mask[:, None, :]).astype(jnp.bfloat16)
    backward_token_rows = (
        backward_gradient_sum * (column_rank_mask * adapter_scale_factor[:, None])[:, None, :]
    ).astype(jnp.bfloat16)
    adapter_gradient_term = jnp.einsum(
        "bnc,bdc->bnd", backward_token_rows, a_blocks, preferred_element_type=jnp.float32
    ).reshape(tok_rows, feat_shard)
    input_gradient_layer = frozen_gradient_share + adapter_gradient_term
    if slot_major:
        a_grad, b_grad = slot_major_grads(
            tokens_in, grad_out, middle_rank_rows, backward_token_rows, block_slot,
            tenant_rank, tenant_slot,
        )
    else:
        a_terms = jnp.einsum(
            "bnd,bnc->bdc", x_blocks, backward_token_rows, preferred_element_type=jnp.float32
        )
        b_terms = (
            jnp.einsum(
                "bnpr,bnpk->bprk",
                middle_rank_rows.reshape(block_count, TENANT_BLOCK, 2, PADDED_RANK),
                dy_blocks,
                preferred_element_type=jnp.float32,
            )
            * adapter_scale_factor[:, None, None, None]
        )
        one_hot = (block_slot[None, :] == jnp.arange(TENANTS)[:, None]).astype(jnp.float32)
        a_flat = jnp.einsum("sb,bdc->sdc", one_hot, a_terms, precision=lax.Precision.HIGHEST).reshape(
            TENANTS * feat_shard, rank_width
        )
        b_flat = jnp.einsum("sb,bprk->sprk", one_hot, b_terms, precision=lax.Precision.HIGHEST).reshape(
            TENANTS * rank_width, kv_shard
        )
        a_per = a_flat.shape[0] // dp_size
        b_per = b_flat.shape[0] // dp_size
        b_wide = b_per * kv_shard // rank_width
        grad_pack = jnp.concatenate(
            [
                a_flat.reshape(dp_size, a_per, rank_width),
                b_flat.reshape(dp_size, b_wide, rank_width),
            ],
            axis=1,
        ).reshape(dp_size * (a_per + b_wide), rank_width)
        grad_parts = lax.all_to_all(
            grad_pack.astype(jnp.bfloat16).reshape(dp_size, a_per + b_wide, rank_width),
            "dp",
            split_axis=0,
            concat_axis=0,
            tiled=True,
        )
        grad_own = jnp.sum(grad_parts.astype(jnp.float32), axis=0)
        a_grad = grad_own[:a_per]
        b_grad = grad_own[a_per:].reshape(b_per, kv_shard)
    return (
        input_gradient_layer,
        a_grad,
        b_grad,
        adam_step(a_grad, a_first, a_second),
        adam_step(b_grad, b_first, b_second),
    )


def solution(mesh):
    in_specs = (
        P("dp", "tensor"),
        P("dp", None, "tensor"),
        P(None, None, "tensor"),
        P(("tensor", "dp"), None),
        P(("tensor", "dp"), None),
        P(("tensor", "dp"), None),
        P(("tensor", "dp"), None),
        P(("tensor", "dp"), None),
        P(("tensor", "dp"), None),
        P("dp"),
        P(),
        P(),
    )
    out_specs = (
        P("dp", "tensor"),
        P(("tensor", "dp"), None),
        P(("tensor", "dp"), None),
        P(("tensor", "dp"), None),
        P(("tensor", "dp"), None),
    )
    return jax.shard_map(local, mesh=mesh, in_specs=in_specs, out_specs=out_specs, check_vma=False)
```

```python
import jax
import jax.numpy as jnp
from jax import lax
from jax.sharding import PartitionSpec as P

PADDED_RANK = 64
TENANTS = 8
TENANT_BLOCK = 128


adapter_alpha_factor = 32.0
beta_one = 0.9
beta_two = 0.999
adam_eps = 1e-08
corr_one = 1.0 - 0.9**3
corr_two = 1.0 - 0.999**3


def adam_step(grad_value, first_moment, second_moment):
    new_first = beta_one * first_moment + (1.0 - beta_one) * grad_value
    new_second = beta_two * second_moment + (1.0 - beta_two) * grad_value * grad_value
    return new_first / corr_one / (jnp.sqrt(new_second / corr_two) + adam_eps)


def tensor_sum_pair(first, second):
    size = lax.axis_size("tensor")
    width = first.shape[-1]
    both = jnp.concatenate([first, second], axis=-1)
    both = both + lax.ppermute(both, "tensor", [(i, i ^ 1) for i in range(size)])
    first, second = both[..., :width], both[..., width:]
    step = 2
    while step < size:
        pairs = [(i, i ^ step) for i in range(size)]
        first = first + lax.ppermute(first, "tensor", pairs)
        second = second + lax.ppermute(second, "tensor", pairs)
        step *= 2
    return first, second


def tensor_sum(parts):
    size = lax.axis_size("tensor")
    step = 1
    while step < size:
        pairs = [(i, i ^ step) for i in range(size)]
        parts = tuple(p + lax.ppermute(p, "tensor", pairs) for p in parts)
        step *= 2
    return parts


def frozen_gradient(grad_out, base_weight, feat_shard):
    tok_rows, _, kv_shard = grad_out.shape
    t_size = lax.axis_size("tensor")
    if t_size != 4:
        weight_split = jnp.transpose(
            base_weight.reshape(2, t_size, feat_shard, kv_shard), (1, 0, 2, 3)
        )
        weight_rows = lax.all_to_all(weight_split, "tensor", split_axis=0, concat_axis=0, tiled=True)
        dy_full = lax.all_gather(grad_out, "tensor", axis=0, tiled=False)
        return jnp.einsum("jtpk,jpdk->td", dy_full, weight_rows, preferred_element_type=jnp.float32)
    me = lax.axis_index("tensor")
    core_bit = me % 2
    row_bit = me // 2
    by_bits = base_weight.reshape(2, 2, 2, feat_shard, kv_shard)
    to_partner = lax.dynamic_index_in_dim(by_bits, 1 - core_bit, axis=2, keepdims=False)
    own_w = lax.dynamic_index_in_dim(by_bits, core_bit, axis=2, keepdims=False)
    core_pairs = [(i, i ^ 1) for i in range(t_size)]
    row_pairs = [(i, i ^ 2) for i in range(t_size)]
    partner_w = lax.ppermute(to_partner, "tensor", core_pairs)
    partner_dy = lax.ppermute(grad_out, "tensor", core_pairs)

    def chip_partial(bit):
        own = lax.dynamic_index_in_dim(own_w, bit, axis=1, keepdims=False)
        other = lax.dynamic_index_in_dim(partner_w, bit, axis=1, keepdims=False)
        first = jnp.einsum("tpk,pdk->td", grad_out, own, preferred_element_type=jnp.float32)
        second = jnp.einsum("tpk,pdk->td", partner_dy, other, preferred_element_type=jnp.float32)
        return first + second

    far_part = chip_partial(1 - row_bit).astype(jnp.bfloat16)
    half = tok_rows // 2
    far_in = jnp.concatenate(
        [
            lax.ppermute(far_part[:half], "tensor", row_pairs),
            lax.ppermute(far_part[half:], "tensor", row_pairs),
        ],
        axis=0,
    )
    return chip_partial(row_bit) + far_in.astype(jnp.float32)


def slot_major_grads(
    tokens_in, grad_out, middle_rank_rows, backward_token_rows, block_slot, tenant_rank, tenant_slot
):
    tok_rows, feat_shard = tokens_in.shape
    kv_shard = grad_out.shape[2]
    rank_width = backward_token_rows.shape[-1]
    token_slot = jnp.repeat(block_slot, TENANT_BLOCK)
    slot_hot = token_slot[:, None] == jnp.arange(TENANTS)[None, :]
    back_rows = backward_token_rows.reshape(tok_rows, rank_width)
    back_sel = jnp.where(slot_hot[:, :, None], back_rows[:, None, :], jnp.zeros((), back_rows.dtype))
    a_sc = jnp.einsum("nsc,nd->scd", back_sel, tokens_in, preferred_element_type=jnp.float32)
    mid_rows = middle_rank_rows.reshape(tok_rows, 2, PADDED_RANK)
    mid_sel = jnp.where(
        slot_hot[:, :, None, None], mid_rows[:, None, :, :], jnp.zeros((), mid_rows.dtype)
    )
    b_sc = jnp.einsum("nspr,npk->sprk", mid_sel, grad_out, preferred_element_type=jnp.float32)
    slot_tenant = jnp.argsort(tenant_slot)
    slot_scale = adapter_alpha_factor / tenant_rank[slot_tenant].astype(jnp.float32)
    b_sc = b_sc * slot_scale[:, None, None, None]
    a_own = grouped_exchange(a_sc)
    b_own = grouped_exchange(b_sc.reshape(TENANTS, rank_width, kv_shard))
    return a_own.T, b_own


def grouped_exchange(full):
    n = full.shape[0]
    if n % 4:
        recv = lax.all_to_all(full.astype(jnp.bfloat16), "dp", split_axis=0, concat_axis=0, tiled=True)
        return jnp.sum(recv.astype(jnp.float32), axis=0)
    groups = n // 4
    me = lax.axis_index("dp")
    member = me % 4
    group = me // 4
    by_member = full.reshape(groups, 4, *full.shape[1:])
    acc = lax.dynamic_index_in_dim(by_member, member, axis=1, keepdims=False)
    for m in (1, 2, 3):
        pairs = [(i, (i // 4) * 4 + ((i % 4) ^ m)) for i in range(n)]
        part = lax.dynamic_index_in_dim(by_member, member ^ m, axis=1, keepdims=False)
        acc = acc + lax.ppermute(part.astype(jnp.bfloat16), "dp", pairs).astype(jnp.float32)
    total = lax.dynamic_index_in_dim(acc, group, axis=0, keepdims=False)
    for m in range(1, groups):
        pairs = [(i, ((i // 4 + m) % groups) * 4 + i % 4) for i in range(n)]
        part = lax.dynamic_index_in_dim(acc, (group + m) % groups, axis=0, keepdims=False)
        total = total + lax.ppermute(part.astype(jnp.bfloat16), "dp", pairs).astype(jnp.float32)
    return total


def local(
    tokens_in,
    grad_out,
    base_weight,
    a_master,
    b_master,
    a_first,
    a_second,
    b_first,
    b_second,
    block_tenant,
    tenant_rank,
    tenant_slot,
):
    tok_rows, feat_shard = tokens_in.shape
    kv_shard = grad_out.shape[2]
    rank_width = a_master.shape[1]
    block_count = tok_rows // TENANT_BLOCK
    dp_size = lax.axis_size("dp")
    a_rows_own = a_master.shape[0]
    b_rows_own = b_master.shape[0]
    b_as_a = b_master.astype(jnp.bfloat16).reshape(b_rows_own * kv_shard // rank_width, rank_width)
    packed = jnp.concatenate([a_master.astype(jnp.bfloat16), b_as_a], axis=0)
    packed_all = lax.all_gather(packed, "dp", axis=0, tiled=False)
    frozen_gradient_share = frozen_gradient(grad_out, base_weight, feat_shard)
    frozen_gradient_share, packed_all = lax.optimization_barrier((frozen_gradient_share, packed_all))
    block_slot = tenant_slot[block_tenant]
    slot_major = dp_size == TENANTS
    if slot_major:
        picked = jnp.take(packed_all, block_slot, axis=0, mode="clip")
        a_blocks = picked[:, :a_rows_own]
        b_blocks = picked[:, a_rows_own:].reshape(block_count, 2, PADDED_RANK, kv_shard)
    else:
        a_all = packed_all[:, :a_rows_own].reshape(TENANTS, feat_shard, rank_width)
        b_all = packed_all[:, a_rows_own:].reshape(dp_size, b_rows_own, kv_shard).reshape(
            TENANTS, rank_width, kv_shard
        )
        a_blocks = a_all[block_slot]
        b_blocks = b_all[block_slot].reshape(block_count, 2, PADDED_RANK, kv_shard)
    rank_of_block = tenant_rank[block_tenant].astype(jnp.float32)
    column_rank = (jnp.arange(rank_width) % PADDED_RANK).astype(jnp.float32)
    column_rank_mask = (column_rank[None, :] < rank_of_block[:, None]).astype(jnp.float32)
    adapter_scale_factor = adapter_alpha_factor / rank_of_block
    x_blocks = tokens_in.reshape(block_count, TENANT_BLOCK, feat_shard)
    dy_blocks = grad_out.reshape(block_count, TENANT_BLOCK, 2, kv_shard)
    mid_part = jnp.einsum("bnd,bdc->bnc", x_blocks, a_blocks, preferred_element_type=jnp.float32)
    back_part = jnp.einsum(
        "bnpk,bprk->bnpr", dy_blocks, b_blocks, preferred_element_type=jnp.float32
    ).reshape(block_count, TENANT_BLOCK, rank_width)
    backward_gradient_sum = tensor_sum((back_part,))[0]
    mid_sum = tensor_sum((mid_part,))[0]
    middle_rank_rows = (mid_sum * column_rank_mask[:, None, :]).astype(jnp.bfloat16)
    backward_token_rows = (
        backward_gradient_sum * (column_rank_mask * adapter_scale_factor[:, None])[:, None, :]
    ).astype(jnp.bfloat16)
    adapter_gradient_term = jnp.einsum(
        "bnc,bdc->bnd", backward_token_rows, a_blocks, preferred_element_type=jnp.float32
    ).reshape(tok_rows, feat_shard)
    input_gradient_layer = frozen_gradient_share + adapter_gradient_term
    if slot_major:
        a_grad, b_grad = slot_major_grads(
            tokens_in, grad_out, middle_rank_rows, backward_token_rows, block_slot,
            tenant_rank, tenant_slot,
        )
    else:
        a_terms = jnp.einsum(
            "bnd,bnc->bdc", x_blocks, backward_token_rows, preferred_element_type=jnp.float32
        )
        b_terms = (
            jnp.einsum(
                "bnpr,bnpk->bprk",
                middle_rank_rows.reshape(block_count, TENANT_BLOCK, 2, PADDED_RANK),
                dy_blocks,
                preferred_element_type=jnp.float32,
            )
            * adapter_scale_factor[:, None, None, None]
        )
        one_hot = (block_slot[None, :] == jnp.arange(TENANTS)[:, None]).astype(jnp.float32)
        a_flat = jnp.einsum("sb,bdc->sdc", one_hot, a_terms, precision=lax.Precision.HIGHEST).reshape(
            TENANTS * feat_shard, rank_width
        )
        b_flat = jnp.einsum("sb,bprk->sprk", one_hot, b_terms, precision=lax.Precision.HIGHEST).reshape(
            TENANTS * rank_width, kv_shard
        )
        a_per = a_flat.shape[0] // dp_size
        b_per = b_flat.shape[0] // dp_size
        b_wide = b_per * kv_shard // rank_width
        grad_pack = jnp.concatenate(
            [
                a_flat.reshape(dp_size, a_per, rank_width),
                b_flat.reshape(dp_size, b_wide, rank_width),
            ],
            axis=1,
        ).reshape(dp_size * (a_per + b_wide), rank_width)
        grad_parts = lax.all_to_all(
            grad_pack.astype(jnp.bfloat16).reshape(dp_size, a_per + b_wide, rank_width),
            "dp",
            split_axis=0,
            concat_axis=0,
            tiled=True,
        )
        grad_own = jnp.sum(grad_parts.astype(jnp.float32), axis=0)
        a_grad = grad_own[:a_per]
        b_grad = grad_own[a_per:].reshape(b_per, kv_shard)
    return (
        input_gradient_layer,
        a_grad,
        b_grad,
        adam_step(a_grad, a_first, a_second),
        adam_step(b_grad, b_first, b_second),
    )


def solution(mesh):
    in_specs = (
        P("dp", "tensor"),
        P("dp", None, "tensor"),
        P(None, None, "tensor"),
        P(("tensor", "dp"), None),
        P(("tensor", "dp"), None),
        P(("tensor", "dp"), None),
        P(("tensor", "dp"), None),
        P(("tensor", "dp"), None),
        P(("tensor", "dp"), None),
        P("dp"),
        P(),
        P(),
    )
    out_specs = (
        P("dp", "tensor"),
        P(("tensor", "dp"), None),
        P(("tensor", "dp"), None),
        P(("tensor", "dp"), None),
        P(("tensor", "dp"), None),
    )
    return jax.shard_map(local, mesh=mesh, in_specs=in_specs, out_specs=out_specs, check_vma=False)
```

```python
import jax
import jax.numpy as jnp
from jax import lax
from jax.sharding import PartitionSpec as P

PADDED_RANK = 64
TENANTS = 8
TENANT_BLOCK = 128


adapter_alpha_factor = 32.0
beta_one = 0.9
beta_two = 0.999
adam_eps = 1e-08
corr_one = 1.0 - 0.9**3
corr_two = 1.0 - 0.999**3


def adam_step(grad_value, first_moment, second_moment):
    new_first = beta_one * first_moment + (1.0 - beta_one) * grad_value
    new_second = beta_two * second_moment + (1.0 - beta_two) * grad_value * grad_value
    return new_first / corr_one / (jnp.sqrt(new_second / corr_two) + adam_eps)


def tensor_sum_pair(first, second):
    size = lax.axis_size("tensor")
    width = first.shape[-1]
    both = jnp.concatenate([first, second], axis=-1)
    both = both + lax.ppermute(both, "tensor", [(i, i ^ 1) for i in range(size)])
    first, second = both[..., :width], both[..., width:]
    step = 2
    while step < size:
        pairs = [(i, i ^ step) for i in range(size)]
        first = first + lax.ppermute(first, "tensor", pairs)
        second = second + lax.ppermute(second, "tensor", pairs)
        step *= 2
    return first, second


def tensor_sum(parts):
    size = lax.axis_size("tensor")
    step = 1
    while step < size:
        pairs = [(i, i ^ step) for i in range(size)]
        parts = tuple(p + lax.ppermute(p, "tensor", pairs) for p in parts)
        step *= 2
    return parts


def frozen_gradient(grad_out, base_weight, feat_shard):
    tok_rows, _, kv_shard = grad_out.shape
    t_size = lax.axis_size("tensor")
    if t_size != 4:
        weight_split = jnp.transpose(
            base_weight.reshape(2, t_size, feat_shard, kv_shard), (1, 0, 2, 3)
        )
        weight_rows = lax.all_to_all(weight_split, "tensor", split_axis=0, concat_axis=0, tiled=True)
        dy_full = lax.all_gather(grad_out, "tensor", axis=0, tiled=False)
        return jnp.einsum("jtpk,jpdk->td", dy_full, weight_rows, preferred_element_type=jnp.float32)
    me = lax.axis_index("tensor")
    core_bit = me % 2
    row_bit = me // 2
    by_bits = base_weight.reshape(2, 2, 2, feat_shard, kv_shard)
    to_partner = lax.dynamic_index_in_dim(by_bits, 1 - core_bit, axis=2, keepdims=False)
    own_w = lax.dynamic_index_in_dim(by_bits, core_bit, axis=2, keepdims=False)
    core_pairs = [(i, i ^ 1) for i in range(t_size)]
    row_pairs = [(i, i ^ 2) for i in range(t_size)]
    partner_w = lax.ppermute(to_partner, "tensor", core_pairs)
    partner_dy = lax.ppermute(grad_out, "tensor", core_pairs)

    def chip_partial(bit):
        own = lax.dynamic_index_in_dim(own_w, bit, axis=1, keepdims=False)
        other = lax.dynamic_index_in_dim(partner_w, bit, axis=1, keepdims=False)
        first = jnp.einsum("tpk,pdk->td", grad_out, own, preferred_element_type=jnp.float32)
        second = jnp.einsum("tpk,pdk->td", partner_dy, other, preferred_element_type=jnp.float32)
        return first + second

    far_part = chip_partial(1 - row_bit).astype(jnp.bfloat16)
    half = tok_rows // 2
    far_in = jnp.concatenate(
        [
            lax.ppermute(far_part[:half], "tensor", row_pairs),
            lax.ppermute(far_part[half:], "tensor", row_pairs),
        ],
        axis=0,
    )
    return chip_partial(row_bit) + far_in.astype(jnp.float32)


def slot_major_grads(
    tokens_in, grad_out, middle_rank_rows, backward_token_rows, block_slot, tenant_rank, tenant_slot
):
    tok_rows, feat_shard = tokens_in.shape
    kv_shard = grad_out.shape[2]
    rank_width = backward_token_rows.shape[-1]
    token_slot = jnp.repeat(block_slot, TENANT_BLOCK)
    slot_hot = token_slot[:, None] == jnp.arange(TENANTS)[None, :]
    back_rows = backward_token_rows.reshape(tok_rows, rank_width)
    back_sel = jnp.where(slot_hot[:, :, None], back_rows[:, None, :], jnp.zeros((), back_rows.dtype))
    a_sc = jnp.einsum("nsc,nd->scd", back_sel, tokens_in, preferred_element_type=jnp.float32)
    mid_rows = middle_rank_rows.reshape(tok_rows, 2, PADDED_RANK)
    mid_sel = jnp.where(
        slot_hot[:, :, None, None], mid_rows[:, None, :, :], jnp.zeros((), mid_rows.dtype)
    )
    b_sc = jnp.einsum("nspr,npk->sprk", mid_sel, grad_out, preferred_element_type=jnp.float32)
    slot_tenant = jnp.argsort(tenant_slot)
    slot_scale = adapter_alpha_factor / tenant_rank[slot_tenant].astype(jnp.float32)
    b_sc = b_sc * slot_scale[:, None, None, None]
    b_full = b_sc.reshape(TENANTS, rank_width, kv_shard)
    if TENANTS % 4:
        a_own = grouped_exchange(a_sc)
        b_own = grouped_exchange(b_full)
    else:
        a_acc = group_stage(a_sc)
        b_full, a_acc = lax.optimization_barrier((b_full, a_acc))
        a_own = cross_stage(a_acc)
        b_own = grouped_exchange(b_full)
    return a_own.T, b_own


def group_stage(full):
    n = full.shape[0]
    member = lax.axis_index("dp") % 4
    by_member = full.reshape(n // 4, 4, *full.shape[1:])
    acc = lax.dynamic_index_in_dim(by_member, member, axis=1, keepdims=False)
    for m in (1, 2, 3):
        pairs = [(i, (i // 4) * 4 + ((i % 4) ^ m)) for i in range(n)]
        part = lax.dynamic_index_in_dim(by_member, member ^ m, axis=1, keepdims=False)
        acc = acc + lax.ppermute(part.astype(jnp.bfloat16), "dp", pairs).astype(jnp.float32)
    return acc


def cross_stage(acc):
    groups = acc.shape[0]
    n = groups * 4
    group = lax.axis_index("dp") // 4
    total = lax.dynamic_index_in_dim(acc, group, axis=0, keepdims=False)
    for m in range(1, groups):
        pairs = [(i, ((i // 4 + m) % groups) * 4 + i % 4) for i in range(n)]
        part = lax.dynamic_index_in_dim(acc, (group + m) % groups, axis=0, keepdims=False)
        total = total + lax.ppermute(part.astype(jnp.bfloat16), "dp", pairs).astype(jnp.float32)
    return total


def grouped_exchange(full):
    n = full.shape[0]
    if n % 4:
        recv = lax.all_to_all(full.astype(jnp.bfloat16), "dp", split_axis=0, concat_axis=0, tiled=True)
        return jnp.sum(recv.astype(jnp.float32), axis=0)
    groups = n // 4
    me = lax.axis_index("dp")
    member = me % 4
    group = me // 4
    by_member = full.reshape(groups, 4, *full.shape[1:])
    acc = lax.dynamic_index_in_dim(by_member, member, axis=1, keepdims=False)
    for m in (1, 2, 3):
        pairs = [(i, (i // 4) * 4 + ((i % 4) ^ m)) for i in range(n)]
        part = lax.dynamic_index_in_dim(by_member, member ^ m, axis=1, keepdims=False)
        acc = acc + lax.ppermute(part.astype(jnp.bfloat16), "dp", pairs).astype(jnp.float32)
    total = lax.dynamic_index_in_dim(acc, group, axis=0, keepdims=False)
    for m in range(1, groups):
        pairs = [(i, ((i // 4 + m) % groups) * 4 + i % 4) for i in range(n)]
        part = lax.dynamic_index_in_dim(acc, (group + m) % groups, axis=0, keepdims=False)
        total = total + lax.ppermute(part.astype(jnp.bfloat16), "dp", pairs).astype(jnp.float32)
    return total


def local(
    tokens_in,
    grad_out,
    base_weight,
    a_master,
    b_master,
    a_first,
    a_second,
    b_first,
    b_second,
    block_tenant,
    tenant_rank,
    tenant_slot,
):
    tok_rows, feat_shard = tokens_in.shape
    kv_shard = grad_out.shape[2]
    rank_width = a_master.shape[1]
    block_count = tok_rows // TENANT_BLOCK
    dp_size = lax.axis_size("dp")
    a_rows_own = a_master.shape[0]
    b_rows_own = b_master.shape[0]
    b_as_a = b_master.astype(jnp.bfloat16).reshape(b_rows_own * kv_shard // rank_width, rank_width)
    packed = jnp.concatenate([a_master.astype(jnp.bfloat16), b_as_a], axis=0)
    packed_all = lax.all_gather(packed, "dp", axis=0, tiled=False)
    frozen_gradient_share = frozen_gradient(grad_out, base_weight, feat_shard)
    frozen_gradient_share, packed_all = lax.optimization_barrier((frozen_gradient_share, packed_all))
    block_slot = tenant_slot[block_tenant]
    slot_major = dp_size == TENANTS
    if slot_major:
        picked = jnp.take(packed_all, block_slot, axis=0, mode="clip")
        a_blocks = picked[:, :a_rows_own]
        b_blocks = picked[:, a_rows_own:].reshape(block_count, 2, PADDED_RANK, kv_shard)
    else:
        a_all = packed_all[:, :a_rows_own].reshape(TENANTS, feat_shard, rank_width)
        b_all = packed_all[:, a_rows_own:].reshape(dp_size, b_rows_own, kv_shard).reshape(
            TENANTS, rank_width, kv_shard
        )
        a_blocks = a_all[block_slot]
        b_blocks = b_all[block_slot].reshape(block_count, 2, PADDED_RANK, kv_shard)
    rank_of_block = tenant_rank[block_tenant].astype(jnp.float32)
    column_rank = (jnp.arange(rank_width) % PADDED_RANK).astype(jnp.float32)
    column_rank_mask = (column_rank[None, :] < rank_of_block[:, None]).astype(jnp.float32)
    adapter_scale_factor = adapter_alpha_factor / rank_of_block
    x_blocks = tokens_in.reshape(block_count, TENANT_BLOCK, feat_shard)
    dy_blocks = grad_out.reshape(block_count, TENANT_BLOCK, 2, kv_shard)
    mid_part = jnp.einsum("bnd,bdc->bnc", x_blocks, a_blocks, preferred_element_type=jnp.float32)
    back_part = jnp.einsum(
        "bnpk,bprk->bnpr", dy_blocks, b_blocks, preferred_element_type=jnp.float32
    ).reshape(block_count, TENANT_BLOCK, rank_width)
    backward_gradient_sum = tensor_sum((back_part,))[0]
    mid_sum = tensor_sum((mid_part,))[0]
    middle_rank_rows = (mid_sum * column_rank_mask[:, None, :]).astype(jnp.bfloat16)
    backward_token_rows = (
        backward_gradient_sum * (column_rank_mask * adapter_scale_factor[:, None])[:, None, :]
    ).astype(jnp.bfloat16)
    adapter_gradient_term = jnp.einsum(
        "bnc,bdc->bnd", backward_token_rows, a_blocks, preferred_element_type=jnp.float32
    ).reshape(tok_rows, feat_shard)
    input_gradient_layer = frozen_gradient_share + adapter_gradient_term
    if slot_major:
        a_grad, b_grad = slot_major_grads(
            tokens_in, grad_out, middle_rank_rows, backward_token_rows, block_slot,
            tenant_rank, tenant_slot,
        )
    else:
        a_terms = jnp.einsum(
            "bnd,bnc->bdc", x_blocks, backward_token_rows, preferred_element_type=jnp.float32
        )
        b_terms = (
            jnp.einsum(
                "bnpr,bnpk->bprk",
                middle_rank_rows.reshape(block_count, TENANT_BLOCK, 2, PADDED_RANK),
                dy_blocks,
                preferred_element_type=jnp.float32,
            )
            * adapter_scale_factor[:, None, None, None]
        )
        one_hot = (block_slot[None, :] == jnp.arange(TENANTS)[:, None]).astype(jnp.float32)
        a_flat = jnp.einsum("sb,bdc->sdc", one_hot, a_terms, precision=lax.Precision.HIGHEST).reshape(
            TENANTS * feat_shard, rank_width
        )
        b_flat = jnp.einsum("sb,bprk->sprk", one_hot, b_terms, precision=lax.Precision.HIGHEST).reshape(
            TENANTS * rank_width, kv_shard
        )
        a_per = a_flat.shape[0] // dp_size
        b_per = b_flat.shape[0] // dp_size
        b_wide = b_per * kv_shard // rank_width
        grad_pack = jnp.concatenate(
            [
                a_flat.reshape(dp_size, a_per, rank_width),
                b_flat.reshape(dp_size, b_wide, rank_width),
            ],
            axis=1,
        ).reshape(dp_size * (a_per + b_wide), rank_width)
        grad_parts = lax.all_to_all(
            grad_pack.astype(jnp.bfloat16).reshape(dp_size, a_per + b_wide, rank_width),
            "dp",
            split_axis=0,
            concat_axis=0,
            tiled=True,
        )
        grad_own = jnp.sum(grad_parts.astype(jnp.float32), axis=0)
        a_grad = grad_own[:a_per]
        b_grad = grad_own[a_per:].reshape(b_per, kv_shard)
    return (
        input_gradient_layer,
        a_grad,
        b_grad,
        adam_step(a_grad, a_first, a_second),
        adam_step(b_grad, b_first, b_second),
    )


def solution(mesh):
    in_specs = (
        P("dp", "tensor"),
        P("dp", None, "tensor"),
        P(None, None, "tensor"),
        P(("tensor", "dp"), None),
        P(("tensor", "dp"), None),
        P(("tensor", "dp"), None),
        P(("tensor", "dp"), None),
        P(("tensor", "dp"), None),
        P(("tensor", "dp"), None),
        P("dp"),
        P(),
        P(),
    )
    out_specs = (
        P("dp", "tensor"),
        P(("tensor", "dp"), None),
        P(("tensor", "dp"), None),
        P(("tensor", "dp"), None),
        P(("tensor", "dp"), None),
    )
    return jax.shard_map(local, mesh=mesh, in_specs=in_specs, out_specs=out_specs, check_vma=False)
```

```python
import jax
import jax.numpy as jnp
from jax import lax
from jax.sharding import PartitionSpec as P

PADDED_RANK = 64
TENANTS = 8
TENANT_BLOCK = 128


adapter_alpha_factor = 32.0
beta_one = 0.9
beta_two = 0.999
adam_eps = 1e-08
corr_one = 1.0 - 0.9**3
corr_two = 1.0 - 0.999**3


def adam_step(grad_value, first_moment, second_moment):
    new_first = beta_one * first_moment + (1.0 - beta_one) * grad_value
    new_second = beta_two * second_moment + (1.0 - beta_two) * grad_value * grad_value
    return new_first / corr_one / (jnp.sqrt(new_second / corr_two) + adam_eps)


def tensor_sum_pair(first, second):
    size = lax.axis_size("tensor")
    width = first.shape[-1]
    both = jnp.concatenate([first, second], axis=-1)
    both = both + lax.ppermute(both, "tensor", [(i, i ^ 1) for i in range(size)])
    first, second = both[..., :width], both[..., width:]
    step = 2
    while step < size:
        pairs = [(i, i ^ step) for i in range(size)]
        first = first + lax.ppermute(first, "tensor", pairs)
        second = second + lax.ppermute(second, "tensor", pairs)
        step *= 2
    return first, second


def tensor_sum(parts):
    size = lax.axis_size("tensor")
    step = 1
    while step < size:
        pairs = [(i, i ^ step) for i in range(size)]
        parts = tuple(p + lax.ppermute(p, "tensor", pairs) for p in parts)
        step *= 2
    return parts


def frozen_gradient(grad_out, base_weight, feat_shard):
    tok_rows, _, kv_shard = grad_out.shape
    t_size = lax.axis_size("tensor")
    if t_size != 4:
        weight_split = jnp.transpose(
            base_weight.reshape(2, t_size, feat_shard, kv_shard), (1, 0, 2, 3)
        )
        weight_rows = lax.all_to_all(weight_split, "tensor", split_axis=0, concat_axis=0, tiled=True)
        dy_full = lax.all_gather(grad_out, "tensor", axis=0, tiled=False)
        return jnp.einsum("jtpk,jpdk->td", dy_full, weight_rows, preferred_element_type=jnp.float32)
    me = lax.axis_index("tensor")
    core_bit = me % 2
    row_bit = me // 2
    by_bits = base_weight.reshape(2, 2, 2, feat_shard, kv_shard)
    to_partner = lax.dynamic_index_in_dim(by_bits, 1 - core_bit, axis=2, keepdims=False)
    own_w = lax.dynamic_index_in_dim(by_bits, core_bit, axis=2, keepdims=False)
    core_pairs = [(i, i ^ 1) for i in range(t_size)]
    row_pairs = [(i, i ^ 2) for i in range(t_size)]
    partner_w = lax.ppermute(to_partner, "tensor", core_pairs)
    partner_dy = lax.ppermute(grad_out, "tensor", core_pairs)

    def chip_partial(bit):
        own = lax.dynamic_index_in_dim(own_w, bit, axis=1, keepdims=False)
        other = lax.dynamic_index_in_dim(partner_w, bit, axis=1, keepdims=False)
        first = jnp.einsum("tpk,pdk->td", grad_out, own, preferred_element_type=jnp.float32)
        second = jnp.einsum("tpk,pdk->td", partner_dy, other, preferred_element_type=jnp.float32)
        return first + second

    far_part = chip_partial(1 - row_bit).astype(jnp.bfloat16)
    half = tok_rows // 2
    far_in = jnp.concatenate(
        [
            lax.ppermute(far_part[:half], "tensor", row_pairs),
            lax.ppermute(far_part[half:], "tensor", row_pairs),
        ],
        axis=0,
    )
    return chip_partial(row_bit) + far_in.astype(jnp.float32)


def slot_major_grads(
    tokens_in, grad_out, middle_rank_rows, backward_token_rows, block_slot, tenant_rank, tenant_slot,
    layer_gradient,
):
    tok_rows, feat_shard = tokens_in.shape
    kv_shard = grad_out.shape[2]
    rank_width = backward_token_rows.shape[-1]
    token_slot = jnp.repeat(block_slot, TENANT_BLOCK)
    slot_hot = token_slot[:, None] == jnp.arange(TENANTS)[None, :]
    back_rows = backward_token_rows.reshape(tok_rows, rank_width)
    back_sel = jnp.where(slot_hot[:, :, None], back_rows[:, None, :], jnp.zeros((), back_rows.dtype))
    a_sc = jnp.einsum("nsc,nd->scd", back_sel, tokens_in, preferred_element_type=jnp.float32)
    mid_rows = middle_rank_rows.reshape(tok_rows, 2, PADDED_RANK)
    mid_sel = jnp.where(
        slot_hot[:, :, None, None], mid_rows[:, None, :, :], jnp.zeros((), mid_rows.dtype)
    )
    b_sc = jnp.einsum("nspr,npk->sprk", mid_sel, grad_out, preferred_element_type=jnp.float32)
    slot_tenant = jnp.argsort(tenant_slot)
    slot_scale = adapter_alpha_factor / tenant_rank[slot_tenant].astype(jnp.float32)
    b_sc = b_sc * slot_scale[:, None, None, None]
    b_full = b_sc.reshape(TENANTS, rank_width, kv_shard)
    if TENANTS % 4:
        a_own = grouped_exchange(a_sc)
        b_own = grouped_exchange(b_full)
    else:
        a_acc = group_stage(a_sc)
        b_full, a_acc, layer_gradient = lax.optimization_barrier((b_full, a_acc, layer_gradient))
        a_own = cross_stage(a_acc)
        b_own = grouped_exchange(b_full)
    return a_own.T, b_own, layer_gradient


def group_stage(full):
    n = full.shape[0]
    member = lax.axis_index("dp") % 4
    by_member = full.reshape(n // 4, 4, *full.shape[1:])
    acc = lax.dynamic_index_in_dim(by_member, member, axis=1, keepdims=False)
    for m in (1, 2, 3):
        pairs = [(i, (i // 4) * 4 + ((i % 4) ^ m)) for i in range(n)]
        part = lax.dynamic_index_in_dim(by_member, member ^ m, axis=1, keepdims=False)
        acc = acc + lax.ppermute(part.astype(jnp.bfloat16), "dp", pairs).astype(jnp.float32)
    return acc


def cross_stage(acc):
    groups = acc.shape[0]
    n = groups * 4
    group = lax.axis_index("dp") // 4
    total = lax.dynamic_index_in_dim(acc, group, axis=0, keepdims=False)
    for m in range(1, groups):
        pairs = [(i, ((i // 4 + m) % groups) * 4 + i % 4) for i in range(n)]
        part = lax.dynamic_index_in_dim(acc, (group + m) % groups, axis=0, keepdims=False)
        total = total + lax.ppermute(part.astype(jnp.bfloat16), "dp", pairs).astype(jnp.float32)
    return total


def grouped_exchange(full):
    n = full.shape[0]
    if n % 4:
        recv = lax.all_to_all(full.astype(jnp.bfloat16), "dp", split_axis=0, concat_axis=0, tiled=True)
        return jnp.sum(recv.astype(jnp.float32), axis=0)
    groups = n // 4
    me = lax.axis_index("dp")
    member = me % 4
    group = me // 4
    by_member = full.reshape(groups, 4, *full.shape[1:])
    acc = lax.dynamic_index_in_dim(by_member, member, axis=1, keepdims=False)
    for m in (1, 2, 3):
        pairs = [(i, (i // 4) * 4 + ((i % 4) ^ m)) for i in range(n)]
        part = lax.dynamic_index_in_dim(by_member, member ^ m, axis=1, keepdims=False)
        acc = acc + lax.ppermute(part.astype(jnp.bfloat16), "dp", pairs).astype(jnp.float32)
    total = lax.dynamic_index_in_dim(acc, group, axis=0, keepdims=False)
    for m in range(1, groups):
        pairs = [(i, ((i // 4 + m) % groups) * 4 + i % 4) for i in range(n)]
        part = lax.dynamic_index_in_dim(acc, (group + m) % groups, axis=0, keepdims=False)
        total = total + lax.ppermute(part.astype(jnp.bfloat16), "dp", pairs).astype(jnp.float32)
    return total


def local(
    tokens_in,
    grad_out,
    base_weight,
    a_master,
    b_master,
    a_first,
    a_second,
    b_first,
    b_second,
    block_tenant,
    tenant_rank,
    tenant_slot,
):
    tok_rows, feat_shard = tokens_in.shape
    kv_shard = grad_out.shape[2]
    rank_width = a_master.shape[1]
    block_count = tok_rows // TENANT_BLOCK
    dp_size = lax.axis_size("dp")
    a_rows_own = a_master.shape[0]
    b_rows_own = b_master.shape[0]
    b_as_a = b_master.astype(jnp.bfloat16).reshape(b_rows_own * kv_shard // rank_width, rank_width)
    packed = jnp.concatenate([a_master.astype(jnp.bfloat16), b_as_a], axis=0)
    packed_all = lax.all_gather(packed, "dp", axis=0, tiled=False)
    frozen_gradient_share = frozen_gradient(grad_out, base_weight, feat_shard)
    frozen_gradient_share, packed_all = lax.optimization_barrier((frozen_gradient_share, packed_all))
    block_slot = tenant_slot[block_tenant]
    slot_major = dp_size == TENANTS
    if slot_major:
        picked = jnp.take(packed_all, block_slot, axis=0, mode="clip")
        a_blocks = picked[:, :a_rows_own]
        b_blocks = picked[:, a_rows_own:].reshape(block_count, 2, PADDED_RANK, kv_shard)
    else:
        a_all = packed_all[:, :a_rows_own].reshape(TENANTS, feat_shard, rank_width)
        b_all = packed_all[:, a_rows_own:].reshape(dp_size, b_rows_own, kv_shard).reshape(
            TENANTS, rank_width, kv_shard
        )
        a_blocks = a_all[block_slot]
        b_blocks = b_all[block_slot].reshape(block_count, 2, PADDED_RANK, kv_shard)
    rank_of_block = tenant_rank[block_tenant].astype(jnp.float32)
    column_rank = (jnp.arange(rank_width) % PADDED_RANK).astype(jnp.float32)
    column_rank_mask = (column_rank[None, :] < rank_of_block[:, None]).astype(jnp.float32)
    adapter_scale_factor = adapter_alpha_factor / rank_of_block
    x_blocks = tokens_in.reshape(block_count, TENANT_BLOCK, feat_shard)
    dy_blocks = grad_out.reshape(block_count, TENANT_BLOCK, 2, kv_shard)
    mid_part = jnp.einsum("bnd,bdc->bnc", x_blocks, a_blocks, preferred_element_type=jnp.float32)
    back_part = jnp.einsum(
        "bnpk,bprk->bnpr", dy_blocks, b_blocks, preferred_element_type=jnp.float32
    ).reshape(block_count, TENANT_BLOCK, rank_width)
    backward_gradient_sum = tensor_sum((back_part,))[0]
    mid_sum = tensor_sum((mid_part,))[0]
    middle_rank_rows = (mid_sum * column_rank_mask[:, None, :]).astype(jnp.bfloat16)
    backward_token_rows = (
        backward_gradient_sum * (column_rank_mask * adapter_scale_factor[:, None])[:, None, :]
    ).astype(jnp.bfloat16)
    adapter_gradient_term = jnp.einsum(
        "bnc,bdc->bnd", backward_token_rows, a_blocks, preferred_element_type=jnp.float32
    ).reshape(tok_rows, feat_shard)
    input_gradient_layer = frozen_gradient_share + adapter_gradient_term
    if slot_major:
        a_grad, b_grad, input_gradient_layer = slot_major_grads(
            tokens_in, grad_out, middle_rank_rows, backward_token_rows, block_slot,
            tenant_rank, tenant_slot, input_gradient_layer,
        )
    else:
        a_terms = jnp.einsum(
            "bnd,bnc->bdc", x_blocks, backward_token_rows, preferred_element_type=jnp.float32
        )
        b_terms = (
            jnp.einsum(
                "bnpr,bnpk->bprk",
                middle_rank_rows.reshape(block_count, TENANT_BLOCK, 2, PADDED_RANK),
                dy_blocks,
                preferred_element_type=jnp.float32,
            )
            * adapter_scale_factor[:, None, None, None]
        )
        one_hot = (block_slot[None, :] == jnp.arange(TENANTS)[:, None]).astype(jnp.float32)
        a_flat = jnp.einsum("sb,bdc->sdc", one_hot, a_terms, precision=lax.Precision.HIGHEST).reshape(
            TENANTS * feat_shard, rank_width
        )
        b_flat = jnp.einsum("sb,bprk->sprk", one_hot, b_terms, precision=lax.Precision.HIGHEST).reshape(
            TENANTS * rank_width, kv_shard
        )
        a_per = a_flat.shape[0] // dp_size
        b_per = b_flat.shape[0] // dp_size
        b_wide = b_per * kv_shard // rank_width
        grad_pack = jnp.concatenate(
            [
                a_flat.reshape(dp_size, a_per, rank_width),
                b_flat.reshape(dp_size, b_wide, rank_width),
            ],
            axis=1,
        ).reshape(dp_size * (a_per + b_wide), rank_width)
        grad_parts = lax.all_to_all(
            grad_pack.astype(jnp.bfloat16).reshape(dp_size, a_per + b_wide, rank_width),
            "dp",
            split_axis=0,
            concat_axis=0,
            tiled=True,
        )
        grad_own = jnp.sum(grad_parts.astype(jnp.float32), axis=0)
        a_grad = grad_own[:a_per]
        b_grad = grad_own[a_per:].reshape(b_per, kv_shard)
    return (
        input_gradient_layer,
        a_grad,
        b_grad,
        adam_step(a_grad, a_first, a_second),
        adam_step(b_grad, b_first, b_second),
    )


def solution(mesh):
    in_specs = (
        P("dp", "tensor"),
        P("dp", None, "tensor"),
        P(None, None, "tensor"),
        P(("tensor", "dp"), None),
        P(("tensor", "dp"), None),
        P(("tensor", "dp"), None),
        P(("tensor", "dp"), None),
        P(("tensor", "dp"), None),
        P(("tensor", "dp"), None),
        P("dp"),
        P(),
        P(),
    )
    out_specs = (
        P("dp", "tensor"),
        P(("tensor", "dp"), None),
        P(("tensor", "dp"), None),
        P(("tensor", "dp"), None),
        P(("tensor", "dp"), None),
    )
    return jax.shard_map(local, mesh=mesh, in_specs=in_specs, out_specs=out_specs, check_vma=False)
```

```python
import jax
import jax.numpy as jnp
from jax import lax
from jax.sharding import PartitionSpec as P

PADDED_RANK = 64
TENANTS = 8
TENANT_BLOCK = 128


adapter_alpha_factor = 32.0
beta_one = 0.9
beta_two = 0.999
adam_eps = 1e-08
corr_one = 1.0 - 0.9**3
corr_two = 1.0 - 0.999**3


def adam_step(grad_value, first_moment, second_moment):
    new_first = beta_one * first_moment + (1.0 - beta_one) * grad_value
    new_second = beta_two * second_moment + (1.0 - beta_two) * grad_value * grad_value
    return new_first / corr_one / (jnp.sqrt(new_second / corr_two) + adam_eps)


def tensor_sum_pair(first, second):
    size = lax.axis_size("tensor")
    width = first.shape[-1]
    both = jnp.concatenate([first, second], axis=-1)
    both = both + lax.ppermute(both, "tensor", [(i, i ^ 1) for i in range(size)])
    first, second = both[..., :width], both[..., width:]
    step = 2
    while step < size:
        pairs = [(i, i ^ step) for i in range(size)]
        first = first + lax.ppermute(first, "tensor", pairs)
        second = second + lax.ppermute(second, "tensor", pairs)
        step *= 2
    return first, second


def tensor_sum(parts):
    size = lax.axis_size("tensor")
    step = 1
    while step < size:
        pairs = [(i, i ^ step) for i in range(size)]
        parts = tuple(p + lax.ppermute(p, "tensor", pairs) for p in parts)
        step *= 2
    return parts


def frozen_gradient(grad_out, base_weight, feat_shard):
    tok_rows, _, kv_shard = grad_out.shape
    t_size = lax.axis_size("tensor")
    if t_size != 4:
        weight_split = jnp.transpose(
            base_weight.reshape(2, t_size, feat_shard, kv_shard), (1, 0, 2, 3)
        )
        weight_rows = lax.all_to_all(weight_split, "tensor", split_axis=0, concat_axis=0, tiled=True)
        dy_full = lax.all_gather(grad_out, "tensor", axis=0, tiled=False)
        return jnp.einsum("jtpk,jpdk->td", dy_full, weight_rows, preferred_element_type=jnp.float32)
    me = lax.axis_index("tensor")
    core_bit = me % 2
    row_bit = me // 2
    by_bits = base_weight.reshape(2, 2, 2, feat_shard, kv_shard)
    to_partner = lax.dynamic_index_in_dim(by_bits, 1 - core_bit, axis=2, keepdims=False)
    own_w = lax.dynamic_index_in_dim(by_bits, core_bit, axis=2, keepdims=False)
    core_pairs = [(i, i ^ 1) for i in range(t_size)]
    row_pairs = [(i, i ^ 2) for i in range(t_size)]
    partner_w = lax.ppermute(to_partner, "tensor", core_pairs)
    partner_dy = lax.ppermute(grad_out, "tensor", core_pairs)

    def chip_partial(bit):
        own = lax.dynamic_index_in_dim(own_w, bit, axis=1, keepdims=False)
        other = lax.dynamic_index_in_dim(partner_w, bit, axis=1, keepdims=False)
        first = jnp.einsum("tpk,pdk->td", grad_out, own, preferred_element_type=jnp.float32)
        second = jnp.einsum("tpk,pdk->td", partner_dy, other, preferred_element_type=jnp.float32)
        return first + second

    far_part = chip_partial(1 - row_bit).astype(jnp.bfloat16)
    half = tok_rows // 2
    far_in = jnp.concatenate(
        [
            lax.ppermute(far_part[:half], "tensor", row_pairs),
            lax.ppermute(far_part[half:], "tensor", row_pairs),
        ],
        axis=0,
    )
    return chip_partial(row_bit) + far_in.astype(jnp.float32)


def slot_major_grads(
    tokens_in, grad_out, middle_rank_rows, backward_token_rows, block_slot, tenant_rank, tenant_slot,
    layer_gradient,
):
    tok_rows, feat_shard = tokens_in.shape
    kv_shard = grad_out.shape[2]
    rank_width = backward_token_rows.shape[-1]
    token_slot = jnp.repeat(block_slot, TENANT_BLOCK)
    slot_hot = token_slot[:, None] == jnp.arange(TENANTS)[None, :]
    back_rows = backward_token_rows.reshape(tok_rows, rank_width)
    back_sel = jnp.where(slot_hot[:, :, None], back_rows[:, None, :], jnp.zeros((), back_rows.dtype))
    a_sc = jnp.einsum("nsc,nd->scd", back_sel, tokens_in, preferred_element_type=jnp.float32)
    mid_rows = middle_rank_rows.reshape(tok_rows, 2, PADDED_RANK)
    mid_sel = jnp.where(
        slot_hot[:, :, None, None], mid_rows[:, None, :, :], jnp.zeros((), mid_rows.dtype)
    )
    b_sc = jnp.einsum("nspr,npk->sprk", mid_sel, grad_out, preferred_element_type=jnp.float32)
    slot_tenant = jnp.argsort(tenant_slot)
    slot_scale = adapter_alpha_factor / tenant_rank[slot_tenant].astype(jnp.float32)
    b_sc = b_sc * slot_scale[:, None, None, None]
    b_full = b_sc.reshape(TENANTS, rank_width, kv_shard)
    if TENANTS % 4:
        a_own = grouped_exchange(a_sc)
        b_own = grouped_exchange(b_full)
    else:
        a_acc = group_stage(a_sc)
        b_own = grouped_exchange(b_full)
        b_own, a_acc, layer_gradient = lax.optimization_barrier((b_own, a_acc, layer_gradient))
        a_own = cross_stage(a_acc)
    return a_own.T, b_own, layer_gradient


def group_stage(full):
    n = full.shape[0]
    member = lax.axis_index("dp") % 4
    by_member = full.reshape(n // 4, 4, *full.shape[1:])
    acc = lax.dynamic_index_in_dim(by_member, member, axis=1, keepdims=False)
    for m in (1, 2, 3):
        pairs = [(i, (i // 4) * 4 + ((i % 4) ^ m)) for i in range(n)]
        part = lax.dynamic_index_in_dim(by_member, member ^ m, axis=1, keepdims=False)
        acc = acc + lax.ppermute(part.astype(jnp.bfloat16), "dp", pairs).astype(jnp.float32)
    return acc


def cross_stage(acc):
    groups = acc.shape[0]
    n = groups * 4
    group = lax.axis_index("dp") // 4
    total = lax.dynamic_index_in_dim(acc, group, axis=0, keepdims=False)
    for m in range(1, groups):
        pairs = [(i, ((i // 4 + m) % groups) * 4 + i % 4) for i in range(n)]
        part = lax.dynamic_index_in_dim(acc, (group + m) % groups, axis=0, keepdims=False)
        total = total + lax.ppermute(part.astype(jnp.bfloat16), "dp", pairs).astype(jnp.float32)
    return total


def grouped_exchange(full):
    n = full.shape[0]
    if n % 4:
        recv = lax.all_to_all(full.astype(jnp.bfloat16), "dp", split_axis=0, concat_axis=0, tiled=True)
        return jnp.sum(recv.astype(jnp.float32), axis=0)
    groups = n // 4
    me = lax.axis_index("dp")
    member = me % 4
    group = me // 4
    by_member = full.reshape(groups, 4, *full.shape[1:])
    acc = lax.dynamic_index_in_dim(by_member, member, axis=1, keepdims=False)
    for m in (1, 2, 3):
        pairs = [(i, (i // 4) * 4 + ((i % 4) ^ m)) for i in range(n)]
        part = lax.dynamic_index_in_dim(by_member, member ^ m, axis=1, keepdims=False)
        acc = acc + lax.ppermute(part.astype(jnp.bfloat16), "dp", pairs).astype(jnp.float32)
    total = lax.dynamic_index_in_dim(acc, group, axis=0, keepdims=False)
    for m in range(1, groups):
        pairs = [(i, ((i // 4 + m) % groups) * 4 + i % 4) for i in range(n)]
        part = lax.dynamic_index_in_dim(acc, (group + m) % groups, axis=0, keepdims=False)
        total = total + lax.ppermute(part.astype(jnp.bfloat16), "dp", pairs).astype(jnp.float32)
    return total


def local(
    tokens_in,
    grad_out,
    base_weight,
    a_master,
    b_master,
    a_first,
    a_second,
    b_first,
    b_second,
    block_tenant,
    tenant_rank,
    tenant_slot,
):
    tok_rows, feat_shard = tokens_in.shape
    kv_shard = grad_out.shape[2]
    rank_width = a_master.shape[1]
    block_count = tok_rows // TENANT_BLOCK
    dp_size = lax.axis_size("dp")
    a_rows_own = a_master.shape[0]
    b_rows_own = b_master.shape[0]
    b_as_a = b_master.astype(jnp.bfloat16).reshape(b_rows_own * kv_shard // rank_width, rank_width)
    packed = jnp.concatenate([a_master.astype(jnp.bfloat16), b_as_a], axis=0)
    packed_all = lax.all_gather(packed, "dp", axis=0, tiled=False)
    frozen_gradient_share = frozen_gradient(grad_out, base_weight, feat_shard)
    frozen_gradient_share, packed_all = lax.optimization_barrier((frozen_gradient_share, packed_all))
    block_slot = tenant_slot[block_tenant]
    slot_major = dp_size == TENANTS
    if slot_major:
        picked = jnp.take(packed_all, block_slot, axis=0, mode="clip")
        a_blocks = picked[:, :a_rows_own]
        b_blocks = picked[:, a_rows_own:].reshape(block_count, 2, PADDED_RANK, kv_shard)
    else:
        a_all = packed_all[:, :a_rows_own].reshape(TENANTS, feat_shard, rank_width)
        b_all = packed_all[:, a_rows_own:].reshape(dp_size, b_rows_own, kv_shard).reshape(
            TENANTS, rank_width, kv_shard
        )
        a_blocks = a_all[block_slot]
        b_blocks = b_all[block_slot].reshape(block_count, 2, PADDED_RANK, kv_shard)
    rank_of_block = tenant_rank[block_tenant].astype(jnp.float32)
    column_rank = (jnp.arange(rank_width) % PADDED_RANK).astype(jnp.float32)
    column_rank_mask = (column_rank[None, :] < rank_of_block[:, None]).astype(jnp.float32)
    adapter_scale_factor = adapter_alpha_factor / rank_of_block
    x_blocks = tokens_in.reshape(block_count, TENANT_BLOCK, feat_shard)
    dy_blocks = grad_out.reshape(block_count, TENANT_BLOCK, 2, kv_shard)
    mid_part = jnp.einsum("bnd,bdc->bnc", x_blocks, a_blocks, preferred_element_type=jnp.float32)
    back_part = jnp.einsum(
        "bnpk,bprk->bnpr", dy_blocks, b_blocks, preferred_element_type=jnp.float32
    ).reshape(block_count, TENANT_BLOCK, rank_width)
    backward_gradient_sum = tensor_sum((back_part,))[0]
    mid_sum = tensor_sum((mid_part,))[0]
    middle_rank_rows = (mid_sum * column_rank_mask[:, None, :]).astype(jnp.bfloat16)
    backward_token_rows = (
        backward_gradient_sum * (column_rank_mask * adapter_scale_factor[:, None])[:, None, :]
    ).astype(jnp.bfloat16)
    adapter_gradient_term = jnp.einsum(
        "bnc,bdc->bnd", backward_token_rows, a_blocks, preferred_element_type=jnp.float32
    ).reshape(tok_rows, feat_shard)
    input_gradient_layer = frozen_gradient_share + adapter_gradient_term
    if slot_major:
        a_grad, b_grad, input_gradient_layer = slot_major_grads(
            tokens_in, grad_out, middle_rank_rows, backward_token_rows, block_slot,
            tenant_rank, tenant_slot, input_gradient_layer,
        )
    else:
        a_terms = jnp.einsum(
            "bnd,bnc->bdc", x_blocks, backward_token_rows, preferred_element_type=jnp.float32
        )
        b_terms = (
            jnp.einsum(
                "bnpr,bnpk->bprk",
                middle_rank_rows.reshape(block_count, TENANT_BLOCK, 2, PADDED_RANK),
                dy_blocks,
                preferred_element_type=jnp.float32,
            )
            * adapter_scale_factor[:, None, None, None]
        )
        one_hot = (block_slot[None, :] == jnp.arange(TENANTS)[:, None]).astype(jnp.float32)
        a_flat = jnp.einsum("sb,bdc->sdc", one_hot, a_terms, precision=lax.Precision.HIGHEST).reshape(
            TENANTS * feat_shard, rank_width
        )
        b_flat = jnp.einsum("sb,bprk->sprk", one_hot, b_terms, precision=lax.Precision.HIGHEST).reshape(
            TENANTS * rank_width, kv_shard
        )
        a_per = a_flat.shape[0] // dp_size
        b_per = b_flat.shape[0] // dp_size
        b_wide = b_per * kv_shard // rank_width
        grad_pack = jnp.concatenate(
            [
                a_flat.reshape(dp_size, a_per, rank_width),
                b_flat.reshape(dp_size, b_wide, rank_width),
            ],
            axis=1,
        ).reshape(dp_size * (a_per + b_wide), rank_width)
        grad_parts = lax.all_to_all(
            grad_pack.astype(jnp.bfloat16).reshape(dp_size, a_per + b_wide, rank_width),
            "dp",
            split_axis=0,
            concat_axis=0,
            tiled=True,
        )
        grad_own = jnp.sum(grad_parts.astype(jnp.float32), axis=0)
        a_grad = grad_own[:a_per]
        b_grad = grad_own[a_per:].reshape(b_per, kv_shard)
    return (
        input_gradient_layer,
        a_grad,
        b_grad,
        adam_step(a_grad, a_first, a_second),
        adam_step(b_grad, b_first, b_second),
    )


def solution(mesh):
    in_specs = (
        P("dp", "tensor"),
        P("dp", None, "tensor"),
        P(None, None, "tensor"),
        P(("tensor", "dp"), None),
        P(("tensor", "dp"), None),
        P(("tensor", "dp"), None),
        P(("tensor", "dp"), None),
        P(("tensor", "dp"), None),
        P(("tensor", "dp"), None),
        P("dp"),
        P(),
        P(),
    )
    out_specs = (
        P("dp", "tensor"),
        P(("tensor", "dp"), None),
        P(("tensor", "dp"), None),
        P(("tensor", "dp"), None),
        P(("tensor", "dp"), None),
    )
    return jax.shard_map(local, mesh=mesh, in_specs=in_specs, out_specs=out_specs, check_vma=False)
```

```python
import jax
import jax.numpy as jnp
from jax import lax
from jax.sharding import PartitionSpec as P

PADDED_RANK = 64
TENANTS = 8
TENANT_BLOCK = 128


adapter_alpha_factor = 32.0
beta_one = 0.9
beta_two = 0.999
adam_eps = 1e-08
corr_one = 1.0 - 0.9**3
corr_two = 1.0 - 0.999**3


def adam_step(grad_value, first_moment, second_moment):
    new_first = beta_one * first_moment + (1.0 - beta_one) * grad_value
    new_second = beta_two * second_moment + (1.0 - beta_two) * grad_value * grad_value
    return new_first / corr_one / (jnp.sqrt(new_second / corr_two) + adam_eps)


def tensor_sum_pair(first, second):
    size = lax.axis_size("tensor")
    width = first.shape[-1]
    both = jnp.concatenate([first, second], axis=-1)
    both = both + lax.ppermute(both, "tensor", [(i, i ^ 1) for i in range(size)])
    first, second = both[..., :width], both[..., width:]
    step = 2
    while step < size:
        pairs = [(i, i ^ step) for i in range(size)]
        first = first + lax.ppermute(first, "tensor", pairs)
        second = second + lax.ppermute(second, "tensor", pairs)
        step *= 2
    return first, second


def tensor_sum(parts):
    size = lax.axis_size("tensor")
    step = 1
    while step < size:
        pairs = [(i, i ^ step) for i in range(size)]
        parts = tuple(p + lax.ppermute(p, "tensor", pairs) for p in parts)
        step *= 2
    return parts


def frozen_gradient(grad_out, base_weight, feat_shard):
    tok_rows, _, kv_shard = grad_out.shape
    t_size = lax.axis_size("tensor")
    if t_size != 4:
        weight_split = jnp.transpose(
            base_weight.reshape(2, t_size, feat_shard, kv_shard), (1, 0, 2, 3)
        )
        weight_rows = lax.all_to_all(weight_split, "tensor", split_axis=0, concat_axis=0, tiled=True)
        dy_full = lax.all_gather(grad_out, "tensor", axis=0, tiled=False)
        return jnp.einsum("jtpk,jpdk->td", dy_full, weight_rows, preferred_element_type=jnp.float32)
    me = lax.axis_index("tensor")
    core_bit = me % 2
    row_bit = me // 2
    by_bits = base_weight.reshape(2, 2, 2, feat_shard, kv_shard)
    to_partner = lax.dynamic_index_in_dim(by_bits, 1 - core_bit, axis=2, keepdims=False)
    own_w = lax.dynamic_index_in_dim(by_bits, core_bit, axis=2, keepdims=False)
    core_pairs = [(i, i ^ 1) for i in range(t_size)]
    row_pairs = [(i, i ^ 2) for i in range(t_size)]
    partner_w = lax.ppermute(to_partner, "tensor", core_pairs)
    partner_dy = lax.ppermute(grad_out, "tensor", core_pairs)

    def chip_partial(bit):
        own = lax.dynamic_index_in_dim(own_w, bit, axis=1, keepdims=False)
        other = lax.dynamic_index_in_dim(partner_w, bit, axis=1, keepdims=False)
        first = jnp.einsum("tpk,pdk->td", grad_out, own, preferred_element_type=jnp.float32)
        second = jnp.einsum("tpk,pdk->td", partner_dy, other, preferred_element_type=jnp.float32)
        return first + second

    far_part = chip_partial(1 - row_bit).astype(jnp.bfloat16)
    half = tok_rows // 2
    far_in = jnp.concatenate(
        [
            lax.ppermute(far_part[:half], "tensor", row_pairs),
            lax.ppermute(far_part[half:], "tensor", row_pairs),
        ],
        axis=0,
    )
    return chip_partial(row_bit) + far_in.astype(jnp.float32)


def slot_major_grads(
    tokens_in, grad_out, middle_rank_rows, backward_token_rows, block_slot, tenant_rank, tenant_slot
):
    tok_rows, feat_shard = tokens_in.shape
    kv_shard = grad_out.shape[2]
    rank_width = backward_token_rows.shape[-1]
    token_slot = jnp.repeat(block_slot, TENANT_BLOCK)
    slot_hot = token_slot[:, None] == jnp.arange(TENANTS)[None, :]
    back_rows = backward_token_rows.reshape(tok_rows, rank_width)
    back_sel = jnp.where(slot_hot[:, :, None], back_rows[:, None, :], jnp.zeros((), back_rows.dtype))
    a_sc = jnp.einsum("nsc,nd->scd", back_sel, tokens_in, preferred_element_type=jnp.float32)
    mid_rows = middle_rank_rows.reshape(tok_rows, 2, PADDED_RANK)
    mid_sel = jnp.where(
        slot_hot[:, :, None, None], mid_rows[:, None, :, :], jnp.zeros((), mid_rows.dtype)
    )
    b_sc = jnp.einsum("nspr,npk->sprk", mid_sel, grad_out, preferred_element_type=jnp.float32)
    slot_tenant = jnp.argsort(tenant_slot)
    slot_scale = adapter_alpha_factor / tenant_rank[slot_tenant].astype(jnp.float32)
    b_sc = b_sc * slot_scale[:, None, None, None]
    b_full = b_sc.reshape(TENANTS, rank_width, kv_shard)
    if TENANTS % 4:
        a_own = grouped_exchange(a_sc)
        b_own = grouped_exchange(b_full)
    else:
        a_acc = group_stage(a_sc)
        b_full, a_acc = lax.optimization_barrier((b_full, a_acc))
        a_own = cross_stage(a_acc)
        b_own = grouped_exchange(b_full)
    return a_own.T, b_own


def group_stage(full):
    n = full.shape[0]
    member = lax.axis_index("dp") % 4
    by_member = full.reshape(n // 4, 4, *full.shape[1:])
    acc = lax.dynamic_index_in_dim(by_member, member, axis=1, keepdims=False)
    for m in (1, 2, 3):
        pairs = [(i, (i // 4) * 4 + ((i % 4) ^ m)) for i in range(n)]
        part = lax.dynamic_index_in_dim(by_member, member ^ m, axis=1, keepdims=False)
        acc = acc + lax.ppermute(part.astype(jnp.bfloat16), "dp", pairs).astype(jnp.float32)
    return acc


def cross_stage(acc):
    groups = acc.shape[0]
    n = groups * 4
    group = lax.axis_index("dp") // 4
    total = lax.dynamic_index_in_dim(acc, group, axis=0, keepdims=False)
    for m in range(1, groups):
        pairs = [(i, ((i // 4 + m) % groups) * 4 + i % 4) for i in range(n)]
        part = lax.dynamic_index_in_dim(acc, (group + m) % groups, axis=0, keepdims=False)
        total = total + lax.ppermute(part.astype(jnp.bfloat16), "dp", pairs).astype(jnp.float32)
    return total


def grouped_exchange(full):
    n = full.shape[0]
    if n % 4:
        recv = lax.all_to_all(full.astype(jnp.bfloat16), "dp", split_axis=0, concat_axis=0, tiled=True)
        return jnp.sum(recv.astype(jnp.float32), axis=0)
    groups = n // 4
    me = lax.axis_index("dp")
    member = me % 4
    group = me // 4
    by_member = full.reshape(groups, 4, *full.shape[1:])
    acc = lax.dynamic_index_in_dim(by_member, member, axis=1, keepdims=False)
    for m in (1, 2, 3):
        pairs = [(i, (i // 4) * 4 + ((i % 4) ^ m)) for i in range(n)]
        part = lax.dynamic_index_in_dim(by_member, member ^ m, axis=1, keepdims=False)
        acc = acc + lax.ppermute(part.astype(jnp.bfloat16), "dp", pairs).astype(jnp.float32)
    total = lax.dynamic_index_in_dim(acc, group, axis=0, keepdims=False)
    for m in range(1, groups):
        pairs = [(i, ((i // 4 + m) % groups) * 4 + i % 4) for i in range(n)]
        part = lax.dynamic_index_in_dim(acc, (group + m) % groups, axis=0, keepdims=False)
        total = total + lax.ppermute(part.astype(jnp.bfloat16), "dp", pairs).astype(jnp.float32)
    return total


def local(
    tokens_in,
    grad_out,
    base_weight,
    a_master,
    b_master,
    a_first,
    a_second,
    b_first,
    b_second,
    block_tenant,
    tenant_rank,
    tenant_slot,
):
    tok_rows, feat_shard = tokens_in.shape
    kv_shard = grad_out.shape[2]
    rank_width = a_master.shape[1]
    block_count = tok_rows // TENANT_BLOCK
    dp_size = lax.axis_size("dp")
    a_rows_own = a_master.shape[0]
    b_rows_own = b_master.shape[0]
    b_as_a = b_master.astype(jnp.bfloat16).reshape(b_rows_own * kv_shard // rank_width, rank_width)
    packed = jnp.concatenate([a_master.astype(jnp.bfloat16), b_as_a], axis=0)
    packed_all = lax.all_gather(packed, "dp", axis=0, tiled=False)
    frozen_gradient_share = frozen_gradient(grad_out, base_weight, feat_shard)
    frozen_gradient_share, packed_all = lax.optimization_barrier((frozen_gradient_share, packed_all))
    block_slot = tenant_slot[block_tenant]
    slot_major = dp_size == TENANTS
    if slot_major:
        b_blocks = jnp.take(packed_all[:, a_rows_own:], block_slot, axis=0, mode="clip").reshape(
            block_count, 2, PADDED_RANK, kv_shard
        )
    else:
        a_all = packed_all[:, :a_rows_own].reshape(TENANTS, feat_shard, rank_width)
        b_all = packed_all[:, a_rows_own:].reshape(dp_size, b_rows_own, kv_shard).reshape(
            TENANTS, rank_width, kv_shard
        )
        a_blocks = a_all[block_slot]
        b_blocks = b_all[block_slot].reshape(block_count, 2, PADDED_RANK, kv_shard)
    rank_of_block = tenant_rank[block_tenant].astype(jnp.float32)
    column_rank = (jnp.arange(rank_width) % PADDED_RANK).astype(jnp.float32)
    column_rank_mask = (column_rank[None, :] < rank_of_block[:, None]).astype(jnp.float32)
    adapter_scale_factor = adapter_alpha_factor / rank_of_block
    x_blocks = tokens_in.reshape(block_count, TENANT_BLOCK, feat_shard)
    dy_blocks = grad_out.reshape(block_count, TENANT_BLOCK, 2, kv_shard)
    back_part = jnp.einsum(
        "bnpk,bprk->bnpr", dy_blocks, b_blocks, preferred_element_type=jnp.float32
    ).reshape(block_count, TENANT_BLOCK, rank_width)
    if slot_major:
        late_all, _ = lax.optimization_barrier((packed_all, back_part))
        a_blocks = jnp.take(late_all, block_slot, axis=0, mode="clip")[:, :a_rows_own]
    mid_part = jnp.einsum("bnd,bdc->bnc", x_blocks, a_blocks, preferred_element_type=jnp.float32)
    backward_gradient_sum = tensor_sum((back_part,))[0]
    mid_sum = tensor_sum((mid_part,))[0]
    middle_rank_rows = (mid_sum * column_rank_mask[:, None, :]).astype(jnp.bfloat16)
    backward_token_rows = (
        backward_gradient_sum * (column_rank_mask * adapter_scale_factor[:, None])[:, None, :]
    ).astype(jnp.bfloat16)
    adapter_gradient_term = jnp.einsum(
        "bnc,bdc->bnd", backward_token_rows, a_blocks, preferred_element_type=jnp.float32
    ).reshape(tok_rows, feat_shard)
    input_gradient_layer = frozen_gradient_share + adapter_gradient_term
    if slot_major:
        a_grad, b_grad = slot_major_grads(
            tokens_in, grad_out, middle_rank_rows, backward_token_rows, block_slot,
            tenant_rank, tenant_slot,
        )
    else:
        a_terms = jnp.einsum(
            "bnd,bnc->bdc", x_blocks, backward_token_rows, preferred_element_type=jnp.float32
        )
        b_terms = (
            jnp.einsum(
                "bnpr,bnpk->bprk",
                middle_rank_rows.reshape(block_count, TENANT_BLOCK, 2, PADDED_RANK),
                dy_blocks,
                preferred_element_type=jnp.float32,
            )
            * adapter_scale_factor[:, None, None, None]
        )
        one_hot = (block_slot[None, :] == jnp.arange(TENANTS)[:, None]).astype(jnp.float32)
        a_flat = jnp.einsum("sb,bdc->sdc", one_hot, a_terms, precision=lax.Precision.HIGHEST).reshape(
            TENANTS * feat_shard, rank_width
        )
        b_flat = jnp.einsum("sb,bprk->sprk", one_hot, b_terms, precision=lax.Precision.HIGHEST).reshape(
            TENANTS * rank_width, kv_shard
        )
        a_per = a_flat.shape[0] // dp_size
        b_per = b_flat.shape[0] // dp_size
        b_wide = b_per * kv_shard // rank_width
        grad_pack = jnp.concatenate(
            [
                a_flat.reshape(dp_size, a_per, rank_width),
                b_flat.reshape(dp_size, b_wide, rank_width),
            ],
            axis=1,
        ).reshape(dp_size * (a_per + b_wide), rank_width)
        grad_parts = lax.all_to_all(
            grad_pack.astype(jnp.bfloat16).reshape(dp_size, a_per + b_wide, rank_width),
            "dp",
            split_axis=0,
            concat_axis=0,
            tiled=True,
        )
        grad_own = jnp.sum(grad_parts.astype(jnp.float32), axis=0)
        a_grad = grad_own[:a_per]
        b_grad = grad_own[a_per:].reshape(b_per, kv_shard)
    return (
        input_gradient_layer,
        a_grad,
        b_grad,
        adam_step(a_grad, a_first, a_second),
        adam_step(b_grad, b_first, b_second),
    )


def solution(mesh):
    in_specs = (
        P("dp", "tensor"),
        P("dp", None, "tensor"),
        P(None, None, "tensor"),
        P(("tensor", "dp"), None),
        P(("tensor", "dp"), None),
        P(("tensor", "dp"), None),
        P(("tensor", "dp"), None),
        P(("tensor", "dp"), None),
        P(("tensor", "dp"), None),
        P("dp"),
        P(),
        P(),
    )
    out_specs = (
        P("dp", "tensor"),
        P(("tensor", "dp"), None),
        P(("tensor", "dp"), None),
        P(("tensor", "dp"), None),
        P(("tensor", "dp"), None),
    )
    return jax.shard_map(local, mesh=mesh, in_specs=in_specs, out_specs=out_specs, check_vma=False)
```

```python
import jax
import jax.numpy as jnp
from jax import lax
from jax.sharding import PartitionSpec as P

PADDED_RANK = 64
TENANTS = 8
TENANT_BLOCK = 128


adapter_alpha_factor = 32.0
beta_one = 0.9
beta_two = 0.999
adam_eps = 1e-08
corr_one = 1.0 - 0.9**3
corr_two = 1.0 - 0.999**3


def adam_step(grad_value, first_moment, second_moment):
    new_first = beta_one * first_moment + (1.0 - beta_one) * grad_value
    new_second = beta_two * second_moment + (1.0 - beta_two) * grad_value * grad_value
    return new_first / corr_one / (jnp.sqrt(new_second / corr_two) + adam_eps)


def tensor_sum_pair(first, second):
    size = lax.axis_size("tensor")
    width = first.shape[-1]
    both = jnp.concatenate([first, second], axis=-1)
    both = both + lax.ppermute(both, "tensor", [(i, i ^ 1) for i in range(size)])
    first, second = both[..., :width], both[..., width:]
    step = 2
    while step < size:
        pairs = [(i, i ^ step) for i in range(size)]
        first = first + lax.ppermute(first, "tensor", pairs)
        second = second + lax.ppermute(second, "tensor", pairs)
        step *= 2
    return first, second


def tensor_sum(parts):
    size = lax.axis_size("tensor")
    step = 1
    while step < size:
        pairs = [(i, i ^ step) for i in range(size)]
        parts = tuple(p + lax.ppermute(p, "tensor", pairs) for p in parts)
        step *= 2
    return parts


def frozen_gradient(grad_out, base_weight, feat_shard):
    tok_rows, _, kv_shard = grad_out.shape
    t_size = lax.axis_size("tensor")
    if t_size != 4:
        weight_split = jnp.transpose(
            base_weight.reshape(2, t_size, feat_shard, kv_shard), (1, 0, 2, 3)
        )
        weight_rows = lax.all_to_all(weight_split, "tensor", split_axis=0, concat_axis=0, tiled=True)
        dy_full = lax.all_gather(grad_out, "tensor", axis=0, tiled=False)
        return jnp.einsum("jtpk,jpdk->td", dy_full, weight_rows, preferred_element_type=jnp.float32)
    me = lax.axis_index("tensor")
    core_bit = me % 2
    row_bit = me // 2
    by_bits = base_weight.reshape(2, 2, 2, feat_shard, kv_shard)
    to_partner = lax.dynamic_index_in_dim(by_bits, 1 - core_bit, axis=2, keepdims=False)
    own_w = lax.dynamic_index_in_dim(by_bits, core_bit, axis=2, keepdims=False)
    core_pairs = [(i, i ^ 1) for i in range(t_size)]
    row_pairs = [(i, i ^ 2) for i in range(t_size)]
    partner_w = lax.ppermute(to_partner, "tensor", core_pairs)
    partner_dy = lax.ppermute(grad_out, "tensor", core_pairs)

    def chip_partial(bit):
        own = lax.dynamic_index_in_dim(own_w, bit, axis=1, keepdims=False)
        other = lax.dynamic_index_in_dim(partner_w, bit, axis=1, keepdims=False)
        first = jnp.einsum("tpk,pdk->td", grad_out, own, preferred_element_type=jnp.float32)
        second = jnp.einsum("tpk,pdk->td", partner_dy, other, preferred_element_type=jnp.float32)
        return first + second

    far_part = chip_partial(1 - row_bit).astype(jnp.bfloat16)
    half = tok_rows // 2
    far_in = jnp.concatenate(
        [
            lax.ppermute(far_part[:half], "tensor", row_pairs),
            lax.ppermute(far_part[half:], "tensor", row_pairs),
        ],
        axis=0,
    )
    return chip_partial(row_bit) + far_in.astype(jnp.float32)


def slot_major_grads(
    tokens_in, grad_out, middle_rank_rows, backward_token_rows, block_slot, tenant_rank, tenant_slot
):
    tok_rows, feat_shard = tokens_in.shape
    kv_shard = grad_out.shape[2]
    rank_width = backward_token_rows.shape[-1]
    token_slot = jnp.repeat(block_slot, TENANT_BLOCK)
    slot_hot = token_slot[:, None] == jnp.arange(TENANTS)[None, :]
    back_rows = backward_token_rows.reshape(tok_rows, rank_width)
    back_sel = jnp.where(slot_hot[:, :, None], back_rows[:, None, :], jnp.zeros((), back_rows.dtype))
    a_sc = jnp.einsum("nsc,nd->scd", back_sel, tokens_in, preferred_element_type=jnp.float32)
    mid_rows = middle_rank_rows.reshape(tok_rows, 2, PADDED_RANK)
    mid_sel = jnp.where(
        slot_hot[:, :, None, None], mid_rows[:, None, :, :], jnp.zeros((), mid_rows.dtype)
    )
    b_sc = jnp.einsum("nspr,npk->sprk", mid_sel, grad_out, preferred_element_type=jnp.float32)
    slot_tenant = jnp.argsort(tenant_slot)
    slot_scale = adapter_alpha_factor / tenant_rank[slot_tenant].astype(jnp.float32)
    b_sc = b_sc * slot_scale[:, None, None, None]
    b_full = b_sc.reshape(TENANTS, rank_width, kv_shard)
    if TENANTS % 4:
        a_own = grouped_exchange(a_sc)
        b_own = grouped_exchange(b_full)
    else:
        feat_cols = a_sc.shape[-1]
        both = jnp.concatenate([group_stage(a_sc), group_stage(b_full)], axis=-1)
        own = cross_stage(both)
        a_own = own[:, :feat_cols]
        b_own = own[:, feat_cols:]
    return a_own.T, b_own


def group_stage(full):
    n = full.shape[0]
    member = lax.axis_index("dp") % 4
    by_member = full.reshape(n // 4, 4, *full.shape[1:])
    acc = lax.dynamic_index_in_dim(by_member, member, axis=1, keepdims=False)
    for m in (1, 2, 3):
        pairs = [(i, (i // 4) * 4 + ((i % 4) ^ m)) for i in range(n)]
        part = lax.dynamic_index_in_dim(by_member, member ^ m, axis=1, keepdims=False)
        acc = acc + lax.ppermute(part.astype(jnp.bfloat16), "dp", pairs).astype(jnp.float32)
    return acc


def cross_stage(acc):
    groups = acc.shape[0]
    n = groups * 4
    group = lax.axis_index("dp") // 4
    total = lax.dynamic_index_in_dim(acc, group, axis=0, keepdims=False)
    for m in range(1, groups):
        pairs = [(i, ((i // 4 + m) % groups) * 4 + i % 4) for i in range(n)]
        part = lax.dynamic_index_in_dim(acc, (group + m) % groups, axis=0, keepdims=False)
        total = total + lax.ppermute(part.astype(jnp.bfloat16), "dp", pairs).astype(jnp.float32)
    return total


def grouped_exchange(full):
    n = full.shape[0]
    if n % 4:
        recv = lax.all_to_all(full.astype(jnp.bfloat16), "dp", split_axis=0, concat_axis=0, tiled=True)
        return jnp.sum(recv.astype(jnp.float32), axis=0)
    groups = n // 4
    me = lax.axis_index("dp")
    member = me % 4
    group = me // 4
    by_member = full.reshape(groups, 4, *full.shape[1:])
    acc = lax.dynamic_index_in_dim(by_member, member, axis=1, keepdims=False)
    for m in (1, 2, 3):
        pairs = [(i, (i // 4) * 4 + ((i % 4) ^ m)) for i in range(n)]
        part = lax.dynamic_index_in_dim(by_member, member ^ m, axis=1, keepdims=False)
        acc = acc + lax.ppermute(part.astype(jnp.bfloat16), "dp", pairs).astype(jnp.float32)
    total = lax.dynamic_index_in_dim(acc, group, axis=0, keepdims=False)
    for m in range(1, groups):
        pairs = [(i, ((i // 4 + m) % groups) * 4 + i % 4) for i in range(n)]
        part = lax.dynamic_index_in_dim(acc, (group + m) % groups, axis=0, keepdims=False)
        total = total + lax.ppermute(part.astype(jnp.bfloat16), "dp", pairs).astype(jnp.float32)
    return total


def local(
    tokens_in,
    grad_out,
    base_weight,
    a_master,
    b_master,
    a_first,
    a_second,
    b_first,
    b_second,
    block_tenant,
    tenant_rank,
    tenant_slot,
):
    tok_rows, feat_shard = tokens_in.shape
    kv_shard = grad_out.shape[2]
    rank_width = a_master.shape[1]
    block_count = tok_rows // TENANT_BLOCK
    dp_size = lax.axis_size("dp")
    a_rows_own = a_master.shape[0]
    b_rows_own = b_master.shape[0]
    b_as_a = b_master.astype(jnp.bfloat16).reshape(b_rows_own * kv_shard // rank_width, rank_width)
    packed = jnp.concatenate([a_master.astype(jnp.bfloat16), b_as_a], axis=0)
    packed_all = lax.all_gather(packed, "dp", axis=0, tiled=False)
    frozen_gradient_share = frozen_gradient(grad_out, base_weight, feat_shard)
    frozen_gradient_share, packed_all = lax.optimization_barrier((frozen_gradient_share, packed_all))
    block_slot = tenant_slot[block_tenant]
    slot_major = dp_size == TENANTS
    if slot_major:
        picked = jnp.take(packed_all, block_slot, axis=0, mode="clip")
        a_blocks = picked[:, :a_rows_own]
        b_blocks = picked[:, a_rows_own:].reshape(block_count, 2, PADDED_RANK, kv_shard)
    else:
        a_all = packed_all[:, :a_rows_own].reshape(TENANTS, feat_shard, rank_width)
        b_all = packed_all[:, a_rows_own:].reshape(dp_size, b_rows_own, kv_shard).reshape(
            TENANTS, rank_width, kv_shard
        )
        a_blocks = a_all[block_slot]
        b_blocks = b_all[block_slot].reshape(block_count, 2, PADDED_RANK, kv_shard)
    rank_of_block = tenant_rank[block_tenant].astype(jnp.float32)
    column_rank = (jnp.arange(rank_width) % PADDED_RANK).astype(jnp.float32)
    column_rank_mask = (column_rank[None, :] < rank_of_block[:, None]).astype(jnp.float32)
    adapter_scale_factor = adapter_alpha_factor / rank_of_block
    x_blocks = tokens_in.reshape(block_count, TENANT_BLOCK, feat_shard)
    dy_blocks = grad_out.reshape(block_count, TENANT_BLOCK, 2, kv_shard)
    mid_part = jnp.einsum("bnd,bdc->bnc", x_blocks, a_blocks, preferred_element_type=jnp.float32)
    back_part = jnp.einsum(
        "bnpk,bprk->bnpr", dy_blocks, b_blocks, preferred_element_type=jnp.float32
    ).reshape(block_count, TENANT_BLOCK, rank_width)
    backward_gradient_sum = tensor_sum((back_part,))[0]
    mid_sum = tensor_sum((mid_part,))[0]
    middle_rank_rows = (mid_sum * column_rank_mask[:, None, :]).astype(jnp.bfloat16)
    backward_token_rows = (
        backward_gradient_sum * (column_rank_mask * adapter_scale_factor[:, None])[:, None, :]
    ).astype(jnp.bfloat16)
    adapter_gradient_term = jnp.einsum(
        "bnc,bdc->bnd", backward_token_rows, a_blocks, preferred_element_type=jnp.float32
    ).reshape(tok_rows, feat_shard)
    input_gradient_layer = frozen_gradient_share + adapter_gradient_term
    if slot_major:
        a_grad, b_grad = slot_major_grads(
            tokens_in, grad_out, middle_rank_rows, backward_token_rows, block_slot,
            tenant_rank, tenant_slot,
        )
    else:
        a_terms = jnp.einsum(
            "bnd,bnc->bdc", x_blocks, backward_token_rows, preferred_element_type=jnp.float32
        )
        b_terms = (
            jnp.einsum(
                "bnpr,bnpk->bprk",
                middle_rank_rows.reshape(block_count, TENANT_BLOCK, 2, PADDED_RANK),
                dy_blocks,
                preferred_element_type=jnp.float32,
            )
            * adapter_scale_factor[:, None, None, None]
        )
        one_hot = (block_slot[None, :] == jnp.arange(TENANTS)[:, None]).astype(jnp.float32)
        a_flat = jnp.einsum("sb,bdc->sdc", one_hot, a_terms, precision=lax.Precision.HIGHEST).reshape(
            TENANTS * feat_shard, rank_width
        )
        b_flat = jnp.einsum("sb,bprk->sprk", one_hot, b_terms, precision=lax.Precision.HIGHEST).reshape(
            TENANTS * rank_width, kv_shard
        )
        a_per = a_flat.shape[0] // dp_size
        b_per = b_flat.shape[0] // dp_size
        b_wide = b_per * kv_shard // rank_width
        grad_pack = jnp.concatenate(
            [
                a_flat.reshape(dp_size, a_per, rank_width),
                b_flat.reshape(dp_size, b_wide, rank_width),
            ],
            axis=1,
        ).reshape(dp_size * (a_per + b_wide), rank_width)
        grad_parts = lax.all_to_all(
            grad_pack.astype(jnp.bfloat16).reshape(dp_size, a_per + b_wide, rank_width),
            "dp",
            split_axis=0,
            concat_axis=0,
            tiled=True,
        )
        grad_own = jnp.sum(grad_parts.astype(jnp.float32), axis=0)
        a_grad = grad_own[:a_per]
        b_grad = grad_own[a_per:].reshape(b_per, kv_shard)
    return (
        input_gradient_layer,
        a_grad,
        b_grad,
        adam_step(a_grad, a_first, a_second),
        adam_step(b_grad, b_first, b_second),
    )


def solution(mesh):
    in_specs = (
        P("dp", "tensor"),
        P("dp", None, "tensor"),
        P(None, None, "tensor"),
        P(("tensor", "dp"), None),
        P(("tensor", "dp"), None),
        P(("tensor", "dp"), None),
        P(("tensor", "dp"), None),
        P(("tensor", "dp"), None),
        P(("tensor", "dp"), None),
        P("dp"),
        P(),
        P(),
    )
    out_specs = (
        P("dp", "tensor"),
        P(("tensor", "dp"), None),
        P(("tensor", "dp"), None),
        P(("tensor", "dp"), None),
        P(("tensor", "dp"), None),
    )
    return jax.shard_map(local, mesh=mesh, in_specs=in_specs, out_specs=out_specs, check_vma=False)
```

```python
import jax
import jax.numpy as jnp
from jax import lax
from jax.sharding import PartitionSpec as P

PADDED_RANK = 64
TENANTS = 8
TENANT_BLOCK = 128


adapter_alpha_factor = 32.0
beta_one = 0.9
beta_two = 0.999
adam_eps = 1e-08
corr_one = 1.0 - 0.9**3
corr_two = 1.0 - 0.999**3


def adam_step(grad_value, first_moment, second_moment):
    new_first = beta_one * first_moment + (1.0 - beta_one) * grad_value
    new_second = beta_two * second_moment + (1.0 - beta_two) * grad_value * grad_value
    return new_first / corr_one / (jnp.sqrt(new_second / corr_two) + adam_eps)


def tensor_sum_pair(first, second):
    size = lax.axis_size("tensor")
    width = first.shape[-1]
    both = jnp.concatenate([first, second], axis=-1)
    both = both + lax.ppermute(both, "tensor", [(i, i ^ 1) for i in range(size)])
    first, second = both[..., :width], both[..., width:]
    step = 2
    while step < size:
        pairs = [(i, i ^ step) for i in range(size)]
        first = first + lax.ppermute(first, "tensor", pairs)
        second = second + lax.ppermute(second, "tensor", pairs)
        step *= 2
    return first, second


def tensor_sum(parts):
    size = lax.axis_size("tensor")
    step = 1
    while step < size:
        pairs = [(i, i ^ step) for i in range(size)]
        parts = tuple(p + lax.ppermute(p, "tensor", pairs) for p in parts)
        step *= 2
    return parts


def frozen_gradient(grad_out, base_weight, feat_shard):
    tok_rows, _, kv_shard = grad_out.shape
    t_size = lax.axis_size("tensor")
    if t_size != 4:
        weight_split = jnp.transpose(
            base_weight.reshape(2, t_size, feat_shard, kv_shard), (1, 0, 2, 3)
        )
        weight_rows = lax.all_to_all(weight_split, "tensor", split_axis=0, concat_axis=0, tiled=True)
        dy_full = lax.all_gather(grad_out, "tensor", axis=0, tiled=False)
        return jnp.einsum("jtpk,jpdk->td", dy_full, weight_rows, preferred_element_type=jnp.float32)
    me = lax.axis_index("tensor")
    core_bit = me % 2
    row_bit = me // 2
    by_bits = base_weight.reshape(2, 2, 2, feat_shard, kv_shard)
    to_partner = lax.dynamic_index_in_dim(by_bits, 1 - core_bit, axis=2, keepdims=False)
    own_w = lax.dynamic_index_in_dim(by_bits, core_bit, axis=2, keepdims=False)
    core_pairs = [(i, i ^ 1) for i in range(t_size)]
    row_pairs = [(i, i ^ 2) for i in range(t_size)]
    partner_w = lax.ppermute(to_partner, "tensor", core_pairs)
    partner_dy = lax.ppermute(grad_out, "tensor", core_pairs)

    def chip_partial(bit):
        own = lax.dynamic_index_in_dim(own_w, bit, axis=1, keepdims=False)
        other = lax.dynamic_index_in_dim(partner_w, bit, axis=1, keepdims=False)
        first = jnp.einsum("tpk,pdk->td", grad_out, own, preferred_element_type=jnp.float32)
        second = jnp.einsum("tpk,pdk->td", partner_dy, other, preferred_element_type=jnp.float32)
        return first + second

    far_part = chip_partial(1 - row_bit).astype(jnp.bfloat16)
    half = tok_rows // 2
    far_in = jnp.concatenate(
        [
            lax.ppermute(far_part[:half], "tensor", row_pairs),
            lax.ppermute(far_part[half:], "tensor", row_pairs),
        ],
        axis=0,
    )
    return chip_partial(row_bit) + far_in.astype(jnp.float32)


def slot_major_grads(
    tokens_in, grad_out, middle_rank_rows, backward_token_rows, block_slot, tenant_rank, tenant_slot
):
    tok_rows, feat_shard = tokens_in.shape
    kv_shard = grad_out.shape[2]
    rank_width = backward_token_rows.shape[-1]
    token_slot = jnp.repeat(block_slot, TENANT_BLOCK)
    slot_hot = token_slot[:, None] == jnp.arange(TENANTS)[None, :]
    back_rows = backward_token_rows.reshape(tok_rows, rank_width)
    back_sel = jnp.where(slot_hot[:, :, None], back_rows[:, None, :], jnp.zeros((), back_rows.dtype))
    a_sc = jnp.einsum("nsc,nd->scd", back_sel, tokens_in, preferred_element_type=jnp.float32)
    mid_rows = middle_rank_rows.reshape(tok_rows, 2, PADDED_RANK)
    mid_sel = jnp.where(
        slot_hot[:, :, None, None], mid_rows[:, None, :, :], jnp.zeros((), mid_rows.dtype)
    )
    b_sc = jnp.einsum("nspr,npk->sprk", mid_sel, grad_out, preferred_element_type=jnp.float32)
    slot_tenant = jnp.argsort(tenant_slot)
    slot_scale = adapter_alpha_factor / tenant_rank[slot_tenant].astype(jnp.float32)
    b_sc = b_sc * slot_scale[:, None, None, None]
    b_full = b_sc.reshape(TENANTS, rank_width, kv_shard)
    if TENANTS % 4:
        a_own = grouped_exchange(a_sc)
        b_own = grouped_exchange(b_full)
    else:
        a_acc = group_stage(a_sc)
        b_acc = group_stage(b_full)
        b_acc, a_acc = lax.optimization_barrier((b_acc, a_acc))
        a_own = cross_stage(a_acc)
        b_own = cross_stage(b_acc)
    return a_own.T, b_own


def group_stage(full):
    n = full.shape[0]
    member = lax.axis_index("dp") % 4
    by_member = full.reshape(n // 4, 4, *full.shape[1:])
    acc = lax.dynamic_index_in_dim(by_member, member, axis=1, keepdims=False)
    for m in (1, 2, 3):
        pairs = [(i, (i // 4) * 4 + ((i % 4) ^ m)) for i in range(n)]
        part = lax.dynamic_index_in_dim(by_member, member ^ m, axis=1, keepdims=False)
        acc = acc + lax.ppermute(part.astype(jnp.bfloat16), "dp", pairs).astype(jnp.float32)
    return acc


def cross_stage(acc):
    groups = acc.shape[0]
    n = groups * 4
    group = lax.axis_index("dp") // 4
    total = lax.dynamic_index_in_dim(acc, group, axis=0, keepdims=False)
    for m in range(1, groups):
        pairs = [(i, ((i // 4 + m) % groups) * 4 + i % 4) for i in range(n)]
        part = lax.dynamic_index_in_dim(acc, (group + m) % groups, axis=0, keepdims=False)
        total = total + lax.ppermute(part.astype(jnp.bfloat16), "dp", pairs).astype(jnp.float32)
    return total


def grouped_exchange(full):
    n = full.shape[0]
    if n % 4:
        recv = lax.all_to_all(full.astype(jnp.bfloat16), "dp", split_axis=0, concat_axis=0, tiled=True)
        return jnp.sum(recv.astype(jnp.float32), axis=0)
    groups = n // 4
    me = lax.axis_index("dp")
    member = me % 4
    group = me // 4
    by_member = full.reshape(groups, 4, *full.shape[1:])
    acc = lax.dynamic_index_in_dim(by_member, member, axis=1, keepdims=False)
    for m in (1, 2, 3):
        pairs = [(i, (i // 4) * 4 + ((i % 4) ^ m)) for i in range(n)]
        part = lax.dynamic_index_in_dim(by_member, member ^ m, axis=1, keepdims=False)
        acc = acc + lax.ppermute(part.astype(jnp.bfloat16), "dp", pairs).astype(jnp.float32)
    total = lax.dynamic_index_in_dim(acc, group, axis=0, keepdims=False)
    for m in range(1, groups):
        pairs = [(i, ((i // 4 + m) % groups) * 4 + i % 4) for i in range(n)]
        part = lax.dynamic_index_in_dim(acc, (group + m) % groups, axis=0, keepdims=False)
        total = total + lax.ppermute(part.astype(jnp.bfloat16), "dp", pairs).astype(jnp.float32)
    return total


def local(
    tokens_in,
    grad_out,
    base_weight,
    a_master,
    b_master,
    a_first,
    a_second,
    b_first,
    b_second,
    block_tenant,
    tenant_rank,
    tenant_slot,
):
    tok_rows, feat_shard = tokens_in.shape
    kv_shard = grad_out.shape[2]
    rank_width = a_master.shape[1]
    block_count = tok_rows // TENANT_BLOCK
    dp_size = lax.axis_size("dp")
    a_rows_own = a_master.shape[0]
    b_rows_own = b_master.shape[0]
    b_as_a = b_master.astype(jnp.bfloat16).reshape(b_rows_own * kv_shard // rank_width, rank_width)
    packed = jnp.concatenate([a_master.astype(jnp.bfloat16), b_as_a], axis=0)
    packed_all = lax.all_gather(packed, "dp", axis=0, tiled=False)
    frozen_gradient_share = frozen_gradient(grad_out, base_weight, feat_shard)
    frozen_gradient_share, packed_all = lax.optimization_barrier((frozen_gradient_share, packed_all))
    block_slot = tenant_slot[block_tenant]
    slot_major = dp_size == TENANTS
    if slot_major:
        picked = jnp.take(packed_all, block_slot, axis=0, mode="clip")
        a_blocks = picked[:, :a_rows_own]
        b_blocks = picked[:, a_rows_own:].reshape(block_count, 2, PADDED_RANK, kv_shard)
    else:
        a_all = packed_all[:, :a_rows_own].reshape(TENANTS, feat_shard, rank_width)
        b_all = packed_all[:, a_rows_own:].reshape(dp_size, b_rows_own, kv_shard).reshape(
            TENANTS, rank_width, kv_shard
        )
        a_blocks = a_all[block_slot]
        b_blocks = b_all[block_slot].reshape(block_count, 2, PADDED_RANK, kv_shard)
    rank_of_block = tenant_rank[block_tenant].astype(jnp.float32)
    column_rank = (jnp.arange(rank_width) % PADDED_RANK).astype(jnp.float32)
    column_rank_mask = (column_rank[None, :] < rank_of_block[:, None]).astype(jnp.float32)
    adapter_scale_factor = adapter_alpha_factor / rank_of_block
    x_blocks = tokens_in.reshape(block_count, TENANT_BLOCK, feat_shard)
    dy_blocks = grad_out.reshape(block_count, TENANT_BLOCK, 2, kv_shard)
    mid_part = jnp.einsum("bnd,bdc->bnc", x_blocks, a_blocks, preferred_element_type=jnp.float32)
    back_part = jnp.einsum(
        "bnpk,bprk->bnpr", dy_blocks, b_blocks, preferred_element_type=jnp.float32
    ).reshape(block_count, TENANT_BLOCK, rank_width)
    backward_gradient_sum = tensor_sum((back_part,))[0]
    mid_sum = tensor_sum((mid_part,))[0]
    middle_rank_rows = (mid_sum * column_rank_mask[:, None, :]).astype(jnp.bfloat16)
    backward_token_rows = (
        backward_gradient_sum * (column_rank_mask * adapter_scale_factor[:, None])[:, None, :]
    ).astype(jnp.bfloat16)
    adapter_gradient_term = jnp.einsum(
        "bnc,bdc->bnd", backward_token_rows, a_blocks, preferred_element_type=jnp.float32
    ).reshape(tok_rows, feat_shard)
    input_gradient_layer = frozen_gradient_share + adapter_gradient_term
    if slot_major:
        a_grad, b_grad = slot_major_grads(
            tokens_in, grad_out, middle_rank_rows, backward_token_rows, block_slot,
            tenant_rank, tenant_slot,
        )
    else:
        a_terms = jnp.einsum(
            "bnd,bnc->bdc", x_blocks, backward_token_rows, preferred_element_type=jnp.float32
        )
        b_terms = (
            jnp.einsum(
                "bnpr,bnpk->bprk",
                middle_rank_rows.reshape(block_count, TENANT_BLOCK, 2, PADDED_RANK),
                dy_blocks,
                preferred_element_type=jnp.float32,
            )
            * adapter_scale_factor[:, None, None, None]
        )
        one_hot = (block_slot[None, :] == jnp.arange(TENANTS)[:, None]).astype(jnp.float32)
        a_flat = jnp.einsum("sb,bdc->sdc", one_hot, a_terms, precision=lax.Precision.HIGHEST).reshape(
            TENANTS * feat_shard, rank_width
        )
        b_flat = jnp.einsum("sb,bprk->sprk", one_hot, b_terms, precision=lax.Precision.HIGHEST).reshape(
            TENANTS * rank_width, kv_shard
        )
        a_per = a_flat.shape[0] // dp_size
        b_per = b_flat.shape[0] // dp_size
        b_wide = b_per * kv_shard // rank_width
        grad_pack = jnp.concatenate(
            [
                a_flat.reshape(dp_size, a_per, rank_width),
                b_flat.reshape(dp_size, b_wide, rank_width),
            ],
            axis=1,
        ).reshape(dp_size * (a_per + b_wide), rank_width)
        grad_parts = lax.all_to_all(
            grad_pack.astype(jnp.bfloat16).reshape(dp_size, a_per + b_wide, rank_width),
            "dp",
            split_axis=0,
            concat_axis=0,
            tiled=True,
        )
        grad_own = jnp.sum(grad_parts.astype(jnp.float32), axis=0)
        a_grad = grad_own[:a_per]
        b_grad = grad_own[a_per:].reshape(b_per, kv_shard)
    return (
        input_gradient_layer,
        a_grad,
        b_grad,
        adam_step(a_grad, a_first, a_second),
        adam_step(b_grad, b_first, b_second),
    )


def solution(mesh):
    in_specs = (
        P("dp", "tensor"),
        P("dp", None, "tensor"),
        P(None, None, "tensor"),
        P(("tensor", "dp"), None),
        P(("tensor", "dp"), None),
        P(("tensor", "dp"), None),
        P(("tensor", "dp"), None),
        P(("tensor", "dp"), None),
        P(("tensor", "dp"), None),
        P("dp"),
        P(),
        P(),
    )
    out_specs = (
        P("dp", "tensor"),
        P(("tensor", "dp"), None),
        P(("tensor", "dp"), None),
        P(("tensor", "dp"), None),
        P(("tensor", "dp"), None),
    )
    return jax.shard_map(local, mesh=mesh, in_specs=in_specs, out_specs=out_specs, check_vma=False)
```
